32 devices in a mesh: tile: 4 (over y, core), orient: 8 (over z, x).
Axes of the slice: x: 2, y: 2, z: 4, core: 2. Of those that a mesh axis runs over, the one named last changes fastest.
Arguments:
- tile_spectra: bfloat16 [4, 2, 512, 512], P('tile', None, 'orient'), may hold values from -6 to 6
- template_spectra: bfloat16 [64, 2, 512, 512], P('orient', None, 'tile'), may hold values from -6 to 6
- peaks: int32 [4, 4, 2], P('tile'), may hold values from 0 to 511
- listed: int32 [4, 4, 48], P('tile'), may hold values from 0 to 63, as said below
Outputs:
- best: float32 [4, 4, 128, 128], P('tile')
- power: float32 [4, 4, 128, 128], P('tile')
The draws below stay inside these ranges and needn't reach their ends.
Inputs may be any that keep to these rules, and one draw needn't show every extreme that they name: The 48 ids listed for one peak are distinct.
All inputs are finite; a program needn't handle non-finite values.
Results may differ from the reference program's by a relative error of at most 0.0026.
Values may be sent and summed in bfloat16 or wider, within the bound.
No kernel may reach another device: no remote copies, remote signals or barrier semaphores. Data moves between devices by JAX's collectives and lax.ppermute only.
A program may use at most 128 MiB of HBM per device.

```python
import math
import jax
import jax.numpy as jnp
from jax import lax

S = 512
W = 128
LIST = 48
PEAKS = 4
TILES = 4
NORI = 64


def draw_listed(key, part):
    total_peaks = TILES * PEAKS
    peak_keys = jax.random.split(key, total_peaks)

    def single_peak(peak_key):
        first_key, shuffle_key = jax.random.split(peak_key)
        first_id = jax.random.randint(first_key, (), 0, NORI)
        shuffle = jax.random.permutation(shuffle_key, 64)[:LIST]
        return (first_id + shuffle - 32) % NORI
    return jax.vmap(single_peak)(peak_keys).reshape(TILES, PEAKS, LIST).astype(jnp.int32)


def place_ends(array, own_key, least, high):
    longest = array.shape.index(max(array.shape))
    spots = []
    for shift in (0, 1):
        where = [jax.random.randint(jax.random.fold_in(own_key, axis), (), 0, length) for axis, length in enumerate(array.shape)]
        where[longest] = (where[longest] + shift) % array.shape[longest]
        spots.append(tuple(where))
    return array.at[spots[0]].set(least).at[spots[1]].set(high)


def shard_levels(stream_key, shape, cuts, low, largest):
    loudness = 1.0
    for axis_at, parts in cuts:
        heights = jax.random.uniform(jax.random.fold_in(jax.random.fold_in(stream_key, 6), axis_at), (parts,), jnp.float32, low / len(cuts), largest / len(cuts))
        loudness = loudness * jnp.repeat(jnp.exp(heights), shape[axis_at] // parts).reshape((-1,) + (1,) * (len(shape) - 1 - axis_at))
    return loudness


def gaussian(rng, extent, spread, limit, cuts=(), kind=jnp.bfloat16):
    factor_of = shard_levels(rng, extent, cuts, -0.22, 0.18) if cuts else 1.0
    drawn = jax.random.normal(rng, extent, jnp.float32) * spread * factor_of
    return jnp.minimum(jnp.maximum(drawn, -limit), limit).astype(kind)


def setup_inputs(seed: int = 0) -> dict:
    seeds = jax.random.split(jax.random.key(seed), 5)
    return {
        "tile_spectra": gaussian(seeds[0], (TILES, 2, S, S), 1.0, 6.0, ((0, 4), (2, 8))),
        "template_spectra": gaussian(seeds[1], (NORI, 2, S, S), 1.0, 6.0, ((0, 8), (2, 4))),
        "peaks": place_ends(jax.random.randint(seeds[2], (TILES, PEAKS, 2), 0, S), jax.random.fold_in(seeds[2], 1), 0, S - 1).astype(jnp.int32),
        "listed": draw_listed(jax.random.fold_in(seeds[4], 71), 0),
    }


def window_tables(peak_rows, size, width):
    offsets = jnp.arange(width, dtype=jnp.int32) - width // 2
    freqs = jnp.arange(size, dtype=jnp.int32)

    def tables_for(coords):
        position = (coords[:, None] + offsets[None, :]) % size
        phase = (freqs[None, :, None] * position[:, None, :]) % size
        angle = phase.astype(jnp.float32) * (2.0 * math.pi / size)
        return jnp.cos(angle).astype(jnp.bfloat16), jnp.sin(angle).astype(jnp.bfloat16)

    cos_row, sin_row = tables_for(peak_rows[:, 0])
    cos_col, sin_col = tables_for(peak_rows[:, 1])
    upper = jnp.concatenate([cos_col, sin_col], axis=-1)
    lower = jnp.concatenate([-sin_col, cos_col], axis=-1)
    return cos_row, sin_row, jnp.concatenate([upper, lower], axis=1)


def cross_spectrum(spectrum, template):
    image_re = spectrum[0].astype(jnp.float32)
    image_im = spectrum[1].astype(jnp.float32)
    tmpl_re = template[..., 0, :, :].astype(jnp.float32)
    tmpl_im = template[..., 1, :, :].astype(jnp.float32)
    mixed_re = image_re * tmpl_re + image_im * tmpl_im
    mixed_im = image_im * tmpl_re - image_re * tmpl_im
    return jnp.concatenate([mixed_re, mixed_im], axis=-1).astype(jnp.bfloat16)


def reference(tile_spectra, template_spectra, peaks, listed):
    size = S
    width = W

    def per_tile(inputs):
        spectrum, peak_rows, listed_ids = inputs
        cos_row, sin_row, col_table = window_tables(peak_rows, size, width)

        def per_peak(stuff):
            row_cos, row_sin, table, slot_ids = stuff
            chosen = template_spectra[slot_ids]
            mixed = cross_spectrum(spectrum, chosen).astype(jnp.float32)
            partial_g = jnp.einsum("nrk,kw->nrw", mixed, table.astype(jnp.float32),
                                   precision=lax.Precision.HIGHEST).astype(jnp.bfloat16).astype(jnp.float32)
            scores = jnp.einsum("ra,nrb->nab", row_cos.astype(jnp.float32), partial_g[..., :width],
                                precision=lax.Precision.HIGHEST)
            scores = scores - jnp.einsum("ra,nrb->nab", row_sin.astype(jnp.float32), partial_g[..., width:],
                                         precision=lax.Precision.HIGHEST)
            scores = scores / size
            return jnp.max(scores, axis=0), jnp.sum(scores * scores, axis=0) / LIST

        return lax.map(per_peak, (cos_row, sin_row, col_table, listed_ids))

    best, power = lax.map(per_tile, (tile_spectra, peaks, listed))
    return best, power
```

```python
import math

import jax
import jax.numpy as jnp
from jax import lax
from jax.sharding import Mesh
from jax.sharding import PartitionSpec as P

W = 128
LIST = 48


lowest_score = -1e30


def xor_pairs(n, k):
    return [(i, i ^ k) for i in range(n)]


def is_pow2(n):
    return n & (n - 1) == 0


def angle_tables(freqs, coords, size, width):
    offsets = jnp.arange(width, dtype=jnp.int32) - width // 2
    position = (coords[:, None] + offsets[None, :]) % size
    phase = freqs[None, :, None] * position[:, None, :] % size
    angle = phase.astype(jnp.float32) * (2.0 * math.pi / size)
    return (jnp.cos(angle).astype(jnp.bfloat16), jnp.sin(angle).astype(jnp.bfloat16))


def col_tables(peak_rows, size, width):
    freqs = jnp.arange(size, dtype=jnp.int32)
    cos_col, sin_col = angle_tables(freqs, peak_rows[:, 1], size, width)
    upper = jnp.concatenate([cos_col, sin_col], axis=-1)
    lower = jnp.concatenate([-sin_col, cos_col], axis=-1)
    return jnp.concatenate([upper, lower], axis=1)


def cross_spectrum(spectrum, template):
    image_re = spectrum[0].astype(jnp.float32)
    image_im = spectrum[1].astype(jnp.float32)
    tmpl_re = template[..., 0, :, :].astype(jnp.float32)
    tmpl_im = template[..., 1, :, :].astype(jnp.float32)
    mixed_re = image_re * tmpl_re + image_im * tmpl_im
    mixed_im = image_im * tmpl_re - image_re * tmpl_im
    return jnp.concatenate([mixed_re, mixed_im], axis=-1).astype(jnp.bfloat16)


def gather_rows(part, axis):
    n = lax.axis_size(axis)
    if not is_pow2(n):
        return lax.all_gather(part, axis)
    me = lax.axis_index(axis)
    blocks = part[None]
    k = n // 2
    while k >= 1:
        got = lax.ppermute(blocks, axis, xor_pairs(n, k))
        blocks = jnp.concatenate([blocks, got])
        k //= 2
    want = jnp.arange(n, dtype=jnp.int32) ^ me
    return blocks[order_of(want, n)]


def order_of(want, count):
    steps = int(math.log2(count))
    slot = jnp.zeros_like(want)
    for j in range(steps):
        k = count >> (j + 1)
        hit = (want & k) != 0
        slot = slot | jnp.where(hit, 1 << j, 0)
    return slot


def reduce_orient(best_part, power_part, axis):
    n = lax.axis_size(axis)
    if not is_pow2(n):
        best = lax.pmax(best_part, axis)
        power = lax.psum(power_part, axis)
        return best, power
    width = best_part.shape[-1]
    joined = jnp.stack([best_part.reshape(-1, width), power_part.reshape(-1, width)], axis=0)
    me = lax.axis_index(axis)
    cur = joined
    k = 1
    while k < n:
        half = cur.shape[1] // 2
        bit = (me // k) % 2
        keep = lax.dynamic_slice_in_dim(cur, bit * half, half, axis=1)
        send = lax.dynamic_slice_in_dim(cur, (1 - bit) * half, half, axis=1)
        got = lax.ppermute(send, axis, xor_pairs(n, k))
        cur = jnp.stack([jnp.maximum(keep[0], got[0]), keep[1] + got[1]])
        k *= 2
    k = n // 2
    while k >= 1:
        got = lax.ppermute(cur, axis, xor_pairs(n, k))
        bit = (me // k) % 2
        cur = jnp.where(bit == 1, jnp.concatenate([got, cur], axis=1), jnp.concatenate([cur, got], axis=1))
        k //= 2
    best = cur[0].reshape(best_part.shape)
    power = cur[1].reshape(power_part.shape)
    return best, power


def local(tile_spectra, template_spectra, peaks, listed):
    size = tile_spectra.shape[3]
    width = W
    chips = lax.axis_size("tchip")
    cores = lax.axis_size("tcore")
    rows_t = template_spectra.shape[2]
    tp = lax.all_gather(template_spectra, "tchip", axis=0)
    tp = lax.all_gather(tp, "tcore", axis=0)
    block_size = tp.shape[2]
    tp = jnp.moveaxis(tp, 2, 0)
    tp = jnp.moveaxis(tp, 3, 1)
    tmpl = tp.reshape(block_size, 2, size, size)
    spec = gather_rows(tile_spectra[0], "orient")
    spec = jnp.moveaxis(spec, 0, 1).reshape(2, size, size)
    spec = spec.reshape(2, chips, cores, rows_t, size)
    spec = jnp.swapaxes(spec, 1, 2).reshape(2, size, size)
    core_i = jnp.arange(cores, dtype=jnp.int32)[:, None, None]
    chip_i = jnp.arange(chips, dtype=jnp.int32)[None, :, None]
    r_i = jnp.arange(rows_t, dtype=jnp.int32)[None, None, :]
    freqs = ((chip_i * cores + core_i) * rows_t + r_i).reshape(size)
    cos_row, sin_row = angle_tables(freqs, peaks[0][:, 0], size, width)
    col_table = col_tables(peaks[0], size, width)
    listed_ids = listed[0]
    mixed = cross_spectrum(spec, tmpl)
    partial_g = jnp.einsum(
        "jnk,pkw->pjnw", mixed, col_table, preferred_element_type=jnp.float32
    ).astype(jnp.bfloat16)
    update = jnp.einsum(
        "pna,pjnb->pjab", cos_row, partial_g[..., :width], preferred_element_type=jnp.float32
    )
    update = update - jnp.einsum(
        "pna,pjnb->pjab", sin_row, partial_g[..., width:], preferred_element_type=jnp.float32
    )
    scores = update / size
    global_ids = lax.axis_index("orient") * block_size + jnp.arange(block_size, dtype=jnp.int32)
    is_listed = jnp.any(listed_ids[:, :, None] == global_ids[None, None, :], axis=1)
    is_listed = is_listed[:, :, None, None]
    best_part = jnp.max(jnp.where(is_listed, scores, lowest_score), axis=1)
    power_part = jnp.sum(jnp.where(is_listed, scores * scores, 0.0), axis=1)
    best_all, power_all = reduce_orient(best_part, power_part, "orient")
    return (best_all[None], (power_all / LIST)[None])


def solution(mesh):
    tiles = mesh.shape["tile"]
    orients = mesh.shape["orient"]
    split = Mesh(mesh.devices.reshape(tiles // 2, 2, orients), ("tchip", "tcore", "orient"))
    tile = ("tchip", "tcore")
    placed = (
        P(tile, None, "orient", None),
        P("orient", None, tile, None),
        P(tile, None, None),
        P(tile, None, None),
    )
    return jax.shard_map(
        local,
        mesh=split,
        in_specs=placed,
        out_specs=(P(tile, None, None, None), P(tile, None, None, None)),
        check_vma=False,
    )
```

```python
import functools
import math

import jax
import jax.numpy as jnp
from jax import lax
from jax.experimental import pallas as pl
from jax.experimental.pallas import tpu as pltpu
from jax.sharding import PartitionSpec as P

W = 128
LIST = 48


lowest_score = -1e30


def xor_pairs(n, k):
    return [(i, i ^ k) for i in range(n)]


def is_pow2(n):
    return n & (n - 1) == 0


def angle_tables(freqs, coords, size, width):
    offsets = jnp.arange(width, dtype=jnp.int32) - width // 2
    position = (coords[:, None] + offsets[None, :]) % size
    phase = freqs[None, :, None] * position[:, None, :] % size
    angle = phase.astype(jnp.float32) * (2.0 * math.pi / size)
    return (jnp.cos(angle).astype(jnp.bfloat16), jnp.sin(angle).astype(jnp.bfloat16))


def col_tables(peak_rows, size, width):
    freqs = jnp.arange(size, dtype=jnp.int32)
    cos_col, sin_col = angle_tables(freqs, peak_rows[:, 1], size, width)
    upper = jnp.concatenate([cos_col, sin_col], axis=-1)
    lower = jnp.concatenate([-sin_col, cos_col], axis=-1)
    return jnp.concatenate([upper, lower], axis=1)


def gather_rows(part, axis):
    n = lax.axis_size(axis)
    if not is_pow2(n):
        return lax.all_gather(part, axis)
    me = lax.axis_index(axis)
    blocks = part[None]
    k = n // 2
    while k >= 1:
        got = lax.ppermute(blocks, axis, xor_pairs(n, k))
        blocks = jnp.concatenate([blocks, got])
        k //= 2
    want = jnp.arange(n, dtype=jnp.int32) ^ me
    return blocks[order_of(want, n)]


def order_of(want, count):
    steps = int(math.log2(count))
    slot = jnp.zeros_like(want)
    for j in range(steps):
        k = count >> (j + 1)
        hit = (want & k) != 0
        slot = slot | jnp.where(hit, 1 << j, 0)
    return slot


def reduce_orient(best_part, power_part, axis):
    n = lax.axis_size(axis)
    if not is_pow2(n):
        best = lax.pmax(best_part, axis)
        power = lax.psum(power_part, axis)
        return best, power
    width = best_part.shape[-1]
    joined = jnp.stack([best_part.reshape(-1, width), power_part.reshape(-1, width)], axis=0)
    me = lax.axis_index(axis)
    cur = joined
    k = 1
    while k < n:
        half = cur.shape[1] // 2
        bit = (me // k) % 2
        keep = lax.dynamic_slice_in_dim(cur, bit * half, half, axis=1)
        send = lax.dynamic_slice_in_dim(cur, (1 - bit) * half, half, axis=1)
        got = lax.ppermute(send, axis, xor_pairs(n, k))
        cur = jnp.stack([jnp.maximum(keep[0], got[0]), keep[1] + got[1]])
        k *= 2
    k = n // 2
    while k >= 1:
        got = lax.ppermute(cur, axis, xor_pairs(n, k))
        bit = (me // k) % 2
        cur = jnp.where(bit == 1, jnp.concatenate([got, cur], axis=1), jnp.concatenate([cur, got], axis=1))
        k //= 2
    best = cur[0].reshape(best_part.shape)
    power = cur[1].reshape(power_part.shape)
    return best, power


def match_kernel(blocks, size, width, rows_t, tiles, peaks_n, l_ref, tm_ref, sp_ref, ct_ref, cr_ref, sr_ref, best_ref, pow_ref, m_ref):
    j = pl.program_id(0)

    @pl.when(j == 0)
    def _():
        best_ref[...] = jnp.full(best_ref.shape, lowest_score, jnp.float32)
        pow_ref[...] = jnp.zeros(pow_ref.shape, jnp.float32)

    for t in range(tiles):
        rows = pl.ds(t * rows_t, rows_t)
        image_re = sp_ref[0, rows, :].astype(jnp.float32)
        image_im = sp_ref[1, rows, :].astype(jnp.float32)
        tmpl_re = tm_ref[t, 0, 0].astype(jnp.float32)
        tmpl_im = tm_ref[t, 0, 1].astype(jnp.float32)
        m_ref[rows, pl.ds(0, size)] = (image_re * tmpl_re + image_im * tmpl_im).astype(jnp.bfloat16)
        m_ref[rows, pl.ds(size, size)] = (image_im * tmpl_re - image_re * tmpl_im).astype(jnp.bfloat16)

    for p in range(peaks_n):
        @pl.when(l_ref[p * blocks + j] > 0)
        def _():
            g = jnp.dot(m_ref[...], ct_ref[p], preferred_element_type=jnp.float32).astype(jnp.bfloat16)
            score = jnp.dot(cr_ref[p], g[:, :width], preferred_element_type=jnp.float32)
            score = score - jnp.dot(sr_ref[p], g[:, width:], preferred_element_type=jnp.float32)
            score = score / size
            best_ref[p] = jnp.maximum(best_ref[p], score)
            pow_ref[p] = pow_ref[p] + score * score


def match(flags, tmpl, spec, col_table, cos_t, sin_t):
    tiles, blocks, _, rows_t, size = tmpl.shape
    peaks_n, width = cos_t.shape[0], cos_t.shape[1]
    kernel = functools.partial(match_kernel, blocks, size, width, rows_t, tiles, peaks_n)
    flops = blocks * peaks_n * (2 * size * 2 * size * 2 * width + 2 * 2 * width * size * width)
    cost = pl.CostEstimate(flops=flops, transcendentals=0, bytes_accessed=tmpl.size * 2 + spec.size * 2 + col_table.size * 2)
    out = jax.ShapeDtypeStruct((peaks_n, width, width), jnp.float32)
    return pl.pallas_call(
        kernel,
        grid_spec=pltpu.PrefetchScalarGridSpec(
            num_scalar_prefetch=1,
            grid=(blocks,),
            in_specs=[
                pl.BlockSpec((tiles, 1, 2, rows_t, size), lambda j, l: (0, j, 0, 0, 0)),
                pl.BlockSpec((2, size, size), lambda j, l: (0, 0, 0)),
                pl.BlockSpec(col_table.shape, lambda j, l: (0, 0, 0)),
                pl.BlockSpec(cos_t.shape, lambda j, l: (0, 0, 0)),
                pl.BlockSpec(sin_t.shape, lambda j, l: (0, 0, 0)),
            ],
            out_specs=[
                pl.BlockSpec((peaks_n, width, width), lambda j, l: (0, 0, 0)),
                pl.BlockSpec((peaks_n, width, width), lambda j, l: (0, 0, 0)),
            ],
            scratch_shapes=[pltpu.VMEM((size, 2 * size), jnp.bfloat16)],
        ),
        out_shape=[out, out],
        compiler_params=pltpu.CompilerParams(dimension_semantics=("arbitrary",)),
        cost_estimate=cost,
    )(flags, tmpl, spec, col_table, cos_t, sin_t)


def local(tile_spectra, template_spectra, peaks, listed):
    size = tile_spectra.shape[3]
    width = W
    tmpl = lax.all_gather(template_spectra, "tile", axis=0)
    block_size = tmpl.shape[1]
    spec = gather_rows(tile_spectra[0], "orient")
    spec = jnp.moveaxis(spec, 0, 1).reshape(2, size, size)
    freqs = jnp.arange(size, dtype=jnp.int32)
    cos_row, sin_row = angle_tables(freqs, peaks[0][:, 0], size, width)
    cos_t = jnp.swapaxes(cos_row, 1, 2)
    sin_t = jnp.swapaxes(sin_row, 1, 2)
    col_table = col_tables(peaks[0], size, width)
    listed_ids = listed[0]
    global_ids = lax.axis_index("orient") * block_size + jnp.arange(block_size, dtype=jnp.int32)
    is_listed = jnp.any(listed_ids[:, :, None] == global_ids[None, None, :], axis=1)
    flags = is_listed.astype(jnp.int32).reshape(-1)
    best_part, power_part = match(flags, tmpl, spec, col_table, cos_t, sin_t)
    best_all, power_all = reduce_orient(best_part, power_part, "orient")
    return (best_all[None], (power_all / LIST)[None])


def solution(mesh):
    placed = (
        P("tile", None, "orient", None),
        P("orient", None, "tile", None),
        P("tile", None, None),
        P("tile", None, None),
    )
    return jax.shard_map(
        local,
        mesh=mesh,
        in_specs=placed,
        out_specs=(P("tile", None, None, None), P("tile", None, None, None)),
        check_vma=False,
    )
```

```python
import functools
import math

import jax
import jax.numpy as jnp
from jax import lax
from jax.experimental import pallas as pl
from jax.experimental.pallas import tpu as pltpu
from jax.sharding import PartitionSpec as P

W = 128
LIST = 48


lowest_score = -1e30


def xor_pairs(n, k):
    return [(i, i ^ k) for i in range(n)]


def is_pow2(n):
    return n & (n - 1) == 0


def angle_tables(freqs, coords, size, width):
    offsets = jnp.arange(width, dtype=jnp.int32) - width // 2
    position = (coords[:, None] + offsets[None, :]) % size
    phase = freqs[None, :, None] * position[:, None, :] % size
    angle = phase.astype(jnp.float32) * (2.0 * math.pi / size)
    return (jnp.cos(angle).astype(jnp.bfloat16), jnp.sin(angle).astype(jnp.bfloat16))


def col_tables(peak_rows, size, width):
    freqs = jnp.arange(size, dtype=jnp.int32)
    cos_col, sin_col = angle_tables(freqs, peak_rows[:, 1], size, width)
    upper = jnp.concatenate([cos_col, sin_col], axis=-1)
    lower = jnp.concatenate([-sin_col, cos_col], axis=-1)
    return jnp.concatenate([upper, lower], axis=1)


def gather_rows(part, axis):
    n = lax.axis_size(axis)
    if not is_pow2(n):
        return lax.all_gather(part, axis)
    me = lax.axis_index(axis)
    blocks = part[None]
    k = n // 2
    while k >= 1:
        got = lax.ppermute(blocks, axis, xor_pairs(n, k))
        blocks = jnp.concatenate([blocks, got])
        k //= 2
    want = jnp.arange(n, dtype=jnp.int32) ^ me
    return blocks[order_of(want, n)]


def order_of(want, count):
    steps = int(math.log2(count))
    slot = jnp.zeros_like(want)
    for j in range(steps):
        k = count >> (j + 1)
        hit = (want & k) != 0
        slot = slot | jnp.where(hit, 1 << j, 0)
    return slot


def reduce_orient(best_part, power_part, axis):
    n = lax.axis_size(axis)
    if not is_pow2(n):
        best = lax.pmax(best_part, axis)
        power = lax.psum(power_part, axis)
        return best, power
    width = best_part.shape[-1]
    joined = jnp.stack([best_part.reshape(-1, width), power_part.reshape(-1, width)], axis=0)
    me = lax.axis_index(axis)
    cur = joined
    k = 1
    while k < n:
        half = cur.shape[1] // 2
        bit = (me // k) % 2
        keep = lax.dynamic_slice_in_dim(cur, bit * half, half, axis=1)
        send = lax.dynamic_slice_in_dim(cur, (1 - bit) * half, half, axis=1)
        got = lax.ppermute(send, axis, xor_pairs(n, k))
        cur = jnp.stack([jnp.maximum(keep[0], got[0]), keep[1] + got[1]])
        k *= 2
    k = n // 2
    while k >= 1:
        got = lax.ppermute(cur, axis, xor_pairs(n, k))
        bit = (me // k) % 2
        cur = jnp.where(bit == 1, jnp.concatenate([got, cur], axis=1), jnp.concatenate([cur, got], axis=1))
        k //= 2
    best = cur[0].reshape(best_part.shape)
    power = cur[1].reshape(power_part.shape)
    return best, power


def match_kernel(blocks, size, width, rows_t, tiles, peaks_n, chunk, l_ref, tm_ref, sp_ref, ct_ref, cr_ref, sr_ref, best_ref, pow_ref, m_ref):
    j = pl.program_id(0)

    @pl.when(j == 0)
    def _():
        best_ref[...] = jnp.full(best_ref.shape, lowest_score, jnp.float32)
        pow_ref[...] = jnp.zeros(pow_ref.shape, jnp.float32)

    per_tile = rows_t // chunk

    def mix(c, carry):
        t = c // per_tile
        row = pl.multiple_of(c * chunk, chunk)
        local_row = pl.multiple_of((c % per_tile) * chunk, chunk)
        image_re = sp_ref[0, pl.ds(row, chunk), :]
        image_im = sp_ref[1, pl.ds(row, chunk), :]
        tmpl_re = tm_ref[t, 0, 0, pl.ds(local_row, chunk), :].astype(jnp.float32)
        tmpl_im = tm_ref[t, 0, 1, pl.ds(local_row, chunk), :].astype(jnp.float32)
        m_ref[pl.ds(row, chunk), pl.ds(0, size)] = (image_re * tmpl_re + image_im * tmpl_im).astype(jnp.bfloat16)
        m_ref[pl.ds(row, chunk), pl.ds(size, size)] = (image_im * tmpl_re - image_re * tmpl_im).astype(jnp.bfloat16)
        return carry

    lax.fori_loop(0, tiles * per_tile, mix, 0, unroll=4)

    for p in range(peaks_n):
        @pl.when(l_ref[p * blocks + j] > 0)
        def _():
            g = jnp.dot(m_ref[...], ct_ref[p], preferred_element_type=jnp.float32).astype(jnp.bfloat16)
            score = jnp.dot(cr_ref[p], g[:, :width], preferred_element_type=jnp.float32)
            score = score - jnp.dot(sr_ref[p], g[:, width:], preferred_element_type=jnp.float32)
            score = score / size
            best_ref[p] = jnp.maximum(best_ref[p], score)
            pow_ref[p] = pow_ref[p] + score * score


def match(flags, tmpl, spec, col_table, cos_t, sin_t):
    tiles, blocks, _, rows_t, size = tmpl.shape
    peaks_n, width = cos_t.shape[0], cos_t.shape[1]
    chunk = math.gcd(rows_t, 16)
    kernel = functools.partial(match_kernel, blocks, size, width, rows_t, tiles, peaks_n, chunk)
    flops = blocks * peaks_n * (2 * size * 2 * size * 2 * width + 2 * 2 * width * size * width)
    cost = pl.CostEstimate(flops=flops, transcendentals=0, bytes_accessed=tmpl.size * 2 + spec.size * 4 + col_table.size * 2)
    out = jax.ShapeDtypeStruct((peaks_n, width, width), jnp.float32)
    return pl.pallas_call(
        kernel,
        grid_spec=pltpu.PrefetchScalarGridSpec(
            num_scalar_prefetch=1,
            grid=(blocks,),
            in_specs=[
                pl.BlockSpec((tiles, 1, 2, rows_t, size), lambda j, l: (0, j, 0, 0, 0)),
                pl.BlockSpec((2, size, size), lambda j, l: (0, 0, 0)),
                pl.BlockSpec(col_table.shape, lambda j, l: (0, 0, 0)),
                pl.BlockSpec(cos_t.shape, lambda j, l: (0, 0, 0)),
                pl.BlockSpec(sin_t.shape, lambda j, l: (0, 0, 0)),
            ],
            out_specs=[
                pl.BlockSpec((peaks_n, width, width), lambda j, l: (0, 0, 0)),
                pl.BlockSpec((peaks_n, width, width), lambda j, l: (0, 0, 0)),
            ],
            scratch_shapes=[pltpu.VMEM((size, 2 * size), jnp.bfloat16)],
        ),
        out_shape=[out, out],
        compiler_params=pltpu.CompilerParams(dimension_semantics=("arbitrary",)),
        cost_estimate=cost,
    )(flags, tmpl, spec, col_table, cos_t, sin_t)


def local(tile_spectra, template_spectra, peaks, listed):
    size = tile_spectra.shape[3]
    width = W
    block_size = template_spectra.shape[0]
    spec = gather_rows(tile_spectra[0], "orient")
    spec = jnp.moveaxis(spec, 0, 1).reshape(2, size, size).astype(jnp.float32)
    freqs = jnp.arange(size, dtype=jnp.int32)
    cos_row, sin_row = angle_tables(freqs, peaks[0][:, 0], size, width)
    cos_t = jnp.swapaxes(cos_row, 1, 2)
    sin_t = jnp.swapaxes(sin_row, 1, 2)
    col_table = col_tables(peaks[0], size, width)
    listed_ids = listed[0]
    halves = 2 if block_size % 2 == 0 else 1
    part = block_size // halves
    best_part, power_part = None, None
    for h in range(halves):
        tmpl = lax.all_gather(template_spectra[h * part:(h + 1) * part], "tile", axis=0)
        global_ids = lax.axis_index("orient") * block_size + h * part + jnp.arange(part, dtype=jnp.int32)
        is_listed = jnp.any(listed_ids[:, :, None] == global_ids[None, None, :], axis=1)
        flags = is_listed.astype(jnp.int32).reshape(-1)
        best_h, power_h = match(flags, tmpl, spec, col_table, cos_t, sin_t)
        if best_part is None:
            best_part, power_part = best_h, power_h
        else:
            best_part = jnp.maximum(best_part, best_h)
            power_part = power_part + power_h
    best_all, power_all = reduce_orient(best_part, power_part, "orient")
    return (best_all[None], (power_all / LIST)[None])


def solution(mesh):
    placed = (
        P("tile", None, "orient", None),
        P("orient", None, "tile", None),
        P("tile", None, None),
        P("tile", None, None),
    )
    return jax.shard_map(
        local,
        mesh=mesh,
        in_specs=placed,
        out_specs=(P("tile", None, None, None), P("tile", None, None, None)),
        check_vma=False,
    )
```

```python
import functools
import math

import jax
import jax.numpy as jnp
from jax import lax
from jax.experimental import pallas as pl
from jax.experimental.pallas import tpu as pltpu
from jax.sharding import PartitionSpec as P

W = 128
LIST = 48


lowest_score = -1e30


def xor_pairs(n, k):
    return [(i, i ^ k) for i in range(n)]


def is_pow2(n):
    return n & (n - 1) == 0


def angle_tables(freqs, coords, size, width):
    offsets = jnp.arange(width, dtype=jnp.int32) - width // 2
    position = (coords[:, None] + offsets[None, :]) % size
    phase = freqs[None, :, None] * position[:, None, :] % size
    angle = phase.astype(jnp.float32) * (2.0 * math.pi / size)
    return (jnp.cos(angle).astype(jnp.bfloat16), jnp.sin(angle).astype(jnp.bfloat16))


def col_tables(peak_rows, size, width):
    freqs = jnp.arange(size, dtype=jnp.int32)
    cos_col, sin_col = angle_tables(freqs, peak_rows[:, 1], size, width)
    upper = jnp.concatenate([cos_col, sin_col], axis=-1)
    lower = jnp.concatenate([-sin_col, cos_col], axis=-1)
    return jnp.concatenate([upper, lower], axis=1)


def gather_rows(part, axis):
    n = lax.axis_size(axis)
    if not is_pow2(n):
        return lax.all_gather(part, axis)
    me = lax.axis_index(axis)
    blocks = part[None]
    k = n // 2
    while k >= 1:
        got = lax.ppermute(blocks, axis, xor_pairs(n, k))
        blocks = jnp.concatenate([blocks, got])
        k //= 2
    want = jnp.arange(n, dtype=jnp.int32) ^ me
    return blocks[order_of(want, n)]


def order_of(want, count):
    steps = int(math.log2(count))
    slot = jnp.zeros_like(want)
    for j in range(steps):
        k = count >> (j + 1)
        hit = (want & k) != 0
        slot = slot | jnp.where(hit, 1 << j, 0)
    return slot


def reduce_orient(best_part, power_part, axis):
    n = lax.axis_size(axis)
    if not is_pow2(n):
        best = lax.pmax(best_part, axis)
        power = lax.psum(power_part, axis)
        return best, power
    width = best_part.shape[-1]
    joined = jnp.stack([best_part.reshape(-1, width), power_part.reshape(-1, width)], axis=0)
    me = lax.axis_index(axis)
    cur = joined
    k = 1
    while k < n:
        half = cur.shape[1] // 2
        bit = (me // k) % 2
        keep = lax.dynamic_slice_in_dim(cur, bit * half, half, axis=1)
        send = lax.dynamic_slice_in_dim(cur, (1 - bit) * half, half, axis=1)
        got = lax.ppermute(send, axis, xor_pairs(n, k))
        cur = jnp.stack([jnp.maximum(keep[0], got[0]), keep[1] + got[1]])
        k *= 2
    k = n // 2
    while k >= 1:
        got = lax.ppermute(cur, axis, xor_pairs(n, k))
        bit = (me // k) % 2
        cur = jnp.where(bit == 1, jnp.concatenate([got, cur], axis=1), jnp.concatenate([cur, got], axis=1))
        k //= 2
    best = cur[0].reshape(best_part.shape)
    power = cur[1].reshape(power_part.shape)
    return best, power


def match_kernel(blocks, size, width, rows_t, tiles, peaks_n, l_ref, tm_ref, sp_ref, ct_ref, cr_ref, sr_ref, best_ref, pow_ref, m_ref):
    j = pl.program_id(0)

    @pl.when(j == 0)
    def _():
        best_ref[...] = jnp.full(best_ref.shape, lowest_score, jnp.float32)
        pow_ref[...] = jnp.zeros(pow_ref.shape, jnp.float32)

    for t in range(tiles):
        rows = pl.ds(t * rows_t, rows_t)
        image_re = sp_ref[0, rows, :].astype(jnp.float32)
        image_im = sp_ref[1, rows, :].astype(jnp.float32)
        tmpl_re = tm_ref[t, 0, 0].astype(jnp.float32)
        tmpl_im = tm_ref[t, 0, 1].astype(jnp.float32)
        m_ref[rows, pl.ds(0, size)] = (image_re * tmpl_re + image_im * tmpl_im).astype(jnp.bfloat16)
        m_ref[rows, pl.ds(size, size)] = (image_im * tmpl_re - image_re * tmpl_im).astype(jnp.bfloat16)

    for p in range(peaks_n):
        @pl.when(l_ref[p * blocks + j] > 0)
        def _():
            g = jnp.dot(m_ref[...], ct_ref[p], preferred_element_type=jnp.float32).astype(jnp.bfloat16)
            score = jnp.dot(cr_ref[p], g[:, :width], preferred_element_type=jnp.float32)
            score = score - jnp.dot(sr_ref[p], g[:, width:], preferred_element_type=jnp.float32)
            score = score / size
            best_ref[p] = jnp.maximum(best_ref[p], score)
            pow_ref[p] = pow_ref[p] + score * score


def match(flags, tmpl, spec, col_table, cos_t, sin_t):
    tiles, blocks, _, rows_t, size = tmpl.shape
    peaks_n, width = cos_t.shape[0], cos_t.shape[1]
    kernel = functools.partial(match_kernel, blocks, size, width, rows_t, tiles, peaks_n)
    flops = blocks * peaks_n * (2 * size * 2 * size * 2 * width + 2 * 2 * width * size * width)
    cost = pl.CostEstimate(flops=flops, transcendentals=0, bytes_accessed=tmpl.size * 2 + spec.size * 2 + col_table.size * 2)
    out = jax.ShapeDtypeStruct((peaks_n, width, width), jnp.float32)
    return pl.pallas_call(
        kernel,
        grid_spec=pltpu.PrefetchScalarGridSpec(
            num_scalar_prefetch=1,
            grid=(blocks,),
            in_specs=[
                pl.BlockSpec((tiles, 1, 2, rows_t, size), lambda j, l: (0, j, 0, 0, 0)),
                pl.BlockSpec((2, size, size), lambda j, l: (0, 0, 0)),
                pl.BlockSpec(col_table.shape, lambda j, l: (0, 0, 0)),
                pl.BlockSpec(cos_t.shape, lambda j, l: (0, 0, 0)),
                pl.BlockSpec(sin_t.shape, lambda j, l: (0, 0, 0)),
            ],
            out_specs=[
                pl.BlockSpec((peaks_n, width, width), lambda j, l: (0, 0, 0)),
                pl.BlockSpec((peaks_n, width, width), lambda j, l: (0, 0, 0)),
            ],
            scratch_shapes=[pltpu.VMEM((size, 2 * size), jnp.bfloat16)],
        ),
        out_shape=[out, out],
        compiler_params=pltpu.CompilerParams(dimension_semantics=("arbitrary",)),
        cost_estimate=cost,
    )(flags, tmpl, spec, col_table, cos_t, sin_t)


def rows_kernel(blocks, size, width, rows_t, peaks_n, chunk, n_steps, final, f_ref, tid_ref, rid_ref, tm_ref, sp_ref, ct_ref, cr_ref, sr_ref, *rest):
    if final:
        init_ref, best_ref, pow_ref, acc_ref, m_ref = rest
    else:
        part_ref, acc_ref, m_ref = rest
    j = pl.program_id(0)
    i = pl.program_id(1)

    if final:
        @pl.when((j == 0) & (i == 0))
        def _():
            best_ref[...] = jnp.full(best_ref.shape, lowest_score, jnp.float32)
            pow_ref[...] = jnp.zeros(pow_ref.shape, jnp.float32)

        @pl.when(i == 0)
        def _():
            acc_ref[...] = init_ref[:, 0]
    else:
        @pl.when(i == 0)
        def _():
            acc_ref[...] = jnp.zeros(acc_ref.shape, jnp.float32)

    def mix(c, carry):
        row = pl.multiple_of(c * chunk, chunk)
        image_re = sp_ref[0, pl.ds(row, chunk), :]
        image_im = sp_ref[1, pl.ds(row, chunk), :]
        tmpl_re = tm_ref[0, 0, 0, pl.ds(row, chunk), :].astype(jnp.float32)
        tmpl_im = tm_ref[0, 0, 1, pl.ds(row, chunk), :].astype(jnp.float32)
        m_ref[pl.ds(row, chunk), pl.ds(0, size)] = (image_re * tmpl_re + image_im * tmpl_im).astype(jnp.bfloat16)
        m_ref[pl.ds(row, chunk), pl.ds(size, size)] = (image_im * tmpl_re - image_re * tmpl_im).astype(jnp.bfloat16)
        return carry

    lax.fori_loop(0, rows_t // chunk, mix, 0, unroll=4)

    for p in range(peaks_n):
        @pl.when(f_ref[p * blocks + j] > 0)
        def _():
            g = jnp.dot(m_ref[...], ct_ref[p], preferred_element_type=jnp.float32).astype(jnp.bfloat16)
            part = jnp.dot(cr_ref[p], g[:, :width], preferred_element_type=jnp.float32)
            part = part - jnp.dot(sr_ref[p], g[:, width:], preferred_element_type=jnp.float32)
            acc_ref[p] = acc_ref[p] + part

    @pl.when(i == n_steps - 1)
    def _():
        if final:
            for p in range(peaks_n):
                @pl.when(f_ref[p * blocks + j] > 0)
                def _():
                    score = acc_ref[p] / size
                    best_ref[p] = jnp.maximum(best_ref[p], score)
                    pow_ref[p] = pow_ref[p] + score * score
        else:
            part_ref[:, 0] = acc_ref[...]


def match_rows(flags, tids, rids, tmpl, spec, col_table, cos_t, sin_t, init=None):
    _, blocks, _, rows_t, size = tmpl.shape
    peaks_n, width = cos_t.shape[0], cos_t.shape[1]
    n_steps = tids.shape[0]
    final = init is not None
    chunk = math.gcd(rows_t, 16)
    kernel = functools.partial(rows_kernel, blocks, size, width, rows_t, peaks_n, chunk, n_steps, final)
    flops = blocks * peaks_n * n_steps * (2 * rows_t * 2 * size * 2 * width + 2 * 2 * width * rows_t * width)
    cost = pl.CostEstimate(flops=flops, transcendentals=0, bytes_accessed=n_steps * blocks * 2 * rows_t * size * 6 + col_table.size * 2)
    in_specs = [
        pl.BlockSpec((1, 1, 2, rows_t, size), lambda j, i, f, t, r: (t[i], j, 0, 0, 0)),
        pl.BlockSpec((2, rows_t, size), lambda j, i, f, t, r: (0, r[i], 0)),
        pl.BlockSpec(col_table.shape, lambda j, i, f, t, r: (0, 0, 0)),
        pl.BlockSpec((peaks_n, width, rows_t), lambda j, i, f, t, r: (0, 0, r[i])),
        pl.BlockSpec((peaks_n, width, rows_t), lambda j, i, f, t, r: (0, 0, r[i])),
    ]
    args = [flags, tids, rids, tmpl, spec, col_table, cos_t, sin_t]
    part_spec = pl.BlockSpec((peaks_n, 1, width, width), lambda j, i, f, t, r: (0, j, 0, 0))
    if final:
        in_specs.append(part_spec)
        args.append(init)
        out = jax.ShapeDtypeStruct((peaks_n, width, width), jnp.float32)
        out_shape = [out, out]
        out_specs = [pl.BlockSpec((peaks_n, width, width), lambda j, i, f, t, r: (0, 0, 0))] * 2
    else:
        out_shape = jax.ShapeDtypeStruct((peaks_n, blocks, width, width), jnp.float32)
        out_specs = part_spec
    return pl.pallas_call(
        kernel,
        grid_spec=pltpu.PrefetchScalarGridSpec(
            num_scalar_prefetch=3,
            grid=(blocks, n_steps),
            in_specs=in_specs,
            out_specs=out_specs,
            scratch_shapes=[pltpu.VMEM((peaks_n, width, width), jnp.float32), pltpu.VMEM((rows_t, 2 * size), jnp.bfloat16)],
        ),
        out_shape=out_shape,
        compiler_params=pltpu.CompilerParams(dimension_semantics=("arbitrary", "arbitrary")),
        cost_estimate=cost,
    )(*args)


def local(tile_spectra, template_spectra, peaks, listed):
    size = tile_spectra.shape[3]
    width = W
    tiles = lax.axis_size("tile")
    rows_t = template_spectra.shape[2]
    tmpl = lax.all_gather(template_spectra, "tile", axis=0)
    block_size = tmpl.shape[1]
    spec = gather_rows(tile_spectra[0], "orient")
    spec = jnp.moveaxis(spec, 0, 1).reshape(2, size, size)
    freqs = jnp.arange(size, dtype=jnp.int32)
    cos_row, sin_row = angle_tables(freqs, peaks[0][:, 0], size, width)
    cos_t = jnp.swapaxes(cos_row, 1, 2)
    sin_t = jnp.swapaxes(sin_row, 1, 2)
    col_table = col_tables(peaks[0], size, width)
    listed_ids = listed[0]
    global_ids = lax.axis_index("orient") * block_size + jnp.arange(block_size, dtype=jnp.int32)
    is_listed = jnp.any(listed_ids[:, :, None] == global_ids[None, None, :], axis=1)
    flags = is_listed.astype(jnp.int32).reshape(-1)
    if rows_t % 128 != 0 or tiles % 2 != 0:
        best_part, power_part = match(flags, tmpl, spec, col_table, cos_t, sin_t)
    else:
        me = lax.axis_index("tile")
        sibling = lax.ppermute(template_spectra, "tile", xor_pairs(tiles, 1))
        near = jnp.stack([template_spectra, sibling])
        spec32 = spec.astype(jnp.float32)
        near_rows = jnp.stack([me, me ^ 1]).astype(jnp.int32)
        partial = match_rows(flags, jnp.arange(2, dtype=jnp.int32), near_rows, near, spec32, col_table, cos_t, sin_t)
        far_rows = far_blocks(me, tiles)
        best_part, power_part = match_rows(flags, far_rows, far_rows, tmpl, spec32, col_table, cos_t, sin_t, init=partial)
    best_all, power_all = reduce_orient(best_part, power_part, "orient")
    return (best_all[None], (power_all / LIST)[None])


def far_blocks(me, tiles):
    steps = jnp.arange(tiles - 2, dtype=jnp.int32)
    pair = steps // 2
    chip = me // 2
    pair = pair + (pair >= chip).astype(jnp.int32)
    return pair * 2 + steps % 2


def solution(mesh):
    placed = (
        P("tile", None, "orient", None),
        P("orient", None, "tile", None),
        P("tile", None, None),
        P("tile", None, None),
    )
    return jax.shard_map(
        local,
        mesh=mesh,
        in_specs=placed,
        out_specs=(P("tile", None, None, None), P("tile", None, None, None)),
        check_vma=False,
    )
```

```python
import functools
import math

import jax
import jax.numpy as jnp
from jax import lax
from jax.experimental import pallas as pl
from jax.experimental.pallas import tpu as pltpu
from jax.sharding import PartitionSpec as P

W = 128
LIST = 48


lowest_score = -1e30


def xor_pairs(n, k):
    return [(i, i ^ k) for i in range(n)]


def is_pow2(n):
    return n & (n - 1) == 0


def angle_tables(freqs, coords, size, width):
    offsets = jnp.arange(width, dtype=jnp.int32) - width // 2
    position = (coords[:, None] + offsets[None, :]) % size
    phase = freqs[None, :, None] * position[:, None, :] % size
    angle = phase.astype(jnp.float32) * (2.0 * math.pi / size)
    return (jnp.cos(angle).astype(jnp.bfloat16), jnp.sin(angle).astype(jnp.bfloat16))


def col_tables(peak_rows, size, width):
    freqs = jnp.arange(size, dtype=jnp.int32)
    cos_col, sin_col = angle_tables(freqs, peak_rows[:, 1], size, width)
    upper = jnp.concatenate([cos_col, sin_col], axis=-1)
    lower = jnp.concatenate([-sin_col, cos_col], axis=-1)
    return jnp.concatenate([upper, lower], axis=1)


def gather_rows(part, axis):
    n = lax.axis_size(axis)
    if not is_pow2(n):
        return lax.all_gather(part, axis)
    me = lax.axis_index(axis)
    blocks = part[None]
    k = n // 2
    while k >= 1:
        got = lax.ppermute(blocks, axis, xor_pairs(n, k))
        blocks = jnp.concatenate([blocks, got])
        k //= 2
    want = jnp.arange(n, dtype=jnp.int32) ^ me
    return blocks[order_of(want, n)]


def order_of(want, count):
    steps = int(math.log2(count))
    slot = jnp.zeros_like(want)
    for j in range(steps):
        k = count >> (j + 1)
        hit = (want & k) != 0
        slot = slot | jnp.where(hit, 1 << j, 0)
    return slot


def reduce_orient(best_part, power_part, axis):
    n = lax.axis_size(axis)
    if not is_pow2(n):
        best = lax.pmax(best_part, axis)
        power = lax.psum(power_part, axis)
        return best, power
    width = best_part.shape[-1]
    joined = jnp.stack([best_part.reshape(-1, width), power_part.reshape(-1, width)], axis=0)
    me = lax.axis_index(axis)
    cur = joined
    k = 1
    while k < n:
        half = cur.shape[1] // 2
        bit = (me // k) % 2
        keep = lax.dynamic_slice_in_dim(cur, bit * half, half, axis=1)
        send = lax.dynamic_slice_in_dim(cur, (1 - bit) * half, half, axis=1)
        got = lax.ppermute(send, axis, xor_pairs(n, k))
        cur = jnp.stack([jnp.maximum(keep[0], got[0]), keep[1] + got[1]])
        k *= 2
    k = n // 2
    while k >= 1:
        got = lax.ppermute(cur, axis, xor_pairs(n, k))
        bit = (me // k) % 2
        cur = jnp.where(bit == 1, jnp.concatenate([got, cur], axis=1), jnp.concatenate([cur, got], axis=1))
        k //= 2
    best = cur[0].reshape(best_part.shape)
    power = cur[1].reshape(power_part.shape)
    return best, power


def match_kernel(blocks, size, width, rows_t, tiles, peaks_n, l_ref, tm_ref, sp_ref, ct_ref, cr_ref, sr_ref, best_ref, pow_ref, m_ref):
    j = pl.program_id(0)

    @pl.when(j == 0)
    def _():
        best_ref[...] = jnp.full(best_ref.shape, lowest_score, jnp.float32)
        pow_ref[...] = jnp.zeros(pow_ref.shape, jnp.float32)

    for t in range(tiles):
        rows = pl.ds(t * rows_t, rows_t)
        image_re = sp_ref[0, rows, :].astype(jnp.float32)
        image_im = sp_ref[1, rows, :].astype(jnp.float32)
        tmpl_re = tm_ref[t, 0, 0].astype(jnp.float32)
        tmpl_im = tm_ref[t, 0, 1].astype(jnp.float32)
        m_ref[rows, pl.ds(0, size)] = (image_re * tmpl_re + image_im * tmpl_im).astype(jnp.bfloat16)
        m_ref[rows, pl.ds(size, size)] = (image_im * tmpl_re - image_re * tmpl_im).astype(jnp.bfloat16)

    for p in range(peaks_n):
        @pl.when(l_ref[p * blocks + j] > 0)
        def _():
            g = jnp.dot(m_ref[...], ct_ref[p], preferred_element_type=jnp.float32).astype(jnp.bfloat16)
            score = jnp.dot(cr_ref[p], g[:, :width], preferred_element_type=jnp.float32)
            score = score - jnp.dot(sr_ref[p], g[:, width:], preferred_element_type=jnp.float32)
            score = score / size
            best_ref[p] = jnp.maximum(best_ref[p], score)
            pow_ref[p] = pow_ref[p] + score * score


def match(flags, tmpl, spec, col_table, cos_t, sin_t):
    tiles, blocks, _, rows_t, size = tmpl.shape
    peaks_n, width = cos_t.shape[0], cos_t.shape[1]
    kernel = functools.partial(match_kernel, blocks, size, width, rows_t, tiles, peaks_n)
    flops = blocks * peaks_n * (2 * size * 2 * size * 2 * width + 2 * 2 * width * size * width)
    cost = pl.CostEstimate(flops=flops, transcendentals=0, bytes_accessed=tmpl.size * 2 + spec.size * 2 + col_table.size * 2)
    out = jax.ShapeDtypeStruct((peaks_n, width, width), jnp.float32)
    return pl.pallas_call(
        kernel,
        grid_spec=pltpu.PrefetchScalarGridSpec(
            num_scalar_prefetch=1,
            grid=(blocks,),
            in_specs=[
                pl.BlockSpec((tiles, 1, 2, rows_t, size), lambda j, l: (0, j, 0, 0, 0)),
                pl.BlockSpec((2, size, size), lambda j, l: (0, 0, 0)),
                pl.BlockSpec(col_table.shape, lambda j, l: (0, 0, 0)),
                pl.BlockSpec(cos_t.shape, lambda j, l: (0, 0, 0)),
                pl.BlockSpec(sin_t.shape, lambda j, l: (0, 0, 0)),
            ],
            out_specs=[
                pl.BlockSpec((peaks_n, width, width), lambda j, l: (0, 0, 0)),
                pl.BlockSpec((peaks_n, width, width), lambda j, l: (0, 0, 0)),
            ],
            scratch_shapes=[pltpu.VMEM((size, 2 * size), jnp.bfloat16)],
        ),
        out_shape=[out, out],
        compiler_params=pltpu.CompilerParams(dimension_semantics=("arbitrary",)),
        cost_estimate=cost,
    )(flags, tmpl, spec, col_table, cos_t, sin_t)


def rows_kernel(blocks, size, width, rows_t, peaks_n, chunk, n_steps, final, f_ref, ta_ref, tb_ref, rid_ref, tma_ref, tmb_ref, sp_ref, ct_ref, cr_ref, sr_ref, *rest):
    if final:
        init_ref, best_ref, pow_ref, acc_ref, m_ref = rest
    else:
        part_ref, acc_ref, m_ref = rest
    j = pl.program_id(0)
    i = pl.program_id(1)

    if final:
        @pl.when((j == 0) & (i == 0))
        def _():
            best_ref[...] = jnp.full(best_ref.shape, lowest_score, jnp.float32)
            pow_ref[...] = jnp.zeros(pow_ref.shape, jnp.float32)

        @pl.when(i == 0)
        def _():
            acc_ref[...] = init_ref[:, 0]
    else:
        @pl.when(i == 0)
        def _():
            acc_ref[...] = jnp.zeros(acc_ref.shape, jnp.float32)

    for u, tm_ref in enumerate((tma_ref, tmb_ref)):
        def mix(c, carry, u=u, tm_ref=tm_ref):
            row = pl.multiple_of(c * chunk, chunk)
            out_row = pl.multiple_of(u * rows_t + c * chunk, chunk)
            image_re = sp_ref[0, pl.ds(out_row, chunk), :]
            image_im = sp_ref[1, pl.ds(out_row, chunk), :]
            tmpl_re = tm_ref[0, 0, 0, pl.ds(row, chunk), :].astype(jnp.float32)
            tmpl_im = tm_ref[0, 0, 1, pl.ds(row, chunk), :].astype(jnp.float32)
            m_ref[pl.ds(out_row, chunk), pl.ds(0, size)] = (image_re * tmpl_re + image_im * tmpl_im).astype(jnp.bfloat16)
            m_ref[pl.ds(out_row, chunk), pl.ds(size, size)] = (image_im * tmpl_re - image_re * tmpl_im).astype(jnp.bfloat16)
            return carry

        lax.fori_loop(0, rows_t // chunk, mix, 0, unroll=4)

    for p in range(peaks_n):
        @pl.when(f_ref[p * blocks + j] > 0)
        def _():
            g = jnp.dot(m_ref[...], ct_ref[p], preferred_element_type=jnp.float32).astype(jnp.bfloat16)
            part = jnp.dot(cr_ref[p], g[:, :width], preferred_element_type=jnp.float32)
            part = part - jnp.dot(sr_ref[p], g[:, width:], preferred_element_type=jnp.float32)
            acc_ref[p] = acc_ref[p] + part

    @pl.when(i == n_steps - 1)
    def _():
        if final:
            for p in range(peaks_n):
                @pl.when(f_ref[p * blocks + j] > 0)
                def _():
                    score = acc_ref[p] / size
                    best_ref[p] = jnp.maximum(best_ref[p], score)
                    pow_ref[p] = pow_ref[p] + score * score
        else:
            part_ref[:, 0] = acc_ref[...]


def match_rows(flags, tas, tbs, rids, tmpl_a, tmpl_b, spec, col_table, cos_t, sin_t, init=None):
    _, blocks, _, rows_t, size = tmpl_a.shape
    peaks_n, width = cos_t.shape[0], cos_t.shape[1]
    n_steps = tas.shape[0]
    final = init is not None
    chunk = math.gcd(rows_t, 16)
    span = 2 * rows_t
    kernel = functools.partial(rows_kernel, blocks, size, width, rows_t, peaks_n, chunk, n_steps, final)
    flops = blocks * peaks_n * n_steps * (2 * span * 2 * size * 2 * width + 2 * 2 * width * span * width)
    cost = pl.CostEstimate(flops=flops, transcendentals=0, bytes_accessed=n_steps * blocks * 2 * span * size * 6 + col_table.size * 2)
    in_specs = [
        pl.BlockSpec((1, 1, 2, rows_t, size), lambda j, i, f, ta, tb, r: (ta[i], j, 0, 0, 0)),
        pl.BlockSpec((1, 1, 2, rows_t, size), lambda j, i, f, ta, tb, r: (tb[i], j, 0, 0, 0)),
        pl.BlockSpec((2, span, size), lambda j, i, f, ta, tb, r: (0, r[i], 0)),
        pl.BlockSpec(col_table.shape, lambda j, i, f, ta, tb, r: (0, 0, 0)),
        pl.BlockSpec((peaks_n, width, span), lambda j, i, f, ta, tb, r: (0, 0, r[i])),
        pl.BlockSpec((peaks_n, width, span), lambda j, i, f, ta, tb, r: (0, 0, r[i])),
    ]
    args = [flags, tas, tbs, rids, tmpl_a, tmpl_b, spec, col_table, cos_t, sin_t]
    part_spec = pl.BlockSpec((peaks_n, 1, width, width), lambda j, i, f, ta, tb, r: (0, j, 0, 0))
    if final:
        in_specs.append(part_spec)
        args.append(init)
        out = jax.ShapeDtypeStruct((peaks_n, width, width), jnp.float32)
        out_shape = [out, out]
        out_specs = [pl.BlockSpec((peaks_n, width, width), lambda j, i, f, ta, tb, r: (0, 0, 0))] * 2
    else:
        out_shape = jax.ShapeDtypeStruct((peaks_n, blocks, width, width), jnp.float32)
        out_specs = part_spec
    return pl.pallas_call(
        kernel,
        grid_spec=pltpu.PrefetchScalarGridSpec(
            num_scalar_prefetch=4,
            grid=(blocks, n_steps),
            in_specs=in_specs,
            out_specs=out_specs,
            scratch_shapes=[pltpu.VMEM((peaks_n, width, width), jnp.float32), pltpu.VMEM((span, 2 * size), jnp.bfloat16)],
        ),
        out_shape=out_shape,
        compiler_params=pltpu.CompilerParams(dimension_semantics=("arbitrary", "arbitrary")),
        cost_estimate=cost,
    )(*args)


def local(tile_spectra, template_spectra, peaks, listed):
    size = tile_spectra.shape[3]
    width = W
    tiles = lax.axis_size("tile")
    rows_t = template_spectra.shape[2]
    tmpl = lax.all_gather(template_spectra, "tile", axis=0)
    block_size = tmpl.shape[1]
    spec = gather_rows(tile_spectra[0], "orient")
    spec = jnp.moveaxis(spec, 0, 1).reshape(2, size, size)
    freqs = jnp.arange(size, dtype=jnp.int32)
    cos_row, sin_row = angle_tables(freqs, peaks[0][:, 0], size, width)
    cos_t = jnp.swapaxes(cos_row, 1, 2)
    sin_t = jnp.swapaxes(sin_row, 1, 2)
    col_table = col_tables(peaks[0], size, width)
    listed_ids = listed[0]
    global_ids = lax.axis_index("orient") * block_size + jnp.arange(block_size, dtype=jnp.int32)
    is_listed = jnp.any(listed_ids[:, :, None] == global_ids[None, None, :], axis=1)
    flags = is_listed.astype(jnp.int32).reshape(-1)
    if rows_t % 128 != 0 or tiles % 2 != 0:
        best_part, power_part = match(flags, tmpl, spec, col_table, cos_t, sin_t)
    else:
        me = lax.axis_index("tile")
        sibling = lax.ppermute(template_spectra, "tile", xor_pairs(tiles, 1))
        near = jnp.stack([template_spectra, sibling])
        spec32 = spec.astype(jnp.float32)
        chip = me // 2
        odd = (me % 2)[None].astype(jnp.int32)
        partial = match_rows(flags, odd, 1 - odd, chip[None].astype(jnp.int32), near, near, spec32, col_table, cos_t, sin_t)
        far = far_chips(chip, tiles // 2)
        best_part, power_part = match_rows(flags, far * 2, far * 2 + 1, far, tmpl, tmpl, spec32, col_table, cos_t, sin_t, init=partial)
    best_all, power_all = reduce_orient(best_part, power_part, "orient")
    return (best_all[None], (power_all / LIST)[None])


def far_chips(chip, chips):
    steps = jnp.arange(chips - 1, dtype=jnp.int32)
    return steps + (steps >= chip).astype(jnp.int32)


def solution(mesh):
    placed = (
        P("tile", None, "orient", None),
        P("orient", None, "tile", None),
        P("tile", None, None),
        P("tile", None, None),
    )
    return jax.shard_map(
        local,
        mesh=mesh,
        in_specs=placed,
        out_specs=(P("tile", None, None, None), P("tile", None, None, None)),
        check_vma=False,
    )
```

```python
import functools
import math

import jax
import jax.numpy as jnp
from jax import lax
from jax.experimental import pallas as pl
from jax.experimental.pallas import tpu as pltpu
from jax.sharding import PartitionSpec as P

W = 128
LIST = 48


lowest_score = -1e30


def xor_pairs(n, k):
    return [(i, i ^ k) for i in range(n)]


def is_pow2(n):
    return n & (n - 1) == 0


def angle_tables(freqs, coords, size, width):
    offsets = jnp.arange(width, dtype=jnp.int32) - width // 2
    position = (coords[:, None] + offsets[None, :]) % size
    phase = freqs[None, :, None] * position[:, None, :] % size
    angle = phase.astype(jnp.float32) * (2.0 * math.pi / size)
    return (jnp.cos(angle).astype(jnp.bfloat16), jnp.sin(angle).astype(jnp.bfloat16))


def col_tables(peak_rows, size, width):
    freqs = jnp.arange(size, dtype=jnp.int32)
    cos_col, sin_col = angle_tables(freqs, peak_rows[:, 1], size, width)
    upper = jnp.concatenate([cos_col, sin_col], axis=-1)
    lower = jnp.concatenate([-sin_col, cos_col], axis=-1)
    return jnp.concatenate([upper, lower], axis=1)


def gather_rows(part, axis):
    n = lax.axis_size(axis)
    if not is_pow2(n):
        return lax.all_gather(part, axis)
    me = lax.axis_index(axis)
    blocks = part[None]
    k = n // 2
    while k >= 1:
        got = lax.ppermute(blocks, axis, xor_pairs(n, k))
        blocks = jnp.concatenate([blocks, got])
        k //= 2
    want = jnp.arange(n, dtype=jnp.int32) ^ me
    return blocks[order_of(want, n)]


def order_of(want, count):
    steps = int(math.log2(count))
    slot = jnp.zeros_like(want)
    for j in range(steps):
        k = count >> (j + 1)
        hit = (want & k) != 0
        slot = slot | jnp.where(hit, 1 << j, 0)
    return slot


def reduce_orient(best_part, power_part, axis):
    n = lax.axis_size(axis)
    if not is_pow2(n):
        best = lax.pmax(best_part, axis)
        power = lax.psum(power_part, axis)
        return best, power
    width = best_part.shape[-1]
    joined = jnp.stack([best_part.reshape(-1, width), power_part.reshape(-1, width)], axis=0)
    return reduce_joined(joined, best_part.shape, axis)


def reduce_joined(joined, shape, axis):
    n = lax.axis_size(axis)
    if not is_pow2(n):
        best = lax.pmax(joined[0], axis)
        power = lax.psum(joined[1], axis)
        return best.reshape(shape), power.reshape(shape)
    me = lax.axis_index(axis)
    cur = joined
    k = 1
    while k < n:
        half = cur.shape[1] // 2
        bit = (me // k) % 2
        keep = lax.dynamic_slice_in_dim(cur, bit * half, half, axis=1)
        send = lax.dynamic_slice_in_dim(cur, (1 - bit) * half, half, axis=1)
        got = lax.ppermute(send, axis, xor_pairs(n, k))
        cur = jnp.stack([jnp.maximum(keep[0], got[0]), keep[1] + got[1]])
        k *= 2
    k = n // 2
    while k >= 1:
        got = lax.ppermute(cur, axis, xor_pairs(n, k))
        bit = (me // k) % 2
        cur = jnp.where(bit == 1, jnp.concatenate([got, cur], axis=1), jnp.concatenate([cur, got], axis=1))
        k //= 2
    return cur[0].reshape(shape), cur[1].reshape(shape)


def match_kernel(blocks, size, width, rows_t, tiles, peaks_n, l_ref, tm_ref, sp_ref, ct_ref, cr_ref, sr_ref, best_ref, pow_ref, m_ref):
    j = pl.program_id(0)

    @pl.when(j == 0)
    def _():
        best_ref[...] = jnp.full(best_ref.shape, lowest_score, jnp.float32)
        pow_ref[...] = jnp.zeros(pow_ref.shape, jnp.float32)

    for t in range(tiles):
        rows = pl.ds(t * rows_t, rows_t)
        image_re = sp_ref[0, rows, :].astype(jnp.float32)
        image_im = sp_ref[1, rows, :].astype(jnp.float32)
        tmpl_re = tm_ref[t, 0, 0].astype(jnp.float32)
        tmpl_im = tm_ref[t, 0, 1].astype(jnp.float32)
        m_ref[rows, pl.ds(0, size)] = (image_re * tmpl_re + image_im * tmpl_im).astype(jnp.bfloat16)
        m_ref[rows, pl.ds(size, size)] = (image_im * tmpl_re - image_re * tmpl_im).astype(jnp.bfloat16)

    for p in range(peaks_n):
        @pl.when(l_ref[p * blocks + j] > 0)
        def _():
            g = jnp.dot(m_ref[...], ct_ref[p], preferred_element_type=jnp.float32).astype(jnp.bfloat16)
            score = jnp.dot(cr_ref[p], g[:, :width], preferred_element_type=jnp.float32)
            score = score - jnp.dot(sr_ref[p], g[:, width:], preferred_element_type=jnp.float32)
            score = score / size
            best_ref[p] = jnp.maximum(best_ref[p], score)
            pow_ref[p] = pow_ref[p] + score * score


def match(flags, tmpl, spec, col_table, cos_t, sin_t):
    tiles, blocks, _, rows_t, size = tmpl.shape
    peaks_n, width = cos_t.shape[0], cos_t.shape[1]
    kernel = functools.partial(match_kernel, blocks, size, width, rows_t, tiles, peaks_n)
    flops = blocks * peaks_n * (2 * size * 2 * size * 2 * width + 2 * 2 * width * size * width)
    cost = pl.CostEstimate(flops=flops, transcendentals=0, bytes_accessed=tmpl.size * 2 + spec.size * 2 + col_table.size * 2)
    out = jax.ShapeDtypeStruct((peaks_n, width, width), jnp.float32)
    return pl.pallas_call(
        kernel,
        grid_spec=pltpu.PrefetchScalarGridSpec(
            num_scalar_prefetch=1,
            grid=(blocks,),
            in_specs=[
                pl.BlockSpec((tiles, 1, 2, rows_t, size), lambda j, l: (0, j, 0, 0, 0)),
                pl.BlockSpec((2, size, size), lambda j, l: (0, 0, 0)),
                pl.BlockSpec(col_table.shape, lambda j, l: (0, 0, 0)),
                pl.BlockSpec(cos_t.shape, lambda j, l: (0, 0, 0)),
                pl.BlockSpec(sin_t.shape, lambda j, l: (0, 0, 0)),
            ],
            out_specs=[
                pl.BlockSpec((peaks_n, width, width), lambda j, l: (0, 0, 0)),
                pl.BlockSpec((peaks_n, width, width), lambda j, l: (0, 0, 0)),
            ],
            scratch_shapes=[pltpu.VMEM((size, 2 * size), jnp.bfloat16)],
        ),
        out_shape=[out, out],
        compiler_params=pltpu.CompilerParams(dimension_semantics=("arbitrary",)),
        cost_estimate=cost,
    )(flags, tmpl, spec, col_table, cos_t, sin_t)


def rows_kernel(blocks, size, width, rows_t, peaks_n, chunk, n_steps, final, f_ref, ta_ref, tb_ref, rid_ref, off_ref, tma_ref, tmb_ref, sp_ref, ct_ref, cr_ref, sr_ref, *rest):
    if final:
        init_ref, out_ref, acc_ref, m_ref = rest
        best_ref, pow_ref = out_ref.at[0], out_ref.at[1]
    else:
        part_ref, acc_ref, m_ref = rest
    j = pl.program_id(0)
    i = pl.program_id(1)

    if final:
        @pl.when((j == 0) & (i == 0))
        def _():
            best_ref[...] = jnp.full(best_ref.shape, lowest_score, jnp.float32)
            pow_ref[...] = jnp.zeros(pow_ref.shape, jnp.float32)

        @pl.when(i == 0)
        def _():
            acc_ref[...] = init_ref[:, 0]
    else:
        @pl.when(i == 0)
        def _():
            acc_ref[...] = jnp.zeros(acc_ref.shape, jnp.float32)

    for u, tm_ref in enumerate((tma_ref, tmb_ref)):
        def mix(c, carry, u=u, tm_ref=tm_ref):
            row = pl.multiple_of(c * chunk, chunk)
            out_row = pl.multiple_of(off_ref[u] + c * chunk, chunk)
            image_re = sp_ref[0, pl.ds(out_row, chunk), :]
            image_im = sp_ref[1, pl.ds(out_row, chunk), :]
            tmpl_re = tm_ref[0, 0, 0, pl.ds(row, chunk), :].astype(jnp.float32)
            tmpl_im = tm_ref[0, 0, 1, pl.ds(row, chunk), :].astype(jnp.float32)
            m_ref[pl.ds(out_row, chunk), pl.ds(0, size)] = (image_re * tmpl_re + image_im * tmpl_im).astype(jnp.bfloat16)
            m_ref[pl.ds(out_row, chunk), pl.ds(size, size)] = (image_im * tmpl_re - image_re * tmpl_im).astype(jnp.bfloat16)
            return carry

        lax.fori_loop(0, rows_t // chunk, mix, 0, unroll=4)

    for p in range(peaks_n):
        @pl.when(f_ref[p * blocks + j] > 0)
        def _():
            g = jnp.dot(m_ref[...], ct_ref[p], preferred_element_type=jnp.float32).astype(jnp.bfloat16)
            part = jnp.dot(cr_ref[p], g[:, :width], preferred_element_type=jnp.float32)
            part = part - jnp.dot(sr_ref[p], g[:, width:], preferred_element_type=jnp.float32)
            acc_ref[p] = acc_ref[p] + part

    @pl.when(i == n_steps - 1)
    def _():
        if final:
            for p in range(peaks_n):
                @pl.when(f_ref[p * blocks + j] > 0)
                def _():
                    score = acc_ref[p] / size
                    best_ref[p] = jnp.maximum(best_ref[p], score)
                    pow_ref[p] = pow_ref[p] + score * score
        else:
            part_ref[:, 0] = acc_ref[...]


def match_rows(flags, tas, tbs, rids, offs, tmpl_a, tmpl_b, spec, col_table, cos_t, sin_t, init=None):
    _, blocks, _, rows_t, size = tmpl_a.shape
    peaks_n, width = cos_t.shape[0], cos_t.shape[1]
    n_steps = tas.shape[0]
    final = init is not None
    chunk = math.gcd(rows_t, 16)
    span = 2 * rows_t
    kernel = functools.partial(rows_kernel, blocks, size, width, rows_t, peaks_n, chunk, n_steps, final)
    flops = blocks * peaks_n * n_steps * (2 * span * 2 * size * 2 * width + 2 * 2 * width * span * width)
    cost = pl.CostEstimate(flops=flops, transcendentals=0, bytes_accessed=n_steps * blocks * 2 * span * size * 6 + col_table.size * 2)
    in_specs = [
        pl.BlockSpec((1, 1, 2, rows_t, size), lambda j, i, f, ta, tb, r, o: (ta[i], j, 0, 0, 0)),
        pl.BlockSpec((1, 1, 2, rows_t, size), lambda j, i, f, ta, tb, r, o: (tb[i], j, 0, 0, 0)),
        pl.BlockSpec((2, span, size), lambda j, i, f, ta, tb, r, o: (0, r[i], 0)),
        pl.BlockSpec(col_table.shape, lambda j, i, f, ta, tb, r, o: (0, 0, 0)),
        pl.BlockSpec((peaks_n, width, span), lambda j, i, f, ta, tb, r, o: (0, 0, r[i])),
        pl.BlockSpec((peaks_n, width, span), lambda j, i, f, ta, tb, r, o: (0, 0, r[i])),
    ]
    args = [flags, tas, tbs, rids, offs, tmpl_a, tmpl_b, spec, col_table, cos_t, sin_t]
    part_spec = pl.BlockSpec((peaks_n, 1, width, width), lambda j, i, f, ta, tb, r, o: (0, j, 0, 0))
    if final:
        in_specs.append(part_spec)
        args.append(init)
        out_shape = jax.ShapeDtypeStruct((2, peaks_n, width, width), jnp.float32)
        out_specs = pl.BlockSpec((2, peaks_n, width, width), lambda j, i, f, ta, tb, r, o: (0, 0, 0, 0))
    else:
        out_shape = jax.ShapeDtypeStruct((peaks_n, blocks, width, width), jnp.float32)
        out_specs = part_spec
    return pl.pallas_call(
        kernel,
        grid_spec=pltpu.PrefetchScalarGridSpec(
            num_scalar_prefetch=5,
            grid=(blocks, n_steps),
            in_specs=in_specs,
            out_specs=out_specs,
            scratch_shapes=[pltpu.VMEM((peaks_n, width, width), jnp.float32), pltpu.VMEM((span, 2 * size), jnp.bfloat16)],
        ),
        out_shape=out_shape,
        compiler_params=pltpu.CompilerParams(dimension_semantics=("arbitrary", "arbitrary")),
        cost_estimate=cost,
    )(*args)


def local(tile_spectra, template_spectra, peaks, listed):
    size = tile_spectra.shape[3]
    width = W
    tiles = lax.axis_size("tile")
    rows_t = template_spectra.shape[2]
    tmpl = lax.all_gather(template_spectra, "tile", axis=0)
    block_size = tmpl.shape[1]
    spec = gather_rows(tile_spectra[0], "orient")
    spec = jnp.moveaxis(spec, 0, 1).reshape(2, size, size)
    freqs = jnp.arange(size, dtype=jnp.int32)
    cos_row, sin_row = angle_tables(freqs, peaks[0][:, 0], size, width)
    cos_t = jnp.swapaxes(cos_row, 1, 2)
    sin_t = jnp.swapaxes(sin_row, 1, 2)
    col_table = col_tables(peaks[0], size, width)
    listed_ids = listed[0]
    global_ids = lax.axis_index("orient") * block_size + jnp.arange(block_size, dtype=jnp.int32)
    is_listed = jnp.any(listed_ids[:, :, None] == global_ids[None, None, :], axis=1)
    flags = is_listed.astype(jnp.int32).reshape(-1)
    best_shape = (listed.shape[1], width, width)
    if rows_t % 128 != 0 or tiles % 2 != 0:
        best_part, power_part = match(flags, tmpl, spec, col_table, cos_t, sin_t)
    else:
        me = lax.axis_index("tile")
        sibling = lax.ppermute(template_spectra, "tile", xor_pairs(tiles, 1))
        spec32 = spec.astype(jnp.float32)
        chip = me // 2
        odd = (me % 2).astype(jnp.int32)
        zero = jnp.zeros((1,), jnp.int32)
        near_offs = jnp.stack([odd, 1 - odd]) * rows_t
        own, sib = template_spectra[None], sibling[None]
        partial = match_rows(flags, zero, zero, chip[None].astype(jnp.int32), near_offs, own, sib, spec32, col_table, cos_t, sin_t)
        far = far_chips(chip, tiles // 2)
        far_offs = jnp.array([0, rows_t], jnp.int32)
        joined = match_rows(flags, far * 2, far * 2 + 1, far, far_offs, tmpl, tmpl, spec32, col_table, cos_t, sin_t, init=partial)
        best_all, power_all = reduce_joined(joined.reshape(2, -1, width), best_shape, "orient")
        return (best_all[None], (power_all / LIST)[None])
    best_all, power_all = reduce_orient(best_part, power_part, "orient")
    return (best_all[None], (power_all / LIST)[None])


def far_chips(chip, chips):
    steps = jnp.arange(chips - 1, dtype=jnp.int32)
    return steps + (steps >= chip).astype(jnp.int32)


def solution(mesh):
    placed = (
        P("tile", None, "orient", None),
        P("orient", None, "tile", None),
        P("tile", None, None),
        P("tile", None, None),
    )
    return jax.shard_map(
        local,
        mesh=mesh,
        in_specs=placed,
        out_specs=(P("tile", None, None, None), P("tile", None, None, None)),
        check_vma=False,
    )
```

```python
import functools
import math

import jax
import jax.numpy as jnp
from jax import lax
from jax.experimental import pallas as pl
from jax.experimental.pallas import tpu as pltpu
from jax.sharding import PartitionSpec as P

W = 128
LIST = 48


lowest_score = -1e30


def xor_pairs(n, k):
    return [(i, i ^ k) for i in range(n)]


def is_pow2(n):
    return n & (n - 1) == 0


def angle_tables(freqs, coords, size, width):
    offsets = jnp.arange(width, dtype=jnp.int32) - width // 2
    position = (coords[:, None] + offsets[None, :]) % size
    phase = freqs[None, :, None] * position[:, None, :] % size
    angle = phase.astype(jnp.float32) * (2.0 * math.pi / size)
    return (jnp.cos(angle).astype(jnp.bfloat16), jnp.sin(angle).astype(jnp.bfloat16))


def col_tables(peak_rows, size, width):
    freqs = jnp.arange(size, dtype=jnp.int32)
    cos_col, sin_col = angle_tables(freqs, peak_rows[:, 1], size, width)
    upper = jnp.concatenate([cos_col, sin_col], axis=-1)
    lower = jnp.concatenate([-sin_col, cos_col], axis=-1)
    return jnp.concatenate([upper, lower], axis=1)


def gather_rows(part, axis):
    n = lax.axis_size(axis)
    if not is_pow2(n):
        return lax.all_gather(part, axis)
    me = lax.axis_index(axis)
    blocks = part[None]
    k = n // 2
    while k >= 1:
        got = lax.ppermute(blocks, axis, xor_pairs(n, k))
        blocks = jnp.concatenate([blocks, got])
        k //= 2
    want = jnp.arange(n, dtype=jnp.int32) ^ me
    return blocks[order_of(want, n)]


def order_of(want, count):
    steps = int(math.log2(count))
    slot = jnp.zeros_like(want)
    for j in range(steps):
        k = count >> (j + 1)
        hit = (want & k) != 0
        slot = slot | jnp.where(hit, 1 << j, 0)
    return slot


def reduce_orient(best_part, power_part, axis):
    n = lax.axis_size(axis)
    if not is_pow2(n):
        best = lax.pmax(best_part, axis)
        power = lax.psum(power_part, axis)
        return best, power
    width = best_part.shape[-1]
    joined = jnp.stack([best_part.reshape(-1, width), power_part.reshape(-1, width)], axis=0)
    return reduce_joined(joined, best_part.shape, axis)


def reduce_joined(joined, shape, axis):
    n = lax.axis_size(axis)
    if not is_pow2(n):
        best = lax.pmax(joined[0], axis)
        power = lax.psum(joined[1], axis)
        return best.reshape(shape), power.reshape(shape)
    me = lax.axis_index(axis)
    cur = joined
    k = 1
    while k < n:
        half = cur.shape[1] // 2
        bit = (me // k) % 2
        keep = lax.dynamic_slice_in_dim(cur, bit * half, half, axis=1)
        send = lax.dynamic_slice_in_dim(cur, (1 - bit) * half, half, axis=1)
        got = lax.ppermute(send, axis, xor_pairs(n, k))
        cur = jnp.stack([jnp.maximum(keep[0], got[0]), keep[1] + got[1]])
        k *= 2
    k = n // 2
    while k >= 1:
        got = lax.ppermute(cur, axis, xor_pairs(n, k))
        bit = (me // k) % 2
        cur = jnp.where(bit == 1, jnp.concatenate([got, cur], axis=1), jnp.concatenate([cur, got], axis=1))
        k //= 2
    return cur[0].reshape(shape), cur[1].reshape(shape)


def match_kernel(blocks, size, width, rows_t, tiles, peaks_n, l_ref, tm_ref, sp_ref, ct_ref, cr_ref, sr_ref, best_ref, pow_ref, m_ref):
    j = pl.program_id(0)

    @pl.when(j == 0)
    def _():
        best_ref[...] = jnp.full(best_ref.shape, lowest_score, jnp.float32)
        pow_ref[...] = jnp.zeros(pow_ref.shape, jnp.float32)

    for t in range(tiles):
        rows = pl.ds(t * rows_t, rows_t)
        image_re = sp_ref[0, rows, :].astype(jnp.float32)
        image_im = sp_ref[1, rows, :].astype(jnp.float32)
        tmpl_re = tm_ref[t, 0, 0].astype(jnp.float32)
        tmpl_im = tm_ref[t, 0, 1].astype(jnp.float32)
        m_ref[rows, pl.ds(0, size)] = (image_re * tmpl_re + image_im * tmpl_im).astype(jnp.bfloat16)
        m_ref[rows, pl.ds(size, size)] = (image_im * tmpl_re - image_re * tmpl_im).astype(jnp.bfloat16)

    for p in range(peaks_n):
        @pl.when(l_ref[p * blocks + j] > 0)
        def _():
            g = jnp.dot(m_ref[...], ct_ref[p], preferred_element_type=jnp.float32).astype(jnp.bfloat16)
            score = jnp.dot(cr_ref[p], g[:, :width], preferred_element_type=jnp.float32)
            score = score - jnp.dot(sr_ref[p], g[:, width:], preferred_element_type=jnp.float32)
            score = score / size
            best_ref[p] = jnp.maximum(best_ref[p], score)
            pow_ref[p] = pow_ref[p] + score * score


def match(flags, tmpl, spec, col_table, cos_t, sin_t):
    tiles, blocks, _, rows_t, size = tmpl.shape
    peaks_n, width = cos_t.shape[0], cos_t.shape[1]
    kernel = functools.partial(match_kernel, blocks, size, width, rows_t, tiles, peaks_n)
    flops = blocks * peaks_n * (2 * size * 2 * size * 2 * width + 2 * 2 * width * size * width)
    cost = pl.CostEstimate(flops=flops, transcendentals=0, bytes_accessed=tmpl.size * 2 + spec.size * 2 + col_table.size * 2)
    out = jax.ShapeDtypeStruct((peaks_n, width, width), jnp.float32)
    return pl.pallas_call(
        kernel,
        grid_spec=pltpu.PrefetchScalarGridSpec(
            num_scalar_prefetch=1,
            grid=(blocks,),
            in_specs=[
                pl.BlockSpec((tiles, 1, 2, rows_t, size), lambda j, l: (0, j, 0, 0, 0)),
                pl.BlockSpec((2, size, size), lambda j, l: (0, 0, 0)),
                pl.BlockSpec(col_table.shape, lambda j, l: (0, 0, 0)),
                pl.BlockSpec(cos_t.shape, lambda j, l: (0, 0, 0)),
                pl.BlockSpec(sin_t.shape, lambda j, l: (0, 0, 0)),
            ],
            out_specs=[
                pl.BlockSpec((peaks_n, width, width), lambda j, l: (0, 0, 0)),
                pl.BlockSpec((peaks_n, width, width), lambda j, l: (0, 0, 0)),
            ],
            scratch_shapes=[pltpu.VMEM((size, 2 * size), jnp.bfloat16)],
        ),
        out_shape=[out, out],
        compiler_params=pltpu.CompilerParams(dimension_semantics=("arbitrary",)),
        cost_estimate=cost,
    )(flags, tmpl, spec, col_table, cos_t, sin_t)


def rows_kernel(blocks, size, width, rows_t, peaks_n, peak_lo, chunk, n_steps, final, f_ref, ta_ref, tb_ref, rid_ref, off_ref, tma_ref, tmb_ref, sp_ref, ct_ref, cr_ref, sr_ref, *rest):
    if final:
        init_ref, out_ref, acc_ref, m_ref = rest
        best_ref, pow_ref = out_ref.at[0], out_ref.at[1]
    else:
        part_ref, acc_ref, m_ref = rest
    j = pl.program_id(0)
    i = pl.program_id(1)

    if final:
        @pl.when((j == 0) & (i == 0))
        def _():
            best_ref[...] = jnp.full(best_ref.shape, lowest_score, jnp.float32)
            pow_ref[...] = jnp.zeros(pow_ref.shape, jnp.float32)

        @pl.when(i == 0)
        def _():
            acc_ref[...] = init_ref[:, 0]
    else:
        @pl.when(i == 0)
        def _():
            acc_ref[...] = jnp.zeros(acc_ref.shape, jnp.float32)

    for u, tm_ref in enumerate((tma_ref, tmb_ref)):
        def mix(c, carry, u=u, tm_ref=tm_ref):
            row = pl.multiple_of(c * chunk, chunk)
            out_row = pl.multiple_of(off_ref[u] + c * chunk, chunk)
            image_re = sp_ref[0, pl.ds(out_row, chunk), :]
            image_im = sp_ref[1, pl.ds(out_row, chunk), :]
            tmpl_re = tm_ref[0, 0, 0, pl.ds(row, chunk), :].astype(jnp.float32)
            tmpl_im = tm_ref[0, 0, 1, pl.ds(row, chunk), :].astype(jnp.float32)
            m_ref[pl.ds(out_row, chunk), pl.ds(0, size)] = (image_re * tmpl_re + image_im * tmpl_im).astype(jnp.bfloat16)
            m_ref[pl.ds(out_row, chunk), pl.ds(size, size)] = (image_im * tmpl_re - image_re * tmpl_im).astype(jnp.bfloat16)
            return carry

        lax.fori_loop(0, rows_t // chunk, mix, 0, unroll=4)

    for p in range(peaks_n):
        @pl.when(f_ref[(peak_lo + p) * blocks + j] > 0)
        def _():
            g = jnp.dot(m_ref[...], ct_ref[p], preferred_element_type=jnp.float32).astype(jnp.bfloat16)
            part = jnp.dot(cr_ref[p], g[:, :width], preferred_element_type=jnp.float32)
            part = part - jnp.dot(sr_ref[p], g[:, width:], preferred_element_type=jnp.float32)
            acc_ref[p] = acc_ref[p] + part

    @pl.when(i == n_steps - 1)
    def _():
        if final:
            for p in range(peaks_n):
                @pl.when(f_ref[(peak_lo + p) * blocks + j] > 0)
                def _():
                    score = acc_ref[p] / size
                    best_ref[p] = jnp.maximum(best_ref[p], score)
                    pow_ref[p] = pow_ref[p] + score * score
        else:
            part_ref[:, 0] = acc_ref[...]


def match_rows(flags, tas, tbs, rids, offs, tmpl_a, tmpl_b, spec, col_table, cos_t, sin_t, init=None, peak_lo=0, peaks_n=None):
    _, blocks, _, rows_t, size = tmpl_a.shape
    width = cos_t.shape[1]
    peaks_n = cos_t.shape[0] if peaks_n is None else peaks_n
    h = peak_lo // peaks_n
    n_steps = tas.shape[0]
    final = init is not None
    chunk = math.gcd(rows_t, 16)
    span = 2 * rows_t
    kernel = functools.partial(rows_kernel, blocks, size, width, rows_t, peaks_n, peak_lo, chunk, n_steps, final)
    flops = blocks * peaks_n * n_steps * (2 * span * 2 * size * 2 * width + 2 * 2 * width * span * width)
    cost = pl.CostEstimate(flops=flops, transcendentals=0, bytes_accessed=n_steps * blocks * 2 * span * size * 6 + col_table.size * 2 * peaks_n // col_table.shape[0])
    in_specs = [
        pl.BlockSpec((1, 1, 2, rows_t, size), lambda j, i, f, ta, tb, r, o: (ta[i], j, 0, 0, 0)),
        pl.BlockSpec((1, 1, 2, rows_t, size), lambda j, i, f, ta, tb, r, o: (tb[i], j, 0, 0, 0)),
        pl.BlockSpec((2, span, size), lambda j, i, f, ta, tb, r, o: (0, r[i], 0)),
        pl.BlockSpec((peaks_n,) + col_table.shape[1:], lambda j, i, f, ta, tb, r, o: (h, 0, 0)),
        pl.BlockSpec((peaks_n, width, span), lambda j, i, f, ta, tb, r, o: (h, 0, r[i])),
        pl.BlockSpec((peaks_n, width, span), lambda j, i, f, ta, tb, r, o: (h, 0, r[i])),
    ]
    args = [flags, tas, tbs, rids, offs, tmpl_a, tmpl_b, spec, col_table, cos_t, sin_t]
    part_spec = pl.BlockSpec((peaks_n, 1, width, width), lambda j, i, f, ta, tb, r, o: (h, j, 0, 0))
    if final:
        in_specs.append(part_spec)
        args.append(init)
        out_shape = jax.ShapeDtypeStruct((2, peaks_n, width, width), jnp.float32)
        out_specs = pl.BlockSpec((2, peaks_n, width, width), lambda j, i, f, ta, tb, r, o: (0, 0, 0, 0))
    else:
        out_shape = jax.ShapeDtypeStruct((peaks_n, blocks, width, width), jnp.float32)
        out_specs = part_spec
    return pl.pallas_call(
        kernel,
        grid_spec=pltpu.PrefetchScalarGridSpec(
            num_scalar_prefetch=5,
            grid=(blocks, n_steps),
            in_specs=in_specs,
            out_specs=out_specs,
            scratch_shapes=[pltpu.VMEM((peaks_n, width, width), jnp.float32), pltpu.VMEM((span, 2 * size), jnp.bfloat16)],
        ),
        out_shape=out_shape,
        compiler_params=pltpu.CompilerParams(dimension_semantics=("arbitrary", "arbitrary")),
        cost_estimate=cost,
    )(*args)


def local(tile_spectra, template_spectra, peaks, listed):
    size = tile_spectra.shape[3]
    width = W
    tiles = lax.axis_size("tile")
    rows_t = template_spectra.shape[2]
    tmpl = lax.all_gather(template_spectra, "tile", axis=0)
    block_size = tmpl.shape[1]
    spec = gather_rows(tile_spectra[0], "orient")
    spec = jnp.moveaxis(spec, 0, 1).reshape(2, size, size)
    freqs = jnp.arange(size, dtype=jnp.int32)
    cos_row, sin_row = angle_tables(freqs, peaks[0][:, 0], size, width)
    cos_t = jnp.swapaxes(cos_row, 1, 2)
    sin_t = jnp.swapaxes(sin_row, 1, 2)
    col_table = col_tables(peaks[0], size, width)
    listed_ids = listed[0]
    global_ids = lax.axis_index("orient") * block_size + jnp.arange(block_size, dtype=jnp.int32)
    is_listed = jnp.any(listed_ids[:, :, None] == global_ids[None, None, :], axis=1)
    flags = is_listed.astype(jnp.int32).reshape(-1)
    best_shape = (listed.shape[1], width, width)
    if rows_t % 128 != 0 or tiles % 2 != 0:
        best_part, power_part = match(flags, tmpl, spec, col_table, cos_t, sin_t)
    else:
        me = lax.axis_index("tile")
        sibling = lax.ppermute(template_spectra, "tile", xor_pairs(tiles, 1))
        spec32 = spec.astype(jnp.float32)
        chip = me // 2
        odd = (me % 2).astype(jnp.int32)
        zero = jnp.zeros((1,), jnp.int32)
        near_offs = jnp.stack([odd, 1 - odd]) * rows_t
        own, sib = template_spectra[None], sibling[None]
        partial = match_rows(flags, zero, zero, chip[None].astype(jnp.int32), near_offs, own, sib, spec32, col_table, cos_t, sin_t)
        far = far_chips(chip, tiles // 2)
        far_offs = jnp.array([0, rows_t], jnp.int32)
        peaks_n = best_shape[0]
        half = peaks_n // 2 if peaks_n % 2 == 0 else peaks_n
        bests, powers = [], []
        for lo in range(0, peaks_n, half):
            joined = match_rows(flags, far * 2, far * 2 + 1, far, far_offs, tmpl, tmpl, spec32, col_table, cos_t, sin_t,
                                init=partial, peak_lo=lo, peaks_n=half)
            best_h, power_h = reduce_joined(joined.reshape(2, -1, width), (half,) + best_shape[1:], "orient")
            bests.append(best_h)
            powers.append(power_h)
        best_all = jnp.concatenate(bests)
        power_all = jnp.concatenate(powers)
        return (best_all[None], (power_all / LIST)[None])
    best_all, power_all = reduce_orient(best_part, power_part, "orient")
    return (best_all[None], (power_all / LIST)[None])


def far_chips(chip, chips):
    steps = jnp.arange(chips - 1, dtype=jnp.int32)
    return steps + (steps >= chip).astype(jnp.int32)


def solution(mesh):
    placed = (
        P("tile", None, "orient", None),
        P("orient", None, "tile", None),
        P("tile", None, None),
        P("tile", None, None),
    )
    return jax.shard_map(
        local,
        mesh=mesh,
        in_specs=placed,
        out_specs=(P("tile", None, None, None), P("tile", None, None, None)),
        check_vma=False,
    )
```

```python
import functools
import math

import jax
import jax.numpy as jnp
from jax import lax
from jax.experimental import pallas as pl
from jax.experimental.pallas import tpu as pltpu
from jax.sharding import PartitionSpec as P

W = 128
LIST = 48


lowest_score = -1e30


def xor_pairs(n, k):
    return [(i, i ^ k) for i in range(n)]


def is_pow2(n):
    return n & (n - 1) == 0


def angle_tables(freqs, coords, size, width):
    offsets = jnp.arange(width, dtype=jnp.int32) - width // 2
    position = (coords[:, None] + offsets[None, :]) % size
    phase = freqs[None, :, None] * position[:, None, :] % size
    angle = phase.astype(jnp.float32) * (2.0 * math.pi / size)
    return (jnp.cos(angle).astype(jnp.bfloat16), jnp.sin(angle).astype(jnp.bfloat16))


def col_tables(peak_rows, size, width):
    freqs = jnp.arange(size, dtype=jnp.int32)
    cos_col, sin_col = angle_tables(freqs, peak_rows[:, 1], size, width)
    upper = jnp.concatenate([cos_col, sin_col], axis=-1)
    lower = jnp.concatenate([-sin_col, cos_col], axis=-1)
    return jnp.concatenate([upper, lower], axis=1)


def gather_rows(part, axis):
    n = lax.axis_size(axis)
    if not is_pow2(n):
        return lax.all_gather(part, axis)
    me = lax.axis_index(axis)
    blocks = part[None]
    k = n // 2
    while k >= 1:
        got = lax.ppermute(blocks, axis, xor_pairs(n, k))
        blocks = jnp.concatenate([blocks, got])
        k //= 2
    want = jnp.arange(n, dtype=jnp.int32) ^ me
    return blocks[order_of(want, n)]


def order_of(want, count):
    steps = int(math.log2(count))
    slot = jnp.zeros_like(want)
    for j in range(steps):
        k = count >> (j + 1)
        hit = (want & k) != 0
        slot = slot | jnp.where(hit, 1 << j, 0)
    return slot


def reduce_orient(best_part, power_part, axis):
    n = lax.axis_size(axis)
    if not is_pow2(n):
        best = lax.pmax(best_part, axis)
        power = lax.psum(power_part, axis)
        return best, power
    width = best_part.shape[-1]
    joined = jnp.stack([best_part.reshape(-1, width), power_part.reshape(-1, width)], axis=0)
    return reduce_joined(joined, best_part.shape, axis)


def reduce_joined(joined, shape, axis):
    n = lax.axis_size(axis)
    if not is_pow2(n):
        best = lax.pmax(joined[0], axis)
        power = lax.psum(joined[1], axis)
        return best.reshape(shape), power.reshape(shape)
    me = lax.axis_index(axis)
    cur = joined
    k = 1
    while k < n:
        half = cur.shape[1] // 2
        bit = (me // k) % 2
        keep = lax.dynamic_slice_in_dim(cur, bit * half, half, axis=1)
        send = lax.dynamic_slice_in_dim(cur, (1 - bit) * half, half, axis=1)
        got = lax.ppermute(send, axis, xor_pairs(n, k))
        cur = jnp.stack([jnp.maximum(keep[0], got[0]), keep[1] + got[1]])
        k *= 2
    k = n // 2
    while k >= 1:
        got = lax.ppermute(cur, axis, xor_pairs(n, k))
        bit = (me // k) % 2
        cur = jnp.where(bit == 1, jnp.concatenate([got, cur], axis=1), jnp.concatenate([cur, got], axis=1))
        k //= 2
    return cur[0].reshape(shape), cur[1].reshape(shape)


def match_kernel(blocks, size, width, rows_t, tiles, peaks_n, l_ref, tm_ref, sp_ref, ct_ref, cr_ref, sr_ref, best_ref, pow_ref, m_ref):
    j = pl.program_id(0)

    @pl.when(j == 0)
    def _():
        best_ref[...] = jnp.full(best_ref.shape, lowest_score, jnp.float32)
        pow_ref[...] = jnp.zeros(pow_ref.shape, jnp.float32)

    for t in range(tiles):
        rows = pl.ds(t * rows_t, rows_t)
        image_re = sp_ref[0, rows, :].astype(jnp.float32)
        image_im = sp_ref[1, rows, :].astype(jnp.float32)
        tmpl_re = tm_ref[t, 0, 0].astype(jnp.float32)
        tmpl_im = tm_ref[t, 0, 1].astype(jnp.float32)
        m_ref[rows, pl.ds(0, size)] = (image_re * tmpl_re + image_im * tmpl_im).astype(jnp.bfloat16)
        m_ref[rows, pl.ds(size, size)] = (image_im * tmpl_re - image_re * tmpl_im).astype(jnp.bfloat16)

    for p in range(peaks_n):
        @pl.when(l_ref[p * blocks + j] > 0)
        def _():
            g = jnp.dot(m_ref[...], ct_ref[p], preferred_element_type=jnp.float32).astype(jnp.bfloat16)
            score = jnp.dot(cr_ref[p], g[:, :width], preferred_element_type=jnp.float32)
            score = score - jnp.dot(sr_ref[p], g[:, width:], preferred_element_type=jnp.float32)
            score = score / size
            best_ref[p] = jnp.maximum(best_ref[p], score)
            pow_ref[p] = pow_ref[p] + score * score


def match(flags, tmpl, spec, col_table, cos_t, sin_t):
    tiles, blocks, _, rows_t, size = tmpl.shape
    peaks_n, width = cos_t.shape[0], cos_t.shape[1]
    kernel = functools.partial(match_kernel, blocks, size, width, rows_t, tiles, peaks_n)
    flops = blocks * peaks_n * (2 * size * 2 * size * 2 * width + 2 * 2 * width * size * width)
    cost = pl.CostEstimate(flops=flops, transcendentals=0, bytes_accessed=tmpl.size * 2 + spec.size * 2 + col_table.size * 2)
    out = jax.ShapeDtypeStruct((peaks_n, width, width), jnp.float32)
    return pl.pallas_call(
        kernel,
        grid_spec=pltpu.PrefetchScalarGridSpec(
            num_scalar_prefetch=1,
            grid=(blocks,),
            in_specs=[
                pl.BlockSpec((tiles, 1, 2, rows_t, size), lambda j, l: (0, j, 0, 0, 0)),
                pl.BlockSpec((2, size, size), lambda j, l: (0, 0, 0)),
                pl.BlockSpec(col_table.shape, lambda j, l: (0, 0, 0)),
                pl.BlockSpec(cos_t.shape, lambda j, l: (0, 0, 0)),
                pl.BlockSpec(sin_t.shape, lambda j, l: (0, 0, 0)),
            ],
            out_specs=[
                pl.BlockSpec((peaks_n, width, width), lambda j, l: (0, 0, 0)),
                pl.BlockSpec((peaks_n, width, width), lambda j, l: (0, 0, 0)),
            ],
            scratch_shapes=[pltpu.VMEM((size, 2 * size), jnp.bfloat16)],
        ),
        out_shape=[out, out],
        compiler_params=pltpu.CompilerParams(dimension_semantics=("arbitrary",)),
        cost_estimate=cost,
    )(flags, tmpl, spec, col_table, cos_t, sin_t)


def rows_kernel(blocks, size, width, rows_t, peaks_n, chunk, n_steps, final, f_ref, ta_ref, tb_ref, rid_ref, off_ref, tma_ref, tmb_ref, sp_ref, ct_ref, cr_ref, sr_ref, *rest):
    if final:
        init_ref, out_ref, acc_ref, m_ref = rest
        best_ref, pow_ref = out_ref.at[0], out_ref.at[1]
    else:
        part_ref, acc_ref, m_ref = rest
    jj = pl.program_id(0)
    i = pl.program_id(1)
    span = 2 * rows_t

    if final:
        @pl.when((jj == 0) & (i == 0))
        def _():
            best_ref[...] = jnp.full(best_ref.shape, lowest_score, jnp.float32)
            pow_ref[...] = jnp.zeros(pow_ref.shape, jnp.float32)

        @pl.when(i == 0)
        def _():
            acc_ref[...] = init_ref[...]
    else:
        @pl.when(i == 0)
        def _():
            acc_ref[...] = jnp.zeros(acc_ref.shape, jnp.float32)

    for o in range(2):
        for u, tm_ref in enumerate((tma_ref, tmb_ref)):
            def mix(c, carry, u=u, o=o, tm_ref=tm_ref):
                row = pl.multiple_of(c * chunk, chunk)
                in_row = pl.multiple_of(off_ref[u] + c * chunk, chunk)
                out_row = pl.multiple_of(o * span + off_ref[u] + c * chunk, chunk)
                image_re = sp_ref[0, pl.ds(in_row, chunk), :]
                image_im = sp_ref[1, pl.ds(in_row, chunk), :]
                tmpl_re = tm_ref[0, o, 0, pl.ds(row, chunk), :].astype(jnp.float32)
                tmpl_im = tm_ref[0, o, 1, pl.ds(row, chunk), :].astype(jnp.float32)
                m_ref[pl.ds(out_row, chunk), pl.ds(0, size)] = (image_re * tmpl_re + image_im * tmpl_im).astype(jnp.bfloat16)
                m_ref[pl.ds(out_row, chunk), pl.ds(size, size)] = (image_im * tmpl_re - image_re * tmpl_im).astype(jnp.bfloat16)
                return carry

            lax.fori_loop(0, rows_t // chunk, mix, 0, unroll=4)

    for p in range(peaks_n):
        first = f_ref[p * blocks + 2 * jj]
        second = f_ref[p * blocks + 2 * jj + 1]

        @pl.when((first > 0) | (second > 0))
        def _():
            g = jnp.dot(m_ref[...], ct_ref[p], preferred_element_type=jnp.float32).astype(jnp.bfloat16)
            for o in range(2):
                rows = slice(o * span, (o + 1) * span)
                part = jnp.dot(cr_ref[p], g[rows, :width], preferred_element_type=jnp.float32)
                part = part - jnp.dot(sr_ref[p], g[rows, width:], preferred_element_type=jnp.float32)
                acc_ref[p, o] = acc_ref[p, o] + part

    @pl.when(i == n_steps - 1)
    def _():
        if final:
            for p in range(peaks_n):
                for o in range(2):
                    @pl.when(f_ref[p * blocks + 2 * jj + o] > 0)
                    def _():
                        score = acc_ref[p, o] / size
                        best_ref[p] = jnp.maximum(best_ref[p], score)
                        pow_ref[p] = pow_ref[p] + score * score
        else:
            part_ref[...] = acc_ref[...]


def match_rows(flags, tas, tbs, rids, offs, tmpl_a, tmpl_b, spec, col_table, cos_t, sin_t, init=None):
    _, blocks, _, rows_t, size = tmpl_a.shape
    peaks_n, width = cos_t.shape[0], cos_t.shape[1]
    n_steps = tas.shape[0]
    final = init is not None
    chunk = math.gcd(rows_t, 16)
    span = 2 * rows_t
    kernel = functools.partial(rows_kernel, blocks, size, width, rows_t, peaks_n, chunk, n_steps, final)
    flops = blocks * peaks_n * n_steps * (2 * span * 2 * size * 2 * width + 2 * 2 * width * span * width)
    cost = pl.CostEstimate(flops=flops, transcendentals=0, bytes_accessed=n_steps * blocks * 2 * span * size * 6 + col_table.size * 2)
    in_specs = [
        pl.BlockSpec((1, 2, 2, rows_t, size), lambda j, i, f, ta, tb, r, o: (ta[i], j, 0, 0, 0)),
        pl.BlockSpec((1, 2, 2, rows_t, size), lambda j, i, f, ta, tb, r, o: (tb[i], j, 0, 0, 0)),
        pl.BlockSpec((2, span, size), lambda j, i, f, ta, tb, r, o: (0, r[i], 0)),
        pl.BlockSpec(col_table.shape, lambda j, i, f, ta, tb, r, o: (0, 0, 0)),
        pl.BlockSpec((peaks_n, width, span), lambda j, i, f, ta, tb, r, o: (0, 0, r[i])),
        pl.BlockSpec((peaks_n, width, span), lambda j, i, f, ta, tb, r, o: (0, 0, r[i])),
    ]
    args = [flags, tas, tbs, rids, offs, tmpl_a, tmpl_b, spec, col_table, cos_t, sin_t]
    part_spec = pl.BlockSpec((peaks_n, 2, width, width), lambda j, i, f, ta, tb, r, o: (0, j, 0, 0))
    if final:
        in_specs.append(part_spec)
        args.append(init)
        out_shape = jax.ShapeDtypeStruct((2, peaks_n, width, width), jnp.float32)
        out_specs = pl.BlockSpec((2, peaks_n, width, width), lambda j, i, f, ta, tb, r, o: (0, 0, 0, 0))
    else:
        out_shape = jax.ShapeDtypeStruct((peaks_n, blocks, width, width), jnp.float32)
        out_specs = part_spec
    return pl.pallas_call(
        kernel,
        grid_spec=pltpu.PrefetchScalarGridSpec(
            num_scalar_prefetch=5,
            grid=(blocks // 2, n_steps),
            in_specs=in_specs,
            out_specs=out_specs,
            scratch_shapes=[pltpu.VMEM((peaks_n, 2, width, width), jnp.float32), pltpu.VMEM((2 * span, 2 * size), jnp.bfloat16)],
        ),
        out_shape=out_shape,
        compiler_params=pltpu.CompilerParams(dimension_semantics=("arbitrary", "arbitrary")),
        cost_estimate=cost,
    )(*args)


def local(tile_spectra, template_spectra, peaks, listed):
    size = tile_spectra.shape[3]
    width = W
    tiles = lax.axis_size("tile")
    rows_t = template_spectra.shape[2]
    tmpl = lax.all_gather(template_spectra, "tile", axis=0)
    block_size = tmpl.shape[1]
    spec = gather_rows(tile_spectra[0], "orient")
    spec = jnp.moveaxis(spec, 0, 1).reshape(2, size, size)
    freqs = jnp.arange(size, dtype=jnp.int32)
    cos_row, sin_row = angle_tables(freqs, peaks[0][:, 0], size, width)
    cos_t = jnp.swapaxes(cos_row, 1, 2)
    sin_t = jnp.swapaxes(sin_row, 1, 2)
    col_table = col_tables(peaks[0], size, width)
    listed_ids = listed[0]
    global_ids = lax.axis_index("orient") * block_size + jnp.arange(block_size, dtype=jnp.int32)
    is_listed = jnp.any(listed_ids[:, :, None] == global_ids[None, None, :], axis=1)
    flags = is_listed.astype(jnp.int32).reshape(-1)
    best_shape = (listed.shape[1], width, width)
    if rows_t % 128 != 0 or tiles % 2 != 0 or block_size % 2 != 0:
        best_part, power_part = match(flags, tmpl, spec, col_table, cos_t, sin_t)
    else:
        me = lax.axis_index("tile")
        sibling = lax.ppermute(template_spectra, "tile", xor_pairs(tiles, 1))
        spec32 = spec.astype(jnp.float32)
        chip = me // 2
        odd = (me % 2).astype(jnp.int32)
        zero = jnp.zeros((1,), jnp.int32)
        near_offs = jnp.stack([odd, 1 - odd]) * rows_t
        own, sib = template_spectra[None], sibling[None]
        partial = match_rows(flags, zero, zero, chip[None].astype(jnp.int32), near_offs, own, sib, spec32, col_table, cos_t, sin_t)
        far = far_chips(chip, tiles // 2)
        far_offs = jnp.array([0, rows_t], jnp.int32)
        joined = match_rows(flags, far * 2, far * 2 + 1, far, far_offs, tmpl, tmpl, spec32, col_table, cos_t, sin_t, init=partial)
        best_all, power_all = reduce_joined(joined.reshape(2, -1, width), best_shape, "orient")
        return (best_all[None], (power_all / LIST)[None])
    best_all, power_all = reduce_orient(best_part, power_part, "orient")
    return (best_all[None], (power_all / LIST)[None])


def far_chips(chip, chips):
    steps = jnp.arange(chips - 1, dtype=jnp.int32)
    return steps + (steps >= chip).astype(jnp.int32)


def solution(mesh):
    placed = (
        P("tile", None, "orient", None),
        P("orient", None, "tile", None),
        P("tile", None, None),
        P("tile", None, None),
    )
    return jax.shard_map(
        local,
        mesh=mesh,
        in_specs=placed,
        out_specs=(P("tile", None, None, None), P("tile", None, None, None)),
        check_vma=False,
    )
```

```python
import functools
import math

import jax
import jax.numpy as jnp
from jax import lax
from jax.experimental import pallas as pl
from jax.experimental.pallas import tpu as pltpu
from jax.sharding import PartitionSpec as P

W = 128
LIST = 48


lowest_score = -1e30


def xor_pairs(n, k):
    return [(i, i ^ k) for i in range(n)]


def is_pow2(n):
    return n & (n - 1) == 0


def angle_tables(freqs, coords, size, width):
    offsets = jnp.arange(width, dtype=jnp.int32) - width // 2
    position = (coords[:, None] + offsets[None, :]) % size
    phase = freqs[None, :, None] * position[:, None, :] % size
    angle = phase.astype(jnp.float32) * (2.0 * math.pi / size)
    return (jnp.cos(angle).astype(jnp.bfloat16), jnp.sin(angle).astype(jnp.bfloat16))


def col_tables(peak_rows, size, width):
    freqs = jnp.arange(size, dtype=jnp.int32)
    cos_col, sin_col = angle_tables(freqs, peak_rows[:, 1], size, width)
    upper = jnp.concatenate([cos_col, sin_col], axis=-1)
    lower = jnp.concatenate([-sin_col, cos_col], axis=-1)
    return jnp.concatenate([upper, lower], axis=1)


def gather_rows(part, axis):
    n = lax.axis_size(axis)
    if not is_pow2(n):
        return lax.all_gather(part, axis)
    me = lax.axis_index(axis)
    blocks = part[None]
    k = n // 2
    while k >= 1:
        got = lax.ppermute(blocks, axis, xor_pairs(n, k))
        blocks = jnp.concatenate([blocks, got])
        k //= 2
    want = jnp.arange(n, dtype=jnp.int32) ^ me
    return blocks[order_of(want, n)]


def order_of(want, count):
    steps = int(math.log2(count))
    slot = jnp.zeros_like(want)
    for j in range(steps):
        k = count >> (j + 1)
        hit = (want & k) != 0
        slot = slot | jnp.where(hit, 1 << j, 0)
    return slot


def reduce_orient(best_part, power_part, axis):
    n = lax.axis_size(axis)
    if not is_pow2(n):
        best = lax.pmax(best_part, axis)
        power = lax.psum(power_part, axis)
        return best, power
    width = best_part.shape[-1]
    joined = jnp.stack([best_part.reshape(-1, width), power_part.reshape(-1, width)], axis=0)
    return reduce_joined(joined, best_part.shape, axis)


def reduce_joined(joined, shape, axis):
    n = lax.axis_size(axis)
    if not is_pow2(n):
        best = lax.pmax(joined[0], axis)
        power = lax.psum(joined[1], axis)
        return best.reshape(shape), power.reshape(shape)
    me = lax.axis_index(axis)
    cur = joined
    k = 1
    while k < n:
        half = cur.shape[1] // 2
        bit = (me // k) % 2
        keep = lax.dynamic_slice_in_dim(cur, bit * half, half, axis=1)
        send = lax.dynamic_slice_in_dim(cur, (1 - bit) * half, half, axis=1)
        got = lax.ppermute(send, axis, xor_pairs(n, k))
        cur = jnp.stack([jnp.maximum(keep[0], got[0]), keep[1] + got[1]])
        k *= 2
    k = n // 2
    while k >= 1:
        got = lax.ppermute(cur, axis, xor_pairs(n, k))
        bit = (me // k) % 2
        cur = jnp.where(bit == 1, jnp.concatenate([got, cur], axis=1), jnp.concatenate([cur, got], axis=1))
        k //= 2
    return cur[0].reshape(shape), cur[1].reshape(shape)


def match_kernel(blocks, size, width, rows_t, tiles, peaks_n, l_ref, tm_ref, sp_ref, ct_ref, cr_ref, sr_ref, best_ref, pow_ref, m_ref):
    j = pl.program_id(0)

    @pl.when(j == 0)
    def _():
        best_ref[...] = jnp.full(best_ref.shape, lowest_score, jnp.float32)
        pow_ref[...] = jnp.zeros(pow_ref.shape, jnp.float32)

    for t in range(tiles):
        rows = pl.ds(t * rows_t, rows_t)
        image_re = sp_ref[0, rows, :].astype(jnp.float32)
        image_im = sp_ref[1, rows, :].astype(jnp.float32)
        tmpl_re = tm_ref[t, 0, 0].astype(jnp.float32)
        tmpl_im = tm_ref[t, 0, 1].astype(jnp.float32)
        m_ref[rows, pl.ds(0, size)] = (image_re * tmpl_re + image_im * tmpl_im).astype(jnp.bfloat16)
        m_ref[rows, pl.ds(size, size)] = (image_im * tmpl_re - image_re * tmpl_im).astype(jnp.bfloat16)

    for p in range(peaks_n):
        @pl.when(l_ref[p * blocks + j] > 0)
        def _():
            g = jnp.dot(m_ref[...], ct_ref[p], preferred_element_type=jnp.float32).astype(jnp.bfloat16)
            score = jnp.dot(cr_ref[p], g[:, :width], preferred_element_type=jnp.float32)
            score = score - jnp.dot(sr_ref[p], g[:, width:], preferred_element_type=jnp.float32)
            score = score / size
            best_ref[p] = jnp.maximum(best_ref[p], score)
            pow_ref[p] = pow_ref[p] + score * score


def match(flags, tmpl, spec, col_table, cos_t, sin_t):
    tiles, blocks, _, rows_t, size = tmpl.shape
    peaks_n, width = cos_t.shape[0], cos_t.shape[1]
    kernel = functools.partial(match_kernel, blocks, size, width, rows_t, tiles, peaks_n)
    flops = blocks * peaks_n * (2 * size * 2 * size * 2 * width + 2 * 2 * width * size * width)
    cost = pl.CostEstimate(flops=flops, transcendentals=0, bytes_accessed=tmpl.size * 2 + spec.size * 2 + col_table.size * 2)
    out = jax.ShapeDtypeStruct((peaks_n, width, width), jnp.float32)
    return pl.pallas_call(
        kernel,
        grid_spec=pltpu.PrefetchScalarGridSpec(
            num_scalar_prefetch=1,
            grid=(blocks,),
            in_specs=[
                pl.BlockSpec((tiles, 1, 2, rows_t, size), lambda j, l: (0, j, 0, 0, 0)),
                pl.BlockSpec((2, size, size), lambda j, l: (0, 0, 0)),
                pl.BlockSpec(col_table.shape, lambda j, l: (0, 0, 0)),
                pl.BlockSpec(cos_t.shape, lambda j, l: (0, 0, 0)),
                pl.BlockSpec(sin_t.shape, lambda j, l: (0, 0, 0)),
            ],
            out_specs=[
                pl.BlockSpec((peaks_n, width, width), lambda j, l: (0, 0, 0)),
                pl.BlockSpec((peaks_n, width, width), lambda j, l: (0, 0, 0)),
            ],
            scratch_shapes=[pltpu.VMEM((size, 2 * size), jnp.bfloat16)],
        ),
        out_shape=[out, out],
        compiler_params=pltpu.CompilerParams(dimension_semantics=("arbitrary",)),
        cost_estimate=cost,
    )(flags, tmpl, spec, col_table, cos_t, sin_t)


def rows_kernel(blocks, size, width, rows_t, peaks_n, chunk, n_steps, final, per, f_ref, ta_ref, tb_ref, rid_ref, off_ref, tma_ref, tmb_ref, sp_ref, ct_ref, cr_ref, sr_ref, *rest):
    if final:
        init_ref, out_ref, acc_ref, m_ref = rest
        best_ref, pow_ref = out_ref.at[0], out_ref.at[1]
    else:
        part_ref, acc_ref, m_ref = rest
    jj = pl.program_id(0)
    i = pl.program_id(1)
    span = 2 * rows_t

    if final:
        @pl.when((jj == 0) & (i == 0))
        def _():
            best_ref[...] = jnp.full(best_ref.shape, lowest_score, jnp.float32)
            pow_ref[...] = jnp.zeros(pow_ref.shape, jnp.float32)

        @pl.when(i == 0)
        def _():
            acc_ref[...] = init_ref[...]
    else:
        @pl.when(i == 0)
        def _():
            acc_ref[...] = jnp.zeros(acc_ref.shape, jnp.float32)

    for o in range(per):
        for u, tm_ref in enumerate((tma_ref, tmb_ref)):
            def mix(c, carry, u=u, o=o, tm_ref=tm_ref):
                row = pl.multiple_of(c * chunk, chunk)
                in_row = pl.multiple_of(off_ref[u] + c * chunk, chunk)
                out_row = pl.multiple_of(o * span + off_ref[u] + c * chunk, chunk)
                image_re = sp_ref[0, pl.ds(in_row, chunk), :]
                image_im = sp_ref[1, pl.ds(in_row, chunk), :]
                tmpl_re = tm_ref[0, o, 0, pl.ds(row, chunk), :].astype(jnp.float32)
                tmpl_im = tm_ref[0, o, 1, pl.ds(row, chunk), :].astype(jnp.float32)
                m_ref[pl.ds(out_row, chunk), pl.ds(0, size)] = (image_re * tmpl_re + image_im * tmpl_im).astype(jnp.bfloat16)
                m_ref[pl.ds(out_row, chunk), pl.ds(size, size)] = (image_im * tmpl_re - image_re * tmpl_im).astype(jnp.bfloat16)
                return carry

            lax.fori_loop(0, rows_t // chunk, mix, 0, unroll=4)

    for p in range(peaks_n):
        count = f_ref[p * blocks + per * jj]
        for o in range(1, per):
            count = count + f_ref[p * blocks + per * jj + o]

        @pl.when(count > 0)
        def _():
            g = jnp.dot(m_ref[...], ct_ref[p], preferred_element_type=jnp.float32).astype(jnp.bfloat16)
            for o in range(per):
                rows = slice(o * span, (o + 1) * span)
                part = jnp.dot(cr_ref[p], g[rows, :width], preferred_element_type=jnp.float32)
                part = part - jnp.dot(sr_ref[p], g[rows, width:], preferred_element_type=jnp.float32)
                acc_ref[p, o] = acc_ref[p, o] + part

    @pl.when(i == n_steps - 1)
    def _():
        if final:
            for p in range(peaks_n):
                for o in range(per):
                    @pl.when(f_ref[p * blocks + per * jj + o] > 0)
                    def _():
                        score = acc_ref[p, o] / size
                        best_ref[p] = jnp.maximum(best_ref[p], score)
                        pow_ref[p] = pow_ref[p] + score * score
        else:
            part_ref[...] = acc_ref[...]


def match_rows(flags, tas, tbs, rids, offs, tmpl_a, tmpl_b, spec, col_table, cos_t, sin_t, init=None):
    _, blocks, _, rows_t, size = tmpl_a.shape
    peaks_n, width = cos_t.shape[0], cos_t.shape[1]
    n_steps = tas.shape[0]
    final = init is not None
    chunk = math.gcd(rows_t, 16)
    span = 2 * rows_t
    per = 4 if blocks % 4 == 0 else 2
    kernel = functools.partial(rows_kernel, blocks, size, width, rows_t, peaks_n, chunk, n_steps, final, per)
    flops = blocks * peaks_n * n_steps * (2 * span * 2 * size * 2 * width + 2 * 2 * width * span * width)
    cost = pl.CostEstimate(flops=flops, transcendentals=0, bytes_accessed=n_steps * blocks * 2 * span * size * 6 + col_table.size * 2)
    in_specs = [
        pl.BlockSpec((1, per, 2, rows_t, size), lambda j, i, f, ta, tb, r, o: (ta[i], j, 0, 0, 0)),
        pl.BlockSpec((1, per, 2, rows_t, size), lambda j, i, f, ta, tb, r, o: (tb[i], j, 0, 0, 0)),
        pl.BlockSpec((2, span, size), lambda j, i, f, ta, tb, r, o: (0, r[i], 0)),
        pl.BlockSpec(col_table.shape, lambda j, i, f, ta, tb, r, o: (0, 0, 0)),
        pl.BlockSpec((peaks_n, width, span), lambda j, i, f, ta, tb, r, o: (0, 0, r[i])),
        pl.BlockSpec((peaks_n, width, span), lambda j, i, f, ta, tb, r, o: (0, 0, r[i])),
    ]
    args = [flags, tas, tbs, rids, offs, tmpl_a, tmpl_b, spec, col_table, cos_t, sin_t]
    part_spec = pl.BlockSpec((peaks_n, per, width, width), lambda j, i, f, ta, tb, r, o: (0, j, 0, 0))
    if final:
        in_specs.append(part_spec)
        args.append(init)
        out_shape = jax.ShapeDtypeStruct((2, peaks_n, width, width), jnp.float32)
        out_specs = pl.BlockSpec((2, peaks_n, width, width), lambda j, i, f, ta, tb, r, o: (0, 0, 0, 0))
    else:
        out_shape = jax.ShapeDtypeStruct((peaks_n, blocks, width, width), jnp.float32)
        out_specs = part_spec
    return pl.pallas_call(
        kernel,
        grid_spec=pltpu.PrefetchScalarGridSpec(
            num_scalar_prefetch=5,
            grid=(blocks // per, n_steps),
            in_specs=in_specs,
            out_specs=out_specs,
            scratch_shapes=[pltpu.VMEM((peaks_n, per, width, width), jnp.float32), pltpu.VMEM((per * span, 2 * size), jnp.bfloat16)],
        ),
        out_shape=out_shape,
        compiler_params=pltpu.CompilerParams(dimension_semantics=("arbitrary", "arbitrary")),
        cost_estimate=cost,
    )(*args)


def local(tile_spectra, template_spectra, peaks, listed):
    size = tile_spectra.shape[3]
    width = W
    tiles = lax.axis_size("tile")
    rows_t = template_spectra.shape[2]
    tmpl = lax.all_gather(template_spectra, "tile", axis=0)
    block_size = tmpl.shape[1]
    spec = gather_rows(tile_spectra[0], "orient")
    spec = jnp.moveaxis(spec, 0, 1).reshape(2, size, size)
    freqs = jnp.arange(size, dtype=jnp.int32)
    cos_row, sin_row = angle_tables(freqs, peaks[0][:, 0], size, width)
    cos_t = jnp.swapaxes(cos_row, 1, 2)
    sin_t = jnp.swapaxes(sin_row, 1, 2)
    col_table = col_tables(peaks[0], size, width)
    listed_ids = listed[0]
    global_ids = lax.axis_index("orient") * block_size + jnp.arange(block_size, dtype=jnp.int32)
    is_listed = jnp.any(listed_ids[:, :, None] == global_ids[None, None, :], axis=1)
    flags = is_listed.astype(jnp.int32).reshape(-1)
    best_shape = (listed.shape[1], width, width)
    if rows_t % 128 != 0 or tiles % 2 != 0 or block_size % 2 != 0:
        best_part, power_part = match(flags, tmpl, spec, col_table, cos_t, sin_t)
    else:
        me = lax.axis_index("tile")
        sibling = lax.ppermute(template_spectra, "tile", xor_pairs(tiles, 1))
        spec32 = spec.astype(jnp.float32)
        chip = me // 2
        odd = (me % 2).astype(jnp.int32)
        zero = jnp.zeros((1,), jnp.int32)
        near_offs = jnp.stack([odd, 1 - odd]) * rows_t
        own, sib = template_spectra[None], sibling[None]
        partial = match_rows(flags, zero, zero, chip[None].astype(jnp.int32), near_offs, own, sib, spec32, col_table, cos_t, sin_t)
        far = far_chips(chip, tiles // 2)
        far_offs = jnp.array([0, rows_t], jnp.int32)
        joined = match_rows(flags, far * 2, far * 2 + 1, far, far_offs, tmpl, tmpl, spec32, col_table, cos_t, sin_t, init=partial)
        best_all, power_all = reduce_joined(joined.reshape(2, -1, width), best_shape, "orient")
        return (best_all[None], (power_all / LIST)[None])
    best_all, power_all = reduce_orient(best_part, power_part, "orient")
    return (best_all[None], (power_all / LIST)[None])


def far_chips(chip, chips):
    steps = jnp.arange(chips - 1, dtype=jnp.int32)
    return steps + (steps >= chip).astype(jnp.int32)


def solution(mesh):
    placed = (
        P("tile", None, "orient", None),
        P("orient", None, "tile", None),
        P("tile", None, None),
        P("tile", None, None),
    )
    return jax.shard_map(
        local,
        mesh=mesh,
        in_specs=placed,
        out_specs=(P("tile", None, None, None), P("tile", None, None, None)),
        check_vma=False,
    )
```

```python
import functools
import math

import jax
import jax.numpy as jnp
from jax import lax
from jax.experimental import pallas as pl
from jax.experimental.pallas import tpu as pltpu
from jax.sharding import PartitionSpec as P

W = 128
LIST = 48


lowest_score = -1e30


def xor_pairs(n, k):
    return [(i, i ^ k) for i in range(n)]


def is_pow2(n):
    return n & (n - 1) == 0


def angle_tables(freqs, coords, size, width):
    offsets = jnp.arange(width, dtype=jnp.int32) - width // 2
    position = (coords[:, None] + offsets[None, :]) % size
    phase = freqs[None, :, None] * position[:, None, :] % size
    angle = phase.astype(jnp.float32) * (2.0 * math.pi / size)
    return (jnp.cos(angle).astype(jnp.bfloat16), jnp.sin(angle).astype(jnp.bfloat16))


def col_tables(peak_rows, size, width):
    freqs = jnp.arange(size, dtype=jnp.int32)
    cos_col, sin_col = angle_tables(freqs, peak_rows[:, 1], size, width)
    upper = jnp.concatenate([cos_col, sin_col], axis=-1)
    lower = jnp.concatenate([-sin_col, cos_col], axis=-1)
    return jnp.concatenate([upper, lower], axis=1)


def gather_rows(part, axis):
    n = lax.axis_size(axis)
    if not is_pow2(n):
        return lax.all_gather(part, axis)
    me = lax.axis_index(axis)
    blocks = part[None]
    k = n // 2
    while k >= 1:
        got = lax.ppermute(blocks, axis, xor_pairs(n, k))
        blocks = jnp.concatenate([blocks, got])
        k //= 2
    want = jnp.arange(n, dtype=jnp.int32) ^ me
    return blocks[order_of(want, n)]


def order_of(want, count):
    steps = int(math.log2(count))
    slot = jnp.zeros_like(want)
    for j in range(steps):
        k = count >> (j + 1)
        hit = (want & k) != 0
        slot = slot | jnp.where(hit, 1 << j, 0)
    return slot


def reduce_orient(best_part, power_part, axis):
    n = lax.axis_size(axis)
    if not is_pow2(n):
        best = lax.pmax(best_part, axis)
        power = lax.psum(power_part, axis)
        return best, power
    width = best_part.shape[-1]
    joined = jnp.stack([best_part.reshape(-1, width), power_part.reshape(-1, width)], axis=0)
    return reduce_joined(joined, best_part.shape, axis)


def reduce_joined(joined, shape, axis):
    n = lax.axis_size(axis)
    rows = joined.shape[1]
    if not is_pow2(n) or rows % n != 0:
        best = lax.pmax(joined[0], axis)
        power = lax.psum(joined[1], axis)
        return best.reshape(shape), power.reshape(shape)
    me = lax.axis_index(axis)
    piece = rows // n
    own = lax.dynamic_slice_in_dim(joined, me * piece, piece, axis=1)
    bests, powers = [own[0]], [own[1]]
    for k in range(1, n):
        send = lax.dynamic_slice_in_dim(joined, (me ^ k) * piece, piece, axis=1)
        got = lax.ppermute(send, axis, xor_pairs(n, k))
        bests.append(got[0])
        powers.append(got[1])
    best = bests[0]
    power = powers[0]
    for b, p in zip(bests[1:], powers[1:]):
        best = jnp.maximum(best, b)
        power = power + p
    done = jnp.stack([best, power])
    slots = [done] + [lax.ppermute(done, axis, xor_pairs(n, k)) for k in range(1, n)]
    pieces = jnp.stack(slots)[jnp.arange(n, dtype=jnp.int32) ^ me]
    whole = jnp.moveaxis(pieces, 0, 1).reshape(2, rows, joined.shape[2])
    return whole[0].reshape(shape), whole[1].reshape(shape)


def match_kernel(blocks, size, width, rows_t, tiles, peaks_n, l_ref, tm_ref, sp_ref, ct_ref, cr_ref, sr_ref, best_ref, pow_ref, m_ref):
    j = pl.program_id(0)

    @pl.when(j == 0)
    def _():
        best_ref[...] = jnp.full(best_ref.shape, lowest_score, jnp.float32)
        pow_ref[...] = jnp.zeros(pow_ref.shape, jnp.float32)

    for t in range(tiles):
        rows = pl.ds(t * rows_t, rows_t)
        image_re = sp_ref[0, rows, :].astype(jnp.float32)
        image_im = sp_ref[1, rows, :].astype(jnp.float32)
        tmpl_re = tm_ref[t, 0, 0].astype(jnp.float32)
        tmpl_im = tm_ref[t, 0, 1].astype(jnp.float32)
        m_ref[rows, pl.ds(0, size)] = (image_re * tmpl_re + image_im * tmpl_im).astype(jnp.bfloat16)
        m_ref[rows, pl.ds(size, size)] = (image_im * tmpl_re - image_re * tmpl_im).astype(jnp.bfloat16)

    for p in range(peaks_n):
        @pl.when(l_ref[p * blocks + j] > 0)
        def _():
            g = jnp.dot(m_ref[...], ct_ref[p], preferred_element_type=jnp.float32).astype(jnp.bfloat16)
            score = jnp.dot(cr_ref[p], g[:, :width], preferred_element_type=jnp.float32)
            score = score - jnp.dot(sr_ref[p], g[:, width:], preferred_element_type=jnp.float32)
            score = score / size
            best_ref[p] = jnp.maximum(best_ref[p], score)
            pow_ref[p] = pow_ref[p] + score * score


def match(flags, tmpl, spec, col_table, cos_t, sin_t):
    tiles, blocks, _, rows_t, size = tmpl.shape
    peaks_n, width = cos_t.shape[0], cos_t.shape[1]
    kernel = functools.partial(match_kernel, blocks, size, width, rows_t, tiles, peaks_n)
    flops = blocks * peaks_n * (2 * size * 2 * size * 2 * width + 2 * 2 * width * size * width)
    cost = pl.CostEstimate(flops=flops, transcendentals=0, bytes_accessed=tmpl.size * 2 + spec.size * 2 + col_table.size * 2)
    out = jax.ShapeDtypeStruct((peaks_n, width, width), jnp.float32)
    return pl.pallas_call(
        kernel,
        grid_spec=pltpu.PrefetchScalarGridSpec(
            num_scalar_prefetch=1,
            grid=(blocks,),
            in_specs=[
                pl.BlockSpec((tiles, 1, 2, rows_t, size), lambda j, l: (0, j, 0, 0, 0)),
                pl.BlockSpec((2, size, size), lambda j, l: (0, 0, 0)),
                pl.BlockSpec(col_table.shape, lambda j, l: (0, 0, 0)),
                pl.BlockSpec(cos_t.shape, lambda j, l: (0, 0, 0)),
                pl.BlockSpec(sin_t.shape, lambda j, l: (0, 0, 0)),
            ],
            out_specs=[
                pl.BlockSpec((peaks_n, width, width), lambda j, l: (0, 0, 0)),
                pl.BlockSpec((peaks_n, width, width), lambda j, l: (0, 0, 0)),
            ],
            scratch_shapes=[pltpu.VMEM((size, 2 * size), jnp.bfloat16)],
        ),
        out_shape=[out, out],
        compiler_params=pltpu.CompilerParams(dimension_semantics=("arbitrary",)),
        cost_estimate=cost,
    )(flags, tmpl, spec, col_table, cos_t, sin_t)


def rows_kernel(blocks, size, width, rows_t, peaks_n, chunk, n_steps, final, per, f_ref, ta_ref, tb_ref, rid_ref, off_ref, tma_ref, tmb_ref, sp_ref, ct_ref, cr_ref, sr_ref, *rest):
    if final:
        init_ref, out_ref, acc_ref, m_ref = rest
        best_ref, pow_ref = out_ref.at[0], out_ref.at[1]
    else:
        part_ref, acc_ref, m_ref = rest
    jj = pl.program_id(0)
    i = pl.program_id(1)
    span = 2 * rows_t

    if final:
        @pl.when((jj == 0) & (i == 0))
        def _():
            best_ref[...] = jnp.full(best_ref.shape, lowest_score, jnp.float32)
            pow_ref[...] = jnp.zeros(pow_ref.shape, jnp.float32)

        @pl.when(i == 0)
        def _():
            acc_ref[...] = init_ref[...]
    else:
        @pl.when(i == 0)
        def _():
            acc_ref[...] = jnp.zeros(acc_ref.shape, jnp.float32)

    for o in range(per):
        for u, tm_ref in enumerate((tma_ref, tmb_ref)):
            def mix(c, carry, u=u, o=o, tm_ref=tm_ref):
                row = pl.multiple_of(c * chunk, chunk)
                in_row = pl.multiple_of(off_ref[u] + c * chunk, chunk)
                out_row = pl.multiple_of(o * span + off_ref[u] + c * chunk, chunk)
                image_re = sp_ref[0, pl.ds(in_row, chunk), :]
                image_im = sp_ref[1, pl.ds(in_row, chunk), :]
                tmpl_re = tm_ref[0, o, 0, pl.ds(row, chunk), :].astype(jnp.float32)
                tmpl_im = tm_ref[0, o, 1, pl.ds(row, chunk), :].astype(jnp.float32)
                m_ref[pl.ds(out_row, chunk), pl.ds(0, size)] = (image_re * tmpl_re + image_im * tmpl_im).astype(jnp.bfloat16)
                m_ref[pl.ds(out_row, chunk), pl.ds(size, size)] = (image_im * tmpl_re - image_re * tmpl_im).astype(jnp.bfloat16)
                return carry

            lax.fori_loop(0, rows_t // chunk, mix, 0, unroll=4)

    for p in range(peaks_n):
        count = f_ref[p * blocks + per * jj]
        for o in range(1, per):
            count = count + f_ref[p * blocks + per * jj + o]

        @pl.when(count > 0)
        def _():
            g = jnp.dot(m_ref[...], ct_ref[p], preferred_element_type=jnp.float32).astype(jnp.bfloat16)
            for o in range(per):
                rows = slice(o * span, (o + 1) * span)
                part = jnp.dot(cr_ref[p], g[rows, :width], preferred_element_type=jnp.float32)
                part = part - jnp.dot(sr_ref[p], g[rows, width:], preferred_element_type=jnp.float32)
                acc_ref[p, o] = acc_ref[p, o] + part

    @pl.when(i == n_steps - 1)
    def _():
        if final:
            for p in range(peaks_n):
                for o in range(per):
                    @pl.when(f_ref[p * blocks + per * jj + o] > 0)
                    def _():
                        score = acc_ref[p, o] / size
                        best_ref[p] = jnp.maximum(best_ref[p], score)
                        pow_ref[p] = pow_ref[p] + score * score
        else:
            part_ref[...] = acc_ref[...]


def match_rows(flags, tas, tbs, rids, offs, tmpl_a, tmpl_b, spec, col_table, cos_t, sin_t, init=None):
    _, blocks, _, rows_t, size = tmpl_a.shape
    peaks_n, width = cos_t.shape[0], cos_t.shape[1]
    n_steps = tas.shape[0]
    final = init is not None
    chunk = math.gcd(rows_t, 16)
    span = 2 * rows_t
    per = 4 if blocks % 4 == 0 else 2
    kernel = functools.partial(rows_kernel, blocks, size, width, rows_t, peaks_n, chunk, n_steps, final, per)
    flops = blocks * peaks_n * n_steps * (2 * span * 2 * size * 2 * width + 2 * 2 * width * span * width)
    cost = pl.CostEstimate(flops=flops, transcendentals=0, bytes_accessed=n_steps * blocks * 2 * span * size * 6 + col_table.size * 2)
    in_specs = [
        pl.BlockSpec((1, per, 2, rows_t, size), lambda j, i, f, ta, tb, r, o: (ta[i], j, 0, 0, 0)),
        pl.BlockSpec((1, per, 2, rows_t, size), lambda j, i, f, ta, tb, r, o: (tb[i], j, 0, 0, 0)),
        pl.BlockSpec((2, span, size), lambda j, i, f, ta, tb, r, o: (0, r[i], 0)),
        pl.BlockSpec(col_table.shape, lambda j, i, f, ta, tb, r, o: (0, 0, 0)),
        pl.BlockSpec((peaks_n, width, span), lambda j, i, f, ta, tb, r, o: (0, 0, r[i])),
        pl.BlockSpec((peaks_n, width, span), lambda j, i, f, ta, tb, r, o: (0, 0, r[i])),
    ]
    args = [flags, tas, tbs, rids, offs, tmpl_a, tmpl_b, spec, col_table, cos_t, sin_t]
    part_spec = pl.BlockSpec((peaks_n, per, width, width), lambda j, i, f, ta, tb, r, o: (0, j, 0, 0))
    if final:
        in_specs.append(part_spec)
        args.append(init)
        out_shape = jax.ShapeDtypeStruct((2, peaks_n, width, width), jnp.float32)
        out_specs = pl.BlockSpec((2, peaks_n, width, width), lambda j, i, f, ta, tb, r, o: (0, 0, 0, 0))
    else:
        out_shape = jax.ShapeDtypeStruct((peaks_n, blocks, width, width), jnp.float32)
        out_specs = part_spec
    return pl.pallas_call(
        kernel,
        grid_spec=pltpu.PrefetchScalarGridSpec(
            num_scalar_prefetch=5,
            grid=(blocks // per, n_steps),
            in_specs=in_specs,
            out_specs=out_specs,
            scratch_shapes=[pltpu.VMEM((peaks_n, per, width, width), jnp.float32), pltpu.VMEM((per * span, 2 * size), jnp.bfloat16)],
        ),
        out_shape=out_shape,
        compiler_params=pltpu.CompilerParams(dimension_semantics=("arbitrary", "arbitrary")),
        cost_estimate=cost,
    )(*args)


def local(tile_spectra, template_spectra, peaks, listed):
    size = tile_spectra.shape[3]
    width = W
    tiles = lax.axis_size("tile")
    rows_t = template_spectra.shape[2]
    tmpl = lax.all_gather(template_spectra, "tile", axis=0)
    block_size = tmpl.shape[1]
    spec = gather_rows(tile_spectra[0], "orient")
    spec = jnp.moveaxis(spec, 0, 1).reshape(2, size, size)
    freqs = jnp.arange(size, dtype=jnp.int32)
    cos_row, sin_row = angle_tables(freqs, peaks[0][:, 0], size, width)
    cos_t = jnp.swapaxes(cos_row, 1, 2)
    sin_t = jnp.swapaxes(sin_row, 1, 2)
    col_table = col_tables(peaks[0], size, width)
    listed_ids = listed[0]
    global_ids = lax.axis_index("orient") * block_size + jnp.arange(block_size, dtype=jnp.int32)
    is_listed = jnp.any(listed_ids[:, :, None] == global_ids[None, None, :], axis=1)
    flags = is_listed.astype(jnp.int32).reshape(-1)
    best_shape = (listed.shape[1], width, width)
    if rows_t % 128 != 0 or tiles % 2 != 0 or block_size % 2 != 0:
        best_part, power_part = match(flags, tmpl, spec, col_table, cos_t, sin_t)
    else:
        me = lax.axis_index("tile")
        sibling = lax.ppermute(template_spectra, "tile", xor_pairs(tiles, 1))
        spec32 = spec.astype(jnp.float32)
        chip = me // 2
        odd = (me % 2).astype(jnp.int32)
        zero = jnp.zeros((1,), jnp.int32)
        near_offs = jnp.stack([odd, 1 - odd]) * rows_t
        own, sib = template_spectra[None], sibling[None]
        partial = match_rows(flags, zero, zero, chip[None].astype(jnp.int32), near_offs, own, sib, spec32, col_table, cos_t, sin_t)
        far = far_chips(chip, tiles // 2)
        far_offs = jnp.array([0, rows_t], jnp.int32)
        joined = match_rows(flags, far * 2, far * 2 + 1, far, far_offs, tmpl, tmpl, spec32, col_table, cos_t, sin_t, init=partial)
        best_all, power_all = reduce_joined(joined.reshape(2, -1, width), best_shape, "orient")
        return (best_all[None], (power_all / LIST)[None])
    best_all, power_all = reduce_orient(best_part, power_part, "orient")
    return (best_all[None], (power_all / LIST)[None])


def far_chips(chip, chips):
    steps = jnp.arange(chips - 1, dtype=jnp.int32)
    return steps + (steps >= chip).astype(jnp.int32)


def solution(mesh):
    placed = (
        P("tile", None, "orient", None),
        P("orient", None, "tile", None),
        P("tile", None, None),
        P("tile", None, None),
    )
    return jax.shard_map(
        local,
        mesh=mesh,
        in_specs=placed,
        out_specs=(P("tile", None, None, None), P("tile", None, None, None)),
        check_vma=False,
    )
```

```python
import functools
import math

import jax
import jax.numpy as jnp
from jax import lax
from jax.experimental import pallas as pl
from jax.experimental.pallas import tpu as pltpu
from jax.sharding import PartitionSpec as P

W = 128
LIST = 48


lowest_score = -1e30


def xor_pairs(n, k):
    return [(i, i ^ k) for i in range(n)]


def is_pow2(n):
    return n & (n - 1) == 0


def angle_tables(freqs, coords, size, width):
    offsets = jnp.arange(width, dtype=jnp.int32) - width // 2
    position = (coords[:, None] + offsets[None, :]) % size
    phase = freqs[None, :, None] * position[:, None, :] % size
    angle = phase.astype(jnp.float32) * (2.0 * math.pi / size)
    return (jnp.cos(angle).astype(jnp.bfloat16), jnp.sin(angle).astype(jnp.bfloat16))


def col_tables(peak_rows, size, width):
    freqs = jnp.arange(size, dtype=jnp.int32)
    cos_col, sin_col = angle_tables(freqs, peak_rows[:, 1], size, width)
    upper = jnp.concatenate([cos_col, sin_col], axis=-1)
    lower = jnp.concatenate([-sin_col, cos_col], axis=-1)
    return jnp.concatenate([upper, lower], axis=1)


def gather_rows(part, axis):
    n = lax.axis_size(axis)
    if not is_pow2(n):
        return lax.all_gather(part, axis)
    me = lax.axis_index(axis)
    blocks = part[None]
    k = n // 2
    while k >= 1:
        got = lax.ppermute(blocks, axis, xor_pairs(n, k))
        blocks = jnp.concatenate([blocks, got])
        k //= 2
    want = jnp.arange(n, dtype=jnp.int32) ^ me
    return blocks[order_of(want, n)]


def order_of(want, count):
    steps = int(math.log2(count))
    slot = jnp.zeros_like(want)
    for j in range(steps):
        k = count >> (j + 1)
        hit = (want & k) != 0
        slot = slot | jnp.where(hit, 1 << j, 0)
    return slot


def reduce_orient(best_part, power_part, axis):
    n = lax.axis_size(axis)
    if not is_pow2(n):
        best = lax.pmax(best_part, axis)
        power = lax.psum(power_part, axis)
        return best, power
    width = best_part.shape[-1]
    joined = jnp.stack([best_part.reshape(-1, width), power_part.reshape(-1, width)], axis=0)
    return reduce_joined(joined, best_part.shape, axis)


def reduce_joined(joined, shape, axis):
    n = lax.axis_size(axis)
    rows = joined.shape[1]
    if not is_pow2(n) or rows % n != 0:
        best = lax.pmax(joined[0], axis)
        power = lax.psum(joined[1], axis)
        return best.reshape(shape), power.reshape(shape)
    me = lax.axis_index(axis)
    piece = rows // n
    own = lax.dynamic_slice_in_dim(joined, me * piece, piece, axis=1)
    bests, powers = [own[0]], [own[1]]
    for k in range(1, n):
        send = lax.dynamic_slice_in_dim(joined, (me ^ k) * piece, piece, axis=1)
        got = lax.ppermute(send, axis, xor_pairs(n, k))
        bests.append(got[0])
        powers.append(got[1])
    best = bests[0]
    power = powers[0]
    for b, p in zip(bests[1:], powers[1:]):
        best = jnp.maximum(best, b)
        power = power + p
    done = jnp.stack([best, power])
    slots = [done] + [lax.ppermute(done, axis, xor_pairs(n, k)) for k in range(1, n)]
    pieces = jnp.stack(slots)[jnp.arange(n, dtype=jnp.int32) ^ me]
    whole = jnp.moveaxis(pieces, 0, 1).reshape(2, rows, joined.shape[2])
    return whole[0].reshape(shape), whole[1].reshape(shape)


def match_kernel(blocks, size, width, rows_t, tiles, peaks_n, l_ref, tm_ref, sp_ref, ct_ref, cr_ref, sr_ref, best_ref, pow_ref, m_ref):
    j = pl.program_id(0)

    @pl.when(j == 0)
    def _():
        best_ref[...] = jnp.full(best_ref.shape, lowest_score, jnp.float32)
        pow_ref[...] = jnp.zeros(pow_ref.shape, jnp.float32)

    for t in range(tiles):
        rows = pl.ds(t * rows_t, rows_t)
        image_re = sp_ref[0, rows, :].astype(jnp.float32)
        image_im = sp_ref[1, rows, :].astype(jnp.float32)
        tmpl_re = tm_ref[t, 0, 0].astype(jnp.float32)
        tmpl_im = tm_ref[t, 0, 1].astype(jnp.float32)
        m_ref[rows, pl.ds(0, size)] = (image_re * tmpl_re + image_im * tmpl_im).astype(jnp.bfloat16)
        m_ref[rows, pl.ds(size, size)] = (image_im * tmpl_re - image_re * tmpl_im).astype(jnp.bfloat16)

    for p in range(peaks_n):
        @pl.when(l_ref[p * blocks + j] > 0)
        def _():
            g = jnp.dot(m_ref[...], ct_ref[p], preferred_element_type=jnp.float32).astype(jnp.bfloat16)
            score = jnp.dot(cr_ref[p], g[:, :width], preferred_element_type=jnp.float32)
            score = score - jnp.dot(sr_ref[p], g[:, width:], preferred_element_type=jnp.float32)
            score = score / size
            best_ref[p] = jnp.maximum(best_ref[p], score)
            pow_ref[p] = pow_ref[p] + score * score


def match(flags, tmpl, spec, col_table, cos_t, sin_t):
    tiles, blocks, _, rows_t, size = tmpl.shape
    peaks_n, width = cos_t.shape[0], cos_t.shape[1]
    kernel = functools.partial(match_kernel, blocks, size, width, rows_t, tiles, peaks_n)
    flops = blocks * peaks_n * (2 * size * 2 * size * 2 * width + 2 * 2 * width * size * width)
    cost = pl.CostEstimate(flops=flops, transcendentals=0, bytes_accessed=tmpl.size * 2 + spec.size * 2 + col_table.size * 2)
    out = jax.ShapeDtypeStruct((peaks_n, width, width), jnp.float32)
    return pl.pallas_call(
        kernel,
        grid_spec=pltpu.PrefetchScalarGridSpec(
            num_scalar_prefetch=1,
            grid=(blocks,),
            in_specs=[
                pl.BlockSpec((tiles, 1, 2, rows_t, size), lambda j, l: (0, j, 0, 0, 0)),
                pl.BlockSpec((2, size, size), lambda j, l: (0, 0, 0)),
                pl.BlockSpec(col_table.shape, lambda j, l: (0, 0, 0)),
                pl.BlockSpec(cos_t.shape, lambda j, l: (0, 0, 0)),
                pl.BlockSpec(sin_t.shape, lambda j, l: (0, 0, 0)),
            ],
            out_specs=[
                pl.BlockSpec((peaks_n, width, width), lambda j, l: (0, 0, 0)),
                pl.BlockSpec((peaks_n, width, width), lambda j, l: (0, 0, 0)),
            ],
            scratch_shapes=[pltpu.VMEM((size, 2 * size), jnp.bfloat16)],
        ),
        out_shape=[out, out],
        compiler_params=pltpu.CompilerParams(dimension_semantics=("arbitrary",)),
        cost_estimate=cost,
    )(flags, tmpl, spec, col_table, cos_t, sin_t)


def rows_kernel(blocks, size, width, rows_t, peaks_n, chunk, n_steps, final, per, f_ref, ta_ref, tb_ref, rid_ref, off_ref, tma_ref, tmb_ref, sp_ref, ct_ref, cr_ref, *rest):
    if final:
        init_ref, out_ref, acc_ref, m_ref = rest
        best_ref, pow_ref = out_ref.at[0], out_ref.at[1]
    else:
        part_ref, acc_ref, m_ref = rest
    jj = pl.program_id(0)
    i = pl.program_id(1)
    span = 2 * rows_t

    if final:
        @pl.when((jj == 0) & (i == 0))
        def _():
            best_ref[...] = jnp.full(best_ref.shape, lowest_score, jnp.float32)
            pow_ref[...] = jnp.zeros(pow_ref.shape, jnp.float32)

        @pl.when(i == 0)
        def _():
            acc_ref[...] = init_ref[...]
    else:
        @pl.when(i == 0)
        def _():
            acc_ref[...] = jnp.zeros(acc_ref.shape, jnp.float32)

    for o in range(per):
        for u, tm_ref in enumerate((tma_ref, tmb_ref)):
            def mix(c, carry, u=u, o=o, tm_ref=tm_ref):
                row = pl.multiple_of(c * chunk, chunk)
                in_row = pl.multiple_of(off_ref[u] + c * chunk, chunk)
                out_row = pl.multiple_of(o * span + off_ref[u] + c * chunk, chunk)
                image_re = sp_ref[0, pl.ds(in_row, chunk), :]
                image_im = sp_ref[1, pl.ds(in_row, chunk), :]
                tmpl_re = tm_ref[0, o, 0, pl.ds(row, chunk), :].astype(jnp.float32)
                tmpl_im = tm_ref[0, o, 1, pl.ds(row, chunk), :].astype(jnp.float32)
                m_ref[pl.ds(out_row, chunk), pl.ds(0, size)] = (image_re * tmpl_re + image_im * tmpl_im).astype(jnp.bfloat16)
                m_ref[pl.ds(out_row, chunk), pl.ds(size, size)] = (image_im * tmpl_re - image_re * tmpl_im).astype(jnp.bfloat16)
                return carry

            lax.fori_loop(0, rows_t // chunk, mix, 0, unroll=4)

    for p in range(peaks_n):
        count = f_ref[p * blocks + per * jj]
        for o in range(1, per):
            count = count + f_ref[p * blocks + per * jj + o]

        @pl.when(count > 0)
        def _():
            g = jnp.dot(m_ref[...], ct_ref[p], preferred_element_type=jnp.float32).astype(jnp.bfloat16)
            for o in range(per):
                rows = slice(o * span, (o + 1) * span)
                stacked = jnp.concatenate([g[rows, :width], g[rows, width:]], axis=0)
                part = jnp.dot(cr_ref[p, 0], stacked, preferred_element_type=jnp.float32)
                acc_ref[p, o] = acc_ref[p, o] + part

    @pl.when(i == n_steps - 1)
    def _():
        if final:
            for p in range(peaks_n):
                for o in range(per):
                    @pl.when(f_ref[p * blocks + per * jj + o] > 0)
                    def _():
                        score = acc_ref[p, o] / size
                        best_ref[p] = jnp.maximum(best_ref[p], score)
                        pow_ref[p] = pow_ref[p] + score * score
        else:
            part_ref[...] = acc_ref[...]


def match_rows(flags, tas, tbs, rids, offs, tmpl_a, tmpl_b, spec, col_table, cos_t, sin_t, init=None):
    _, blocks, _, rows_t, size = tmpl_a.shape
    peaks_n, width = cos_t.shape[0], cos_t.shape[1]
    n_steps = tas.shape[0]
    final = init is not None
    chunk = math.gcd(rows_t, 16)
    span = 2 * rows_t
    per = 4 if blocks % 4 == 0 else 2
    kernel = functools.partial(rows_kernel, blocks, size, width, rows_t, peaks_n, chunk, n_steps, final, per)
    flops = blocks * peaks_n * n_steps * (2 * span * 2 * size * 2 * width + 2 * 2 * width * span * width)
    cost = pl.CostEstimate(flops=flops, transcendentals=0, bytes_accessed=n_steps * blocks * 2 * span * size * 6 + col_table.size * 2)
    in_specs = [
        pl.BlockSpec((1, per, 2, rows_t, size), lambda j, i, f, ta, tb, r, o: (ta[i], j, 0, 0, 0)),
        pl.BlockSpec((1, per, 2, rows_t, size), lambda j, i, f, ta, tb, r, o: (tb[i], j, 0, 0, 0)),
        pl.BlockSpec((2, span, size), lambda j, i, f, ta, tb, r, o: (0, r[i], 0)),
        pl.BlockSpec(col_table.shape, lambda j, i, f, ta, tb, r, o: (0, 0, 0)),
        pl.BlockSpec((peaks_n, 1, width, 2 * span), lambda j, i, f, ta, tb, r, o: (0, r[i], 0, 0)),
    ]
    chips = cos_t.shape[2] // span
    row_table = jnp.concatenate([cos_t.reshape(peaks_n, width, chips, span), -sin_t.reshape(peaks_n, width, chips, span)], axis=3)
    row_table = jnp.swapaxes(row_table, 1, 2)
    args = [flags, tas, tbs, rids, offs, tmpl_a, tmpl_b, spec, col_table, row_table]
    part_spec = pl.BlockSpec((peaks_n, per, width, width), lambda j, i, f, ta, tb, r, o: (0, j, 0, 0))
    if final:
        in_specs.append(part_spec)
        args.append(init)
        out_shape = jax.ShapeDtypeStruct((2, peaks_n, width, width), jnp.float32)
        out_specs = pl.BlockSpec((2, peaks_n, width, width), lambda j, i, f, ta, tb, r, o: (0, 0, 0, 0))
    else:
        out_shape = jax.ShapeDtypeStruct((peaks_n, blocks, width, width), jnp.float32)
        out_specs = part_spec
    return pl.pallas_call(
        kernel,
        grid_spec=pltpu.PrefetchScalarGridSpec(
            num_scalar_prefetch=5,
            grid=(blocks // per, n_steps),
            in_specs=in_specs,
            out_specs=out_specs,
            scratch_shapes=[pltpu.VMEM((peaks_n, per, width, width), jnp.float32), pltpu.VMEM((per * span, 2 * size), jnp.bfloat16)],
        ),
        out_shape=out_shape,
        compiler_params=pltpu.CompilerParams(dimension_semantics=("arbitrary", "arbitrary")),
        cost_estimate=cost,
    )(*args)


def local(tile_spectra, template_spectra, peaks, listed):
    size = tile_spectra.shape[3]
    width = W
    tiles = lax.axis_size("tile")
    rows_t = template_spectra.shape[2]
    tmpl = lax.all_gather(template_spectra, "tile", axis=0)
    block_size = tmpl.shape[1]
    spec = gather_rows(tile_spectra[0], "orient")
    spec = jnp.moveaxis(spec, 0, 1).reshape(2, size, size)
    freqs = jnp.arange(size, dtype=jnp.int32)
    cos_row, sin_row = angle_tables(freqs, peaks[0][:, 0], size, width)
    cos_t = jnp.swapaxes(cos_row, 1, 2)
    sin_t = jnp.swapaxes(sin_row, 1, 2)
    col_table = col_tables(peaks[0], size, width)
    listed_ids = listed[0]
    global_ids = lax.axis_index("orient") * block_size + jnp.arange(block_size, dtype=jnp.int32)
    is_listed = jnp.any(listed_ids[:, :, None] == global_ids[None, None, :], axis=1)
    flags = is_listed.astype(jnp.int32).reshape(-1)
    best_shape = (listed.shape[1], width, width)
    if rows_t % 128 != 0 or tiles % 2 != 0 or block_size % 2 != 0:
        best_part, power_part = match(flags, tmpl, spec, col_table, cos_t, sin_t)
    else:
        me = lax.axis_index("tile")
        sibling = lax.ppermute(template_spectra, "tile", xor_pairs(tiles, 1))
        spec32 = spec.astype(jnp.float32)
        chip = me // 2
        odd = (me % 2).astype(jnp.int32)
        zero = jnp.zeros((1,), jnp.int32)
        near_offs = jnp.stack([odd, 1 - odd]) * rows_t
        own, sib = template_spectra[None], sibling[None]
        partial = match_rows(flags, zero, zero, chip[None].astype(jnp.int32), near_offs, own, sib, spec32, col_table, cos_t, sin_t)
        far = far_chips(chip, tiles // 2)
        far_offs = jnp.array([0, rows_t], jnp.int32)
        joined = match_rows(flags, far * 2, far * 2 + 1, far, far_offs, tmpl, tmpl, spec32, col_table, cos_t, sin_t, init=partial)
        best_all, power_all = reduce_joined(joined.reshape(2, -1, width), best_shape, "orient")
        return (best_all[None], (power_all / LIST)[None])
    best_all, power_all = reduce_orient(best_part, power_part, "orient")
    return (best_all[None], (power_all / LIST)[None])


def far_chips(chip, chips):
    steps = jnp.arange(chips - 1, dtype=jnp.int32)
    return steps + (steps >= chip).astype(jnp.int32)


def solution(mesh):
    placed = (
        P("tile", None, "orient", None),
        P("orient", None, "tile", None),
        P("tile", None, None),
        P("tile", None, None),
    )
    return jax.shard_map(
        local,
        mesh=mesh,
        in_specs=placed,
        out_specs=(P("tile", None, None, None), P("tile", None, None, None)),
        check_vma=False,
    )
```

```python
import functools
import math

import jax
import jax.numpy as jnp
from jax import lax
from jax.experimental import pallas as pl
from jax.experimental.pallas import tpu as pltpu
from jax.sharding import PartitionSpec as P

W = 128
LIST = 48


lowest_score = -1e30


def xor_pairs(n, k):
    return [(i, i ^ k) for i in range(n)]


def is_pow2(n):
    return n & (n - 1) == 0


def angle_tables(freqs, coords, size, width):
    offsets = jnp.arange(width, dtype=jnp.int32) - width // 2
    position = (coords[:, None] + offsets[None, :]) % size
    phase = freqs[None, :, None] * position[:, None, :] % size
    angle = phase.astype(jnp.float32) * (2.0 * math.pi / size)
    return (jnp.cos(angle).astype(jnp.bfloat16), jnp.sin(angle).astype(jnp.bfloat16))


def col_tables(peak_rows, size, width):
    freqs = jnp.arange(size, dtype=jnp.int32)
    cos_col, sin_col = angle_tables(freqs, peak_rows[:, 1], size, width)
    upper = jnp.concatenate([cos_col, sin_col], axis=-1)
    lower = jnp.concatenate([-sin_col, cos_col], axis=-1)
    return jnp.concatenate([upper, lower], axis=1)


def gather_rows(part, axis):
    n = lax.axis_size(axis)
    if not is_pow2(n):
        return lax.all_gather(part, axis)
    me = lax.axis_index(axis)
    blocks = part[None]
    k = n // 2
    while k >= 1:
        got = lax.ppermute(blocks, axis, xor_pairs(n, k))
        blocks = jnp.concatenate([blocks, got])
        k //= 2
    want = jnp.arange(n, dtype=jnp.int32) ^ me
    return blocks[order_of(want, n)]


def order_of(want, count):
    steps = int(math.log2(count))
    slot = jnp.zeros_like(want)
    for j in range(steps):
        k = count >> (j + 1)
        hit = (want & k) != 0
        slot = slot | jnp.where(hit, 1 << j, 0)
    return slot


def reduce_orient(best_part, power_part, axis):
    n = lax.axis_size(axis)
    if not is_pow2(n):
        best = lax.pmax(best_part, axis)
        power = lax.psum(power_part, axis)
        return best, power
    width = best_part.shape[-1]
    joined = jnp.stack([best_part.reshape(-1, width), power_part.reshape(-1, width)], axis=0)
    return reduce_joined(joined, best_part.shape, axis)


def reduce_joined(joined, shape, axis):
    n = lax.axis_size(axis)
    rows = joined.shape[1]
    if not is_pow2(n) or rows % n != 0:
        best = lax.pmax(joined[0], axis)
        power = lax.psum(joined[1], axis)
        return best.reshape(shape), power.reshape(shape)
    me = lax.axis_index(axis)
    piece = rows // n
    own = lax.dynamic_slice_in_dim(joined, me * piece, piece, axis=1)
    bests, powers = [own[0]], [own[1]]
    for k in range(1, n):
        send = lax.dynamic_slice_in_dim(joined, (me ^ k) * piece, piece, axis=1)
        got = lax.ppermute(send, axis, xor_pairs(n, k))
        bests.append(got[0])
        powers.append(got[1])
    best = bests[0]
    power = powers[0]
    for b, p in zip(bests[1:], powers[1:]):
        best = jnp.maximum(best, b)
        power = power + p
    done = jnp.stack([best, power])
    slots = [done] + [lax.ppermute(done, axis, xor_pairs(n, k)) for k in range(1, n)]
    pieces = jnp.stack(slots)[jnp.arange(n, dtype=jnp.int32) ^ me]
    whole = jnp.moveaxis(pieces, 0, 1).reshape(2, rows, joined.shape[2])
    return whole[0].reshape(shape), whole[1].reshape(shape)


def match_kernel(blocks, size, width, rows_t, tiles, peaks_n, l_ref, tm_ref, sp_ref, ct_ref, cr_ref, sr_ref, best_ref, pow_ref, m_ref):
    j = pl.program_id(0)

    @pl.when(j == 0)
    def _():
        best_ref[...] = jnp.full(best_ref.shape, lowest_score, jnp.float32)
        pow_ref[...] = jnp.zeros(pow_ref.shape, jnp.float32)

    for t in range(tiles):
        rows = pl.ds(t * rows_t, rows_t)
        image_re = sp_ref[0, rows, :].astype(jnp.float32)
        image_im = sp_ref[1, rows, :].astype(jnp.float32)
        tmpl_re = tm_ref[t, 0, 0].astype(jnp.float32)
        tmpl_im = tm_ref[t, 0, 1].astype(jnp.float32)
        m_ref[rows, pl.ds(0, size)] = (image_re * tmpl_re + image_im * tmpl_im).astype(jnp.bfloat16)
        m_ref[rows, pl.ds(size, size)] = (image_im * tmpl_re - image_re * tmpl_im).astype(jnp.bfloat16)

    for p in range(peaks_n):
        @pl.when(l_ref[p * blocks + j] > 0)
        def _():
            g = jnp.dot(m_ref[...], ct_ref[p], preferred_element_type=jnp.float32).astype(jnp.bfloat16)
            score = jnp.dot(cr_ref[p], g[:, :width], preferred_element_type=jnp.float32)
            score = score - jnp.dot(sr_ref[p], g[:, width:], preferred_element_type=jnp.float32)
            score = score / size
            best_ref[p] = jnp.maximum(best_ref[p], score)
            pow_ref[p] = pow_ref[p] + score * score


def match(flags, tmpl, spec, col_table, cos_t, sin_t):
    tiles, blocks, _, rows_t, size = tmpl.shape
    peaks_n, width = cos_t.shape[0], cos_t.shape[1]
    kernel = functools.partial(match_kernel, blocks, size, width, rows_t, tiles, peaks_n)
    flops = blocks * peaks_n * (2 * size * 2 * size * 2 * width + 2 * 2 * width * size * width)
    cost = pl.CostEstimate(flops=flops, transcendentals=0, bytes_accessed=tmpl.size * 2 + spec.size * 2 + col_table.size * 2)
    out = jax.ShapeDtypeStruct((peaks_n, width, width), jnp.float32)
    return pl.pallas_call(
        kernel,
        grid_spec=pltpu.PrefetchScalarGridSpec(
            num_scalar_prefetch=1,
            grid=(blocks,),
            in_specs=[
                pl.BlockSpec((tiles, 1, 2, rows_t, size), lambda j, l: (0, j, 0, 0, 0)),
                pl.BlockSpec((2, size, size), lambda j, l: (0, 0, 0)),
                pl.BlockSpec(col_table.shape, lambda j, l: (0, 0, 0)),
                pl.BlockSpec(cos_t.shape, lambda j, l: (0, 0, 0)),
                pl.BlockSpec(sin_t.shape, lambda j, l: (0, 0, 0)),
            ],
            out_specs=[
                pl.BlockSpec((peaks_n, width, width), lambda j, l: (0, 0, 0)),
                pl.BlockSpec((peaks_n, width, width), lambda j, l: (0, 0, 0)),
            ],
            scratch_shapes=[pltpu.VMEM((size, 2 * size), jnp.bfloat16)],
        ),
        out_shape=[out, out],
        compiler_params=pltpu.CompilerParams(dimension_semantics=("arbitrary",)),
        cost_estimate=cost,
    )(flags, tmpl, spec, col_table, cos_t, sin_t)


def rows_kernel(blocks, size, width, rows_t, peaks_n, chunk, n_steps, final, per, f_ref, ta_ref, tb_ref, rid_ref, off_ref, tma_ref, tmb_ref, sp_ref, ct_ref, cr_ref, *rest):
    if final:
        init_ref, out_ref, acc_ref, m_ref = rest
        best_ref, pow_ref = out_ref.at[0], out_ref.at[1]
    else:
        part_ref, acc_ref, m_ref = rest
    jj = pl.program_id(0)
    i = pl.program_id(1)
    span = 2 * rows_t

    if final:
        @pl.when((jj == 0) & (i == 0))
        def _():
            best_ref[...] = jnp.full(best_ref.shape, lowest_score, jnp.float32)
            pow_ref[...] = jnp.zeros(pow_ref.shape, jnp.float32)

        @pl.when(i == 0)
        def _():
            acc_ref[...] = init_ref[...]
    else:
        @pl.when(i == 0)
        def _():
            acc_ref[...] = jnp.zeros(acc_ref.shape, jnp.float32)

    for o in range(per):
        for u, tm_ref in enumerate((tma_ref, tmb_ref)):
            def mix(c, carry, u=u, o=o, tm_ref=tm_ref):
                row = pl.multiple_of(c * chunk, chunk)
                in_row = pl.multiple_of(off_ref[u] + c * chunk, chunk)
                out_row = pl.multiple_of(o * span + off_ref[u] + c * chunk, chunk)
                image_re = sp_ref[0, pl.ds(in_row, chunk), :]
                image_im = sp_ref[1, pl.ds(in_row, chunk), :]
                tmpl_re = tm_ref[0, o, 0, pl.ds(row, chunk), :].astype(jnp.float32)
                tmpl_im = tm_ref[0, o, 1, pl.ds(row, chunk), :].astype(jnp.float32)
                m_ref[pl.ds(out_row, chunk), pl.ds(0, size)] = (image_re * tmpl_re + image_im * tmpl_im).astype(jnp.bfloat16)
                m_ref[pl.ds(out_row, chunk), pl.ds(size, size)] = (image_im * tmpl_re - image_re * tmpl_im).astype(jnp.bfloat16)
                return carry

            lax.fori_loop(0, rows_t // chunk, mix, 0, unroll=4)

    for p in range(peaks_n):
        count = f_ref[p * blocks + per * jj]
        for o in range(1, per):
            count = count + f_ref[p * blocks + per * jj + o]

        @pl.when(count > 0)
        def _():
            g = jnp.dot(m_ref[...], ct_ref[p], preferred_element_type=jnp.float32).astype(jnp.bfloat16)
            for o in range(per):
                rows = slice(o * span, (o + 1) * span)
                stacked = jnp.concatenate([g[rows, :width], g[rows, width:]], axis=0)
                part = jnp.dot(cr_ref[p, 0], stacked, preferred_element_type=jnp.float32)
                acc_ref[p, o] = acc_ref[p, o] + part

    @pl.when(i == n_steps - 1)
    def _():
        if final:
            for p in range(peaks_n):
                for o in range(per):
                    @pl.when(f_ref[p * blocks + per * jj + o] > 0)
                    def _():
                        score = acc_ref[p, o] / size
                        best_ref[p] = jnp.maximum(best_ref[p], score)
                        pow_ref[p] = pow_ref[p] + score * score
        else:
            part_ref[...] = acc_ref[...]


def match_rows(flags, tas, tbs, rids, offs, tmpl_a, tmpl_b, spec, col_table, cos_t, sin_t, init=None):
    _, blocks, _, rows_t, size = tmpl_a.shape
    peaks_n, width = cos_t.shape[0], cos_t.shape[1]
    n_steps = tas.shape[0]
    final = init is not None
    chunk = math.gcd(rows_t, 16)
    span = 2 * rows_t
    per = 4 if blocks % 4 == 0 else 2
    kernel = functools.partial(rows_kernel, blocks, size, width, rows_t, peaks_n, chunk, n_steps, final, per)
    flops = blocks * peaks_n * n_steps * (2 * span * 2 * size * 2 * width + 2 * 2 * width * span * width)
    cost = pl.CostEstimate(flops=flops, transcendentals=0, bytes_accessed=n_steps * blocks * 2 * span * size * 6 + col_table.size * 2)
    in_specs = [
        pl.BlockSpec((1, per, 2, rows_t, size), lambda j, i, f, ta, tb, r, o: (ta[i], j, 0, 0, 0)),
        pl.BlockSpec((1, per, 2, rows_t, size), lambda j, i, f, ta, tb, r, o: (tb[i], j, 0, 0, 0)),
        pl.BlockSpec((2, span, size), lambda j, i, f, ta, tb, r, o: (0, r[i], 0)),
        pl.BlockSpec(col_table.shape, lambda j, i, f, ta, tb, r, o: (0, 0, 0)),
        pl.BlockSpec((peaks_n, 1, width, 2 * span), lambda j, i, f, ta, tb, r, o: (0, r[i], 0, 0)),
    ]
    chips = cos_t.shape[2] // span
    row_table = jnp.concatenate([cos_t.reshape(peaks_n, width, chips, span), -sin_t.reshape(peaks_n, width, chips, span)], axis=3)
    row_table = jnp.swapaxes(row_table, 1, 2)
    args = [flags, tas, tbs, rids, offs, tmpl_a, tmpl_b, spec, col_table, row_table]
    part_spec = pl.BlockSpec((peaks_n, per, width, width), lambda j, i, f, ta, tb, r, o: (0, j, 0, 0))
    if final:
        in_specs.append(part_spec)
        args.append(init)
        out_shape = jax.ShapeDtypeStruct((2, peaks_n, width, width), jnp.float32)
        out_specs = pl.BlockSpec((2, peaks_n, width, width), lambda j, i, f, ta, tb, r, o: (0, 0, 0, 0))
    else:
        out_shape = jax.ShapeDtypeStruct((peaks_n, blocks, width, width), jnp.float32)
        out_specs = part_spec
    return pl.pallas_call(
        kernel,
        grid_spec=pltpu.PrefetchScalarGridSpec(
            num_scalar_prefetch=5,
            grid=(blocks // per, n_steps),
            in_specs=in_specs,
            out_specs=out_specs,
            scratch_shapes=[pltpu.VMEM((peaks_n, per, width, width), jnp.float32), pltpu.VMEM((per * span, 2 * size), jnp.bfloat16)],
        ),
        out_shape=out_shape,
        compiler_params=pltpu.CompilerParams(dimension_semantics=("arbitrary", "arbitrary")),
        cost_estimate=cost,
    )(*args)


def local(tile_spectra, template_spectra, peaks, listed):
    size = tile_spectra.shape[3]
    width = W
    tiles = lax.axis_size("tile")
    rows_t = template_spectra.shape[2]
    block_size = template_spectra.shape[0]
    freqs = jnp.arange(size, dtype=jnp.int32)
    cos_row, sin_row = angle_tables(freqs, peaks[0][:, 0], size, width)
    cos_t = jnp.swapaxes(cos_row, 1, 2)
    sin_t = jnp.swapaxes(sin_row, 1, 2)
    col_table = col_tables(peaks[0], size, width)
    listed_ids = listed[0]
    global_ids = lax.axis_index("orient") * block_size + jnp.arange(block_size, dtype=jnp.int32)
    is_listed = jnp.any(listed_ids[:, :, None] == global_ids[None, None, :], axis=1)
    flags = is_listed.astype(jnp.int32).reshape(-1)
    best_shape = (listed.shape[1], width, width)
    if rows_t % 128 != 0 or tiles != 4 or block_size % 4 != 0:
        tmpl = lax.all_gather(template_spectra, "tile", axis=0)
        spec = gather_rows(tile_spectra[0], "orient")
        spec = jnp.moveaxis(spec, 0, 1).reshape(2, size, size)
        best_part, power_part = match(flags, tmpl, spec, col_table, cos_t, sin_t)
        best_all, power_all = reduce_orient(best_part, power_part, "orient")
        return (best_all[None], (power_all / LIST)[None])
    me = lax.axis_index("tile")
    spec = lax.all_gather(tile_spectra, "orient", axis=2, tiled=True)[0]
    spec32 = spec.astype(jnp.float32)
    sibling = lax.ppermute(template_spectra, "tile", xor_pairs(tiles, 1))
    far_own = lax.ppermute(template_spectra, "tile", xor_pairs(tiles, 2))
    far_sib = lax.ppermute(far_own, "tile", xor_pairs(tiles, 1))
    chip = (me // 2).astype(jnp.int32)
    odd = (me % 2).astype(jnp.int32)
    zero = jnp.zeros((1,), jnp.int32)
    offs = jnp.stack([odd, 1 - odd]) * rows_t
    partial = match_rows(flags, zero, zero, chip[None], offs, template_spectra[None], sibling[None], spec32, col_table, cos_t, sin_t)
    joined = match_rows(flags, zero, zero, (1 - chip)[None], offs, far_own[None], far_sib[None], spec32, col_table, cos_t, sin_t, init=partial)
    best_all, power_all = reduce_joined(joined.reshape(2, -1, width), best_shape, "orient")
    return (best_all[None], (power_all / LIST)[None])


def far_chips(chip, chips):
    steps = jnp.arange(chips - 1, dtype=jnp.int32)
    return steps + (steps >= chip).astype(jnp.int32)


def solution(mesh):
    placed = (
        P("tile", None, "orient", None),
        P("orient", None, "tile", None),
        P("tile", None, None),
        P("tile", None, None),
    )
    return jax.shard_map(
        local,
        mesh=mesh,
        in_specs=placed,
        out_specs=(P("tile", None, None, None), P("tile", None, None, None)),
        check_vma=False,
    )
```

```python
import functools
import math

import jax
import jax.numpy as jnp
from jax import lax
from jax.experimental import pallas as pl
from jax.experimental.pallas import tpu as pltpu
from jax.sharding import PartitionSpec as P

W = 128
LIST = 48


lowest_score = -1e30


def xor_pairs(n, k):
    return [(i, i ^ k) for i in range(n)]


def is_pow2(n):
    return n & (n - 1) == 0


def angle_tables(freqs, coords, size, width):
    offsets = jnp.arange(width, dtype=jnp.int32) - width // 2
    position = (coords[:, None] + offsets[None, :]) % size
    phase = freqs[None, :, None] * position[:, None, :] % size
    angle = phase.astype(jnp.float32) * (2.0 * math.pi / size)
    return (jnp.cos(angle).astype(jnp.bfloat16), jnp.sin(angle).astype(jnp.bfloat16))


def col_tables(peak_rows, size, width):
    freqs = jnp.arange(size, dtype=jnp.int32)
    cos_col, sin_col = angle_tables(freqs, peak_rows[:, 1], size, width)
    upper = jnp.concatenate([cos_col, sin_col], axis=-1)
    lower = jnp.concatenate([-sin_col, cos_col], axis=-1)
    return jnp.concatenate([upper, lower], axis=1)


def gather_rows(part, axis):
    n = lax.axis_size(axis)
    if not is_pow2(n):
        return lax.all_gather(part, axis)
    me = lax.axis_index(axis)
    blocks = part[None]
    k = n // 2
    while k >= 1:
        got = lax.ppermute(blocks, axis, xor_pairs(n, k))
        blocks = jnp.concatenate([blocks, got])
        k //= 2
    want = jnp.arange(n, dtype=jnp.int32) ^ me
    return blocks[order_of(want, n)]


def order_of(want, count):
    steps = int(math.log2(count))
    slot = jnp.zeros_like(want)
    for j in range(steps):
        k = count >> (j + 1)
        hit = (want & k) != 0
        slot = slot | jnp.where(hit, 1 << j, 0)
    return slot


def reduce_orient(best_part, power_part, axis):
    n = lax.axis_size(axis)
    if not is_pow2(n):
        best = lax.pmax(best_part, axis)
        power = lax.psum(power_part, axis)
        return best, power
    width = best_part.shape[-1]
    joined = jnp.stack([best_part.reshape(-1, width), power_part.reshape(-1, width)], axis=0)
    return reduce_joined(joined, best_part.shape, axis)


def reduce_joined(joined, shape, axis):
    n = lax.axis_size(axis)
    rows = joined.shape[1]
    if not is_pow2(n) or n < 2 or rows % n != 0:
        best = lax.pmax(joined[0], axis)
        power = lax.psum(joined[1], axis)
        return best.reshape(shape), power.reshape(shape)
    me = lax.axis_index(axis)
    half = rows // 2
    bit = me % 2
    keep = lax.dynamic_slice_in_dim(joined, bit * half, half, axis=1)
    send = lax.dynamic_slice_in_dim(joined, (1 - bit) * half, half, axis=1)
    got = lax.ppermute(send, axis, xor_pairs(n, 1))
    cur = jnp.stack([jnp.maximum(keep[0], got[0]), keep[1] + got[1]])
    members = n // 2
    group = me // 2
    piece = half // members
    own = lax.dynamic_slice_in_dim(cur, group * piece, piece, axis=1)
    best, power = own[0], own[1]
    for m in range(1, members):
        out = lax.dynamic_slice_in_dim(cur, (group ^ m) * piece, piece, axis=1)
        got = lax.ppermute(out, axis, xor_pairs(n, 2 * m))
        best = jnp.maximum(best, got[0])
        power = power + got[1]
    done = jnp.stack([best, power])
    slots = [done] + [lax.ppermute(done, axis, xor_pairs(n, 2 * m)) for m in range(1, members)]
    pieces = jnp.stack(slots)[jnp.arange(members, dtype=jnp.int32) ^ group]
    mine = jnp.moveaxis(pieces, 0, 1).reshape(2, half, joined.shape[2])
    other = lax.ppermute(mine, axis, xor_pairs(n, 1))
    whole = jnp.where(bit == 1, jnp.concatenate([other, mine], axis=1), jnp.concatenate([mine, other], axis=1))
    return whole[0].reshape(shape), whole[1].reshape(shape)


def match_kernel(blocks, size, width, rows_t, tiles, peaks_n, l_ref, tm_ref, sp_ref, ct_ref, cr_ref, sr_ref, best_ref, pow_ref, m_ref):
    j = pl.program_id(0)

    @pl.when(j == 0)
    def _():
        best_ref[...] = jnp.full(best_ref.shape, lowest_score, jnp.float32)
        pow_ref[...] = jnp.zeros(pow_ref.shape, jnp.float32)

    for t in range(tiles):
        rows = pl.ds(t * rows_t, rows_t)
        image_re = sp_ref[0, rows, :].astype(jnp.float32)
        image_im = sp_ref[1, rows, :].astype(jnp.float32)
        tmpl_re = tm_ref[t, 0, 0].astype(jnp.float32)
        tmpl_im = tm_ref[t, 0, 1].astype(jnp.float32)
        m_ref[rows, pl.ds(0, size)] = (image_re * tmpl_re + image_im * tmpl_im).astype(jnp.bfloat16)
        m_ref[rows, pl.ds(size, size)] = (image_im * tmpl_re - image_re * tmpl_im).astype(jnp.bfloat16)

    for p in range(peaks_n):
        @pl.when(l_ref[p * blocks + j] > 0)
        def _():
            g = jnp.dot(m_ref[...], ct_ref[p], preferred_element_type=jnp.float32).astype(jnp.bfloat16)
            score = jnp.dot(cr_ref[p], g[:, :width], preferred_element_type=jnp.float32)
            score = score - jnp.dot(sr_ref[p], g[:, width:], preferred_element_type=jnp.float32)
            score = score / size
            best_ref[p] = jnp.maximum(best_ref[p], score)
            pow_ref[p] = pow_ref[p] + score * score


def match(flags, tmpl, spec, col_table, cos_t, sin_t):
    tiles, blocks, _, rows_t, size = tmpl.shape
    peaks_n, width = cos_t.shape[0], cos_t.shape[1]
    kernel = functools.partial(match_kernel, blocks, size, width, rows_t, tiles, peaks_n)
    flops = blocks * peaks_n * (2 * size * 2 * size * 2 * width + 2 * 2 * width * size * width)
    cost = pl.CostEstimate(flops=flops, transcendentals=0, bytes_accessed=tmpl.size * 2 + spec.size * 2 + col_table.size * 2)
    out = jax.ShapeDtypeStruct((peaks_n, width, width), jnp.float32)
    return pl.pallas_call(
        kernel,
        grid_spec=pltpu.PrefetchScalarGridSpec(
            num_scalar_prefetch=1,
            grid=(blocks,),
            in_specs=[
                pl.BlockSpec((tiles, 1, 2, rows_t, size), lambda j, l: (0, j, 0, 0, 0)),
                pl.BlockSpec((2, size, size), lambda j, l: (0, 0, 0)),
                pl.BlockSpec(col_table.shape, lambda j, l: (0, 0, 0)),
                pl.BlockSpec(cos_t.shape, lambda j, l: (0, 0, 0)),
                pl.BlockSpec(sin_t.shape, lambda j, l: (0, 0, 0)),
            ],
            out_specs=[
                pl.BlockSpec((peaks_n, width, width), lambda j, l: (0, 0, 0)),
                pl.BlockSpec((peaks_n, width, width), lambda j, l: (0, 0, 0)),
            ],
            scratch_shapes=[pltpu.VMEM((size, 2 * size), jnp.bfloat16)],
        ),
        out_shape=[out, out],
        compiler_params=pltpu.CompilerParams(dimension_semantics=("arbitrary",)),
        cost_estimate=cost,
    )(flags, tmpl, spec, col_table, cos_t, sin_t)


def rows_kernel(blocks, size, width, rows_t, peaks_n, chunk, n_steps, final, per, f_ref, ta_ref, tb_ref, rid_ref, off_ref, tma_ref, tmb_ref, sp_ref, ct_ref, cr_ref, sr_ref, *rest):
    if final:
        init_ref, out_ref, acc_ref, m_ref = rest
        best_ref, pow_ref = out_ref.at[0], out_ref.at[1]
    else:
        part_ref, acc_ref, m_ref = rest
    jj = pl.program_id(0)
    i = pl.program_id(1)
    span = 2 * rows_t

    if final:
        @pl.when((jj == 0) & (i == 0))
        def _():
            best_ref[...] = jnp.full(best_ref.shape, lowest_score, jnp.float32)
            pow_ref[...] = jnp.zeros(pow_ref.shape, jnp.float32)

        @pl.when(i == 0)
        def _():
            acc_ref[...] = init_ref[...]
    else:
        @pl.when(i == 0)
        def _():
            acc_ref[...] = jnp.zeros(acc_ref.shape, jnp.float32)

    for o in range(per):
        for u, tm_ref in enumerate((tma_ref, tmb_ref)):
            def mix(c, carry, u=u, o=o, tm_ref=tm_ref):
                row = pl.multiple_of(c * chunk, chunk)
                in_row = pl.multiple_of(off_ref[u] + c * chunk, chunk)
                out_row = pl.multiple_of(o * span + off_ref[u] + c * chunk, chunk)
                image_re = sp_ref[0, pl.ds(in_row, chunk), :]
                image_im = sp_ref[1, pl.ds(in_row, chunk), :]
                tmpl_re = tm_ref[0, o, 0, pl.ds(row, chunk), :].astype(jnp.float32)
                tmpl_im = tm_ref[0, o, 1, pl.ds(row, chunk), :].astype(jnp.float32)
                m_ref[pl.ds(out_row, chunk), pl.ds(0, size)] = (image_re * tmpl_re + image_im * tmpl_im).astype(jnp.bfloat16)
                m_ref[pl.ds(out_row, chunk), pl.ds(size, size)] = (image_im * tmpl_re - image_re * tmpl_im).astype(jnp.bfloat16)
                return carry

            lax.fori_loop(0, rows_t // chunk, mix, 0, unroll=4)

    for p in range(peaks_n):
        count = f_ref[p * blocks + per * jj]
        for o in range(1, per):
            count = count + f_ref[p * blocks + per * jj + o]

        @pl.when(count > 0)
        def _():
            g = jnp.dot(m_ref[...], ct_ref[p], preferred_element_type=jnp.float32).astype(jnp.bfloat16)
            for o in range(per):
                rows = slice(o * span, (o + 1) * span)
                part = jnp.dot(cr_ref[p], g[rows, :width], preferred_element_type=jnp.float32)
                part = part - jnp.dot(sr_ref[p], g[rows, width:], preferred_element_type=jnp.float32)
                acc_ref[p, o] = acc_ref[p, o] + part

    @pl.when(i == n_steps - 1)
    def _():
        if final:
            for p in range(peaks_n):
                for o in range(per):
                    @pl.when(f_ref[p * blocks + per * jj + o] > 0)
                    def _():
                        score = acc_ref[p, o] / size
                        best_ref[p] = jnp.maximum(best_ref[p], score)
                        pow_ref[p] = pow_ref[p] + score * score
        else:
            part_ref[...] = acc_ref[...]


def match_rows(flags, tas, tbs, rids, offs, tmpl_a, tmpl_b, spec, col_table, cos_t, sin_t, init=None):
    _, blocks, _, rows_t, size = tmpl_a.shape
    peaks_n, width = cos_t.shape[0], cos_t.shape[1]
    n_steps = tas.shape[0]
    final = init is not None
    chunk = math.gcd(rows_t, 16)
    span = 2 * rows_t
    per = 4 if blocks % 4 == 0 else 2
    kernel = functools.partial(rows_kernel, blocks, size, width, rows_t, peaks_n, chunk, n_steps, final, per)
    flops = blocks * peaks_n * n_steps * (2 * span * 2 * size * 2 * width + 2 * 2 * width * span * width)
    cost = pl.CostEstimate(flops=flops, transcendentals=0, bytes_accessed=n_steps * blocks * 2 * span * size * 6 + col_table.size * 2)
    in_specs = [
        pl.BlockSpec((1, per, 2, rows_t, size), lambda j, i, f, ta, tb, r, o: (ta[i], j, 0, 0, 0)),
        pl.BlockSpec((1, per, 2, rows_t, size), lambda j, i, f, ta, tb, r, o: (tb[i], j, 0, 0, 0)),
        pl.BlockSpec((2, span, size), lambda j, i, f, ta, tb, r, o: (0, r[i], 0)),
        pl.BlockSpec(col_table.shape, lambda j, i, f, ta, tb, r, o: (0, 0, 0)),
        pl.BlockSpec((peaks_n, width, span), lambda j, i, f, ta, tb, r, o: (0, 0, r[i])),
        pl.BlockSpec((peaks_n, width, span), lambda j, i, f, ta, tb, r, o: (0, 0, r[i])),
    ]
    args = [flags, tas, tbs, rids, offs, tmpl_a, tmpl_b, spec, col_table, cos_t, sin_t]
    part_spec = pl.BlockSpec((peaks_n, per, width, width), lambda j, i, f, ta, tb, r, o: (0, j, 0, 0))
    if final:
        in_specs.append(part_spec)
        args.append(init)
        out_shape = jax.ShapeDtypeStruct((2, peaks_n, width, width), jnp.float32)
        out_specs = pl.BlockSpec((2, peaks_n, width, width), lambda j, i, f, ta, tb, r, o: (0, 0, 0, 0))
    else:
        out_shape = jax.ShapeDtypeStruct((peaks_n, blocks, width, width), jnp.float32)
        out_specs = part_spec
    return pl.pallas_call(
        kernel,
        grid_spec=pltpu.PrefetchScalarGridSpec(
            num_scalar_prefetch=5,
            grid=(blocks // per, n_steps),
            in_specs=in_specs,
            out_specs=out_specs,
            scratch_shapes=[pltpu.VMEM((peaks_n, per, width, width), jnp.float32), pltpu.VMEM((per * span, 2 * size), jnp.bfloat16)],
        ),
        out_shape=out_shape,
        compiler_params=pltpu.CompilerParams(dimension_semantics=("arbitrary", "arbitrary")),
        cost_estimate=cost,
    )(*args)


def local(tile_spectra, template_spectra, peaks, listed):
    size = tile_spectra.shape[3]
    width = W
    tiles = lax.axis_size("tile")
    rows_t = template_spectra.shape[2]
    tmpl = lax.all_gather(template_spectra, "tile", axis=0)
    block_size = tmpl.shape[1]
    spec = gather_rows(tile_spectra[0], "orient")
    spec = jnp.moveaxis(spec, 0, 1).reshape(2, size, size)
    freqs = jnp.arange(size, dtype=jnp.int32)
    cos_row, sin_row = angle_tables(freqs, peaks[0][:, 0], size, width)
    cos_t = jnp.swapaxes(cos_row, 1, 2)
    sin_t = jnp.swapaxes(sin_row, 1, 2)
    col_table = col_tables(peaks[0], size, width)
    listed_ids = listed[0]
    global_ids = lax.axis_index("orient") * block_size + jnp.arange(block_size, dtype=jnp.int32)
    is_listed = jnp.any(listed_ids[:, :, None] == global_ids[None, None, :], axis=1)
    flags = is_listed.astype(jnp.int32).reshape(-1)
    best_shape = (listed.shape[1], width, width)
    if rows_t % 128 != 0 or tiles % 2 != 0 or block_size % 2 != 0:
        best_part, power_part = match(flags, tmpl, spec, col_table, cos_t, sin_t)
    else:
        me = lax.axis_index("tile")
        sibling = lax.ppermute(template_spectra, "tile", xor_pairs(tiles, 1))
        spec32 = spec.astype(jnp.float32)
        chip = me // 2
        odd = (me % 2).astype(jnp.int32)
        zero = jnp.zeros((1,), jnp.int32)
        near_offs = jnp.stack([odd, 1 - odd]) * rows_t
        own, sib = template_spectra[None], sibling[None]
        partial = match_rows(flags, zero, zero, chip[None].astype(jnp.int32), near_offs, own, sib, spec32, col_table, cos_t, sin_t)
        far = far_chips(chip, tiles // 2)
        far_offs = jnp.array([0, rows_t], jnp.int32)
        joined = match_rows(flags, far * 2, far * 2 + 1, far, far_offs, tmpl, tmpl, spec32, col_table, cos_t, sin_t, init=partial)
        best_all, power_all = reduce_joined(joined.reshape(2, -1, width), best_shape, "orient")
        return (best_all[None], (power_all / LIST)[None])
    best_all, power_all = reduce_orient(best_part, power_part, "orient")
    return (best_all[None], (power_all / LIST)[None])


def far_chips(chip, chips):
    steps = jnp.arange(chips - 1, dtype=jnp.int32)
    return steps + (steps >= chip).astype(jnp.int32)


def solution(mesh):
    placed = (
        P("tile", None, "orient", None),
        P("orient", None, "tile", None),
        P("tile", None, None),
        P("tile", None, None),
    )
    return jax.shard_map(
        local,
        mesh=mesh,
        in_specs=placed,
        out_specs=(P("tile", None, None, None), P("tile", None, None, None)),
        check_vma=False,
    )
```

```python
import functools
import math

import jax
import jax.numpy as jnp
from jax import lax
from jax.experimental import pallas as pl
from jax.experimental.pallas import tpu as pltpu
from jax.sharding import PartitionSpec as P

W = 128
LIST = 48


lowest_score = -1e30


def xor_pairs(n, k):
    return [(i, i ^ k) for i in range(n)]


def is_pow2(n):
    return n & (n - 1) == 0


def angle_tables(freqs, coords, size, width):
    offsets = jnp.arange(width, dtype=jnp.int32) - width // 2
    position = (coords[:, None] + offsets[None, :]) % size
    phase = freqs[None, :, None] * position[:, None, :] % size
    angle = phase.astype(jnp.float32) * (2.0 * math.pi / size)
    return (jnp.cos(angle).astype(jnp.bfloat16), jnp.sin(angle).astype(jnp.bfloat16))


def col_tables(peak_rows, size, width):
    freqs = jnp.arange(size, dtype=jnp.int32)
    cos_col, sin_col = angle_tables(freqs, peak_rows[:, 1], size, width)
    upper = jnp.concatenate([cos_col, sin_col], axis=-1)
    lower = jnp.concatenate([-sin_col, cos_col], axis=-1)
    return jnp.concatenate([upper, lower], axis=1)


def gather_rows(part, axis):
    n = lax.axis_size(axis)
    if not is_pow2(n):
        return lax.all_gather(part, axis)
    me = lax.axis_index(axis)
    blocks = part[None]
    k = n // 2
    while k >= 1:
        got = lax.ppermute(blocks, axis, xor_pairs(n, k))
        blocks = jnp.concatenate([blocks, got])
        k //= 2
    want = jnp.arange(n, dtype=jnp.int32) ^ me
    return blocks[order_of(want, n)]


def order_of(want, count):
    steps = int(math.log2(count))
    slot = jnp.zeros_like(want)
    for j in range(steps):
        k = count >> (j + 1)
        hit = (want & k) != 0
        slot = slot | jnp.where(hit, 1 << j, 0)
    return slot


def reduce_orient(best_part, power_part, axis):
    n = lax.axis_size(axis)
    if not is_pow2(n):
        best = lax.pmax(best_part, axis)
        power = lax.psum(power_part, axis)
        return best, power
    width = best_part.shape[-1]
    joined = jnp.stack([best_part.reshape(-1, width), power_part.reshape(-1, width)], axis=0)
    return reduce_joined(joined, best_part.shape, axis)


def reduce_joined(joined, shape, axis):
    n = lax.axis_size(axis)
    rows = joined.shape[1]
    if not is_pow2(n) or n < 2 or rows % n != 0:
        best = lax.pmax(joined[0], axis)
        power = lax.psum(joined[1], axis)
        return best.reshape(shape), power.reshape(shape)
    me = lax.axis_index(axis)
    half = rows // 2
    bit = me % 2
    keep = lax.dynamic_slice_in_dim(joined, bit * half, half, axis=1)
    send = lax.dynamic_slice_in_dim(joined, (1 - bit) * half, half, axis=1)
    got = lax.ppermute(send, axis, xor_pairs(n, 1))
    cur = jnp.stack([jnp.maximum(keep[0], got[0]), keep[1] + got[1]])
    return reduce_rest(cur, shape, axis)


def reduce_rest(cur, shape, axis):
    n = lax.axis_size(axis)
    me = lax.axis_index(axis)
    bit = me % 2
    half = cur.shape[1]
    members = n // 2
    group = me // 2
    piece = half // members
    own = lax.dynamic_slice_in_dim(cur, group * piece, piece, axis=1)
    best, power = own[0], own[1]
    for m in range(1, members):
        out = lax.dynamic_slice_in_dim(cur, (group ^ m) * piece, piece, axis=1)
        got = lax.ppermute(out, axis, xor_pairs(n, 2 * m))
        best = jnp.maximum(best, got[0])
        power = power + got[1]
    done = jnp.stack([best, power])
    slots = [done] + [lax.ppermute(done, axis, xor_pairs(n, 2 * m)) for m in range(1, members)]
    pieces = jnp.stack(slots)[jnp.arange(members, dtype=jnp.int32) ^ group]
    mine = jnp.moveaxis(pieces, 0, 1).reshape(2, half, cur.shape[2])
    other = lax.ppermute(mine, axis, xor_pairs(n, 1))
    whole = jnp.where(bit == 1, jnp.concatenate([other, mine], axis=1), jnp.concatenate([mine, other], axis=1))
    return whole[0].reshape(shape), whole[1].reshape(shape)


def match_kernel(blocks, size, width, rows_t, tiles, peaks_n, l_ref, tm_ref, sp_ref, ct_ref, cr_ref, sr_ref, best_ref, pow_ref, m_ref):
    j = pl.program_id(0)

    @pl.when(j == 0)
    def _():
        best_ref[...] = jnp.full(best_ref.shape, lowest_score, jnp.float32)
        pow_ref[...] = jnp.zeros(pow_ref.shape, jnp.float32)

    for t in range(tiles):
        rows = pl.ds(t * rows_t, rows_t)
        image_re = sp_ref[0, rows, :].astype(jnp.float32)
        image_im = sp_ref[1, rows, :].astype(jnp.float32)
        tmpl_re = tm_ref[t, 0, 0].astype(jnp.float32)
        tmpl_im = tm_ref[t, 0, 1].astype(jnp.float32)
        m_ref[rows, pl.ds(0, size)] = (image_re * tmpl_re + image_im * tmpl_im).astype(jnp.bfloat16)
        m_ref[rows, pl.ds(size, size)] = (image_im * tmpl_re - image_re * tmpl_im).astype(jnp.bfloat16)

    for p in range(peaks_n):
        @pl.when(l_ref[p * blocks + j] > 0)
        def _():
            g = jnp.dot(m_ref[...], ct_ref[p], preferred_element_type=jnp.float32).astype(jnp.bfloat16)
            score = jnp.dot(cr_ref[p], g[:, :width], preferred_element_type=jnp.float32)
            score = score - jnp.dot(sr_ref[p], g[:, width:], preferred_element_type=jnp.float32)
            score = score / size
            best_ref[p] = jnp.maximum(best_ref[p], score)
            pow_ref[p] = pow_ref[p] + score * score


def match(flags, tmpl, spec, col_table, cos_t, sin_t):
    tiles, blocks, _, rows_t, size = tmpl.shape
    peaks_n, width = cos_t.shape[0], cos_t.shape[1]
    kernel = functools.partial(match_kernel, blocks, size, width, rows_t, tiles, peaks_n)
    flops = blocks * peaks_n * (2 * size * 2 * size * 2 * width + 2 * 2 * width * size * width)
    cost = pl.CostEstimate(flops=flops, transcendentals=0, bytes_accessed=tmpl.size * 2 + spec.size * 2 + col_table.size * 2)
    out = jax.ShapeDtypeStruct((peaks_n, width, width), jnp.float32)
    return pl.pallas_call(
        kernel,
        grid_spec=pltpu.PrefetchScalarGridSpec(
            num_scalar_prefetch=1,
            grid=(blocks,),
            in_specs=[
                pl.BlockSpec((tiles, 1, 2, rows_t, size), lambda j, l: (0, j, 0, 0, 0)),
                pl.BlockSpec((2, size, size), lambda j, l: (0, 0, 0)),
                pl.BlockSpec(col_table.shape, lambda j, l: (0, 0, 0)),
                pl.BlockSpec(cos_t.shape, lambda j, l: (0, 0, 0)),
                pl.BlockSpec(sin_t.shape, lambda j, l: (0, 0, 0)),
            ],
            out_specs=[
                pl.BlockSpec((peaks_n, width, width), lambda j, l: (0, 0, 0)),
                pl.BlockSpec((peaks_n, width, width), lambda j, l: (0, 0, 0)),
            ],
            scratch_shapes=[pltpu.VMEM((size, 2 * size), jnp.bfloat16)],
        ),
        out_shape=[out, out],
        compiler_params=pltpu.CompilerParams(dimension_semantics=("arbitrary",)),
        cost_estimate=cost,
    )(flags, tmpl, spec, col_table, cos_t, sin_t)


def rows_kernel(blocks, size, width, rows_t, peaks_n, chunk, n_steps, final, per, f_ref, ta_ref, tb_ref, rid_ref, off_ref, pos_ref, tma_ref, tmb_ref, sp_ref, ct_ref, cr_ref, sr_ref, *rest):
    if final:
        init_ref, out_ref, acc_ref, m_ref = rest
    else:
        part_ref, acc_ref, m_ref = rest
    jj = pl.program_id(0)
    i = pl.program_id(1)
    span = 2 * rows_t

    if final:
        @pl.when((jj == 0) & (i == 0))
        def _():
            out_ref[:, 0] = jnp.full((peaks_n, width, width), lowest_score, jnp.float32)
            out_ref[:, 1] = jnp.zeros((peaks_n, width, width), jnp.float32)

        @pl.when(i == 0)
        def _():
            acc_ref[...] = init_ref[...]
    else:
        @pl.when(i == 0)
        def _():
            acc_ref[...] = jnp.zeros(acc_ref.shape, jnp.float32)

    for o in range(per):
        for u, tm_ref in enumerate((tma_ref, tmb_ref)):
            def mix(c, carry, u=u, o=o, tm_ref=tm_ref):
                row = pl.multiple_of(c * chunk, chunk)
                in_row = pl.multiple_of(off_ref[u] + c * chunk, chunk)
                out_row = pl.multiple_of(o * span + off_ref[u] + c * chunk, chunk)
                image_re = sp_ref[0, pl.ds(in_row, chunk), :]
                image_im = sp_ref[1, pl.ds(in_row, chunk), :]
                tmpl_re = tm_ref[0, o, 0, pl.ds(row, chunk), :].astype(jnp.float32)
                tmpl_im = tm_ref[0, o, 1, pl.ds(row, chunk), :].astype(jnp.float32)
                m_ref[pl.ds(out_row, chunk), pl.ds(0, size)] = (image_re * tmpl_re + image_im * tmpl_im).astype(jnp.bfloat16)
                m_ref[pl.ds(out_row, chunk), pl.ds(size, size)] = (image_im * tmpl_re - image_re * tmpl_im).astype(jnp.bfloat16)
                return carry

            lax.fori_loop(0, rows_t // chunk, mix, 0, unroll=4)

    for p in range(peaks_n):
        count = f_ref[p * blocks + per * jj]
        for o in range(1, per):
            count = count + f_ref[p * blocks + per * jj + o]

        @pl.when(count > 0)
        def _():
            g = jnp.dot(m_ref[...], ct_ref[p], preferred_element_type=jnp.float32).astype(jnp.bfloat16)
            for o in range(per):
                rows = slice(o * span, (o + 1) * span)
                part = jnp.dot(cr_ref[p], g[rows, :width], preferred_element_type=jnp.float32)
                part = part - jnp.dot(sr_ref[p], g[rows, width:], preferred_element_type=jnp.float32)
                acc_ref[p, o] = acc_ref[p, o] + part

    @pl.when(i == n_steps - 1)
    def _():
        if final:
            for p in range(peaks_n):
                for o in range(per):
                    @pl.when(f_ref[p * blocks + per * jj + o] > 0)
                    def _():
                        score = acc_ref[p, o] / size
                        q = pos_ref[p]
                        out_ref[q, 0] = jnp.maximum(out_ref[q, 0], score)
                        out_ref[q, 1] = out_ref[q, 1] + score * score
        else:
            part_ref[...] = acc_ref[...]


def match_rows(flags, tas, tbs, rids, offs, pos, tmpl_a, tmpl_b, spec, col_table, cos_t, sin_t, init=None):
    _, blocks, _, rows_t, size = tmpl_a.shape
    peaks_n, width = cos_t.shape[0], cos_t.shape[1]
    n_steps = tas.shape[0]
    final = init is not None
    chunk = math.gcd(rows_t, 16)
    span = 2 * rows_t
    per = 4 if blocks % 4 == 0 else 2
    kernel = functools.partial(rows_kernel, blocks, size, width, rows_t, peaks_n, chunk, n_steps, final, per)
    flops = blocks * peaks_n * n_steps * (2 * span * 2 * size * 2 * width + 2 * 2 * width * span * width)
    cost = pl.CostEstimate(flops=flops, transcendentals=0, bytes_accessed=n_steps * blocks * 2 * span * size * 6 + col_table.size * 2)
    in_specs = [
        pl.BlockSpec((1, per, 2, rows_t, size), lambda j, i, f, ta, tb, r, o, q: (ta[i], j, 0, 0, 0)),
        pl.BlockSpec((1, per, 2, rows_t, size), lambda j, i, f, ta, tb, r, o, q: (tb[i], j, 0, 0, 0)),
        pl.BlockSpec((2, span, size), lambda j, i, f, ta, tb, r, o, q: (0, r[i], 0)),
        pl.BlockSpec(col_table.shape, lambda j, i, f, ta, tb, r, o, q: (0, 0, 0)),
        pl.BlockSpec((peaks_n, width, span), lambda j, i, f, ta, tb, r, o, q: (0, 0, r[i])),
        pl.BlockSpec((peaks_n, width, span), lambda j, i, f, ta, tb, r, o, q: (0, 0, r[i])),
    ]
    args = [flags, tas, tbs, rids, offs, pos, tmpl_a, tmpl_b, spec, col_table, cos_t, sin_t]
    part_spec = pl.BlockSpec((peaks_n, per, width, width), lambda j, i, f, ta, tb, r, o, q: (0, j, 0, 0))
    if final:
        in_specs.append(part_spec)
        args.append(init)
        out_shape = jax.ShapeDtypeStruct((peaks_n, 2, width, width), jnp.float32)
        out_specs = pl.BlockSpec((peaks_n, 2, width, width), lambda j, i, f, ta, tb, r, o, q: (0, 0, 0, 0))
    else:
        out_shape = jax.ShapeDtypeStruct((peaks_n, blocks, width, width), jnp.float32)
        out_specs = part_spec
    return pl.pallas_call(
        kernel,
        grid_spec=pltpu.PrefetchScalarGridSpec(
            num_scalar_prefetch=6,
            grid=(blocks // per, n_steps),
            in_specs=in_specs,
            out_specs=out_specs,
            scratch_shapes=[pltpu.VMEM((peaks_n, per, width, width), jnp.float32), pltpu.VMEM((per * span, 2 * size), jnp.bfloat16)],
        ),
        out_shape=out_shape,
        compiler_params=pltpu.CompilerParams(dimension_semantics=("arbitrary", "arbitrary")),
        cost_estimate=cost,
    )(*args)


def local(tile_spectra, template_spectra, peaks, listed):
    size = tile_spectra.shape[3]
    width = W
    tiles = lax.axis_size("tile")
    rows_t = template_spectra.shape[2]
    tmpl = lax.all_gather(template_spectra, "tile", axis=0)
    block_size = tmpl.shape[1]
    spec = gather_rows(tile_spectra[0], "orient")
    spec = jnp.moveaxis(spec, 0, 1).reshape(2, size, size)
    freqs = jnp.arange(size, dtype=jnp.int32)
    cos_row, sin_row = angle_tables(freqs, peaks[0][:, 0], size, width)
    cos_t = jnp.swapaxes(cos_row, 1, 2)
    sin_t = jnp.swapaxes(sin_row, 1, 2)
    col_table = col_tables(peaks[0], size, width)
    listed_ids = listed[0]
    global_ids = lax.axis_index("orient") * block_size + jnp.arange(block_size, dtype=jnp.int32)
    is_listed = jnp.any(listed_ids[:, :, None] == global_ids[None, None, :], axis=1)
    flags = is_listed.astype(jnp.int32).reshape(-1)
    best_shape = (listed.shape[1], width, width)
    if rows_t % 128 != 0 or tiles % 2 != 0 or block_size % 2 != 0:
        best_part, power_part = match(flags, tmpl, spec, col_table, cos_t, sin_t)
    else:
        me = lax.axis_index("tile")
        sibling = lax.ppermute(template_spectra, "tile", xor_pairs(tiles, 1))
        spec32 = spec.astype(jnp.float32)
        chip = me // 2
        odd = (me % 2).astype(jnp.int32)
        zero = jnp.zeros((1,), jnp.int32)
        near_offs = jnp.stack([odd, 1 - odd]) * rows_t
        own, sib = template_spectra[None], sibling[None]
        peaks_n = best_shape[0]
        if peaks_n % 2 == 0:
            pos = jnp.arange(peaks_n, dtype=jnp.int32) ^ ((1 - odd_orient()) * (peaks_n // 2))
        else:
            pos = jnp.arange(peaks_n, dtype=jnp.int32)
        partial = match_rows(flags, zero, zero, chip[None].astype(jnp.int32), near_offs, pos, own, sib, spec32, col_table, cos_t, sin_t)
        far = far_chips(chip, tiles // 2)
        far_offs = jnp.array([0, rows_t], jnp.int32)
        placed = match_rows(flags, far * 2, far * 2 + 1, far, far_offs, pos, tmpl, tmpl, spec32, col_table, cos_t, sin_t, init=partial)
        n = lax.axis_size("orient")
        if peaks_n % 2 == 0 and is_pow2(n) and n >= 2 and (peaks_n * width) % n == 0:
            half_peaks = peaks_n // 2
            send, keep = placed[:half_peaks], placed[half_peaks:]
            got = lax.ppermute(send, "orient", xor_pairs(n, 1))
            cur = jnp.stack([jnp.maximum(keep[:, 0], got[:, 0]), keep[:, 1] + got[:, 1]])
            best_all, power_all = reduce_rest(cur.reshape(2, half_peaks * width, width), best_shape, "orient")
        else:
            joined = jnp.moveaxis(placed, 1, 0).reshape(2, -1, width)
            best_all, power_all = reduce_joined(joined, best_shape, "orient")
        return (best_all[None], (power_all / LIST)[None])
    best_all, power_all = reduce_orient(best_part, power_part, "orient")
    return (best_all[None], (power_all / LIST)[None])


def odd_orient():
    return (lax.axis_index("orient") % 2).astype(jnp.int32)


def far_chips(chip, chips):
    steps = jnp.arange(chips - 1, dtype=jnp.int32)
    return steps + (steps >= chip).astype(jnp.int32)


def solution(mesh):
    placed = (
        P("tile", None, "orient", None),
        P("orient", None, "tile", None),
        P("tile", None, None),
        P("tile", None, None),
    )
    return jax.shard_map(
        local,
        mesh=mesh,
        in_specs=placed,
        out_specs=(P("tile", None, None, None), P("tile", None, None, None)),
        check_vma=False,
    )
```

```python
import functools
import math

import jax
import jax.numpy as jnp
from jax import lax
from jax.experimental import pallas as pl
from jax.experimental.pallas import tpu as pltpu
from jax.sharding import PartitionSpec as P

W = 128
LIST = 48


lowest_score = -1e30


def xor_pairs(n, k):
    return [(i, i ^ k) for i in range(n)]


def is_pow2(n):
    return n & (n - 1) == 0


def angle_tables(freqs, coords, size, width):
    offsets = jnp.arange(width, dtype=jnp.int32) - width // 2
    position = (coords[:, None] + offsets[None, :]) % size
    phase = freqs[None, :, None] * position[:, None, :] % size
    angle = phase.astype(jnp.float32) * (2.0 * math.pi / size)
    return (jnp.cos(angle).astype(jnp.bfloat16), jnp.sin(angle).astype(jnp.bfloat16))


def col_tables(peak_rows, size, width):
    freqs = jnp.arange(size, dtype=jnp.int32)
    cos_col, sin_col = angle_tables(freqs, peak_rows[:, 1], size, width)
    upper = jnp.concatenate([cos_col, sin_col], axis=-1)
    lower = jnp.concatenate([-sin_col, cos_col], axis=-1)
    return jnp.concatenate([upper, lower], axis=1)


def gather_rows(part, axis):
    n = lax.axis_size(axis)
    if not is_pow2(n):
        return lax.all_gather(part, axis)
    me = lax.axis_index(axis)
    blocks = part[None]
    k = n // 2
    while k >= 1:
        got = lax.ppermute(blocks, axis, xor_pairs(n, k))
        blocks = jnp.concatenate([blocks, got])
        k //= 2
    want = jnp.arange(n, dtype=jnp.int32) ^ me
    return blocks[order_of(want, n)]


def order_of(want, count):
    steps = int(math.log2(count))
    slot = jnp.zeros_like(want)
    for j in range(steps):
        k = count >> (j + 1)
        hit = (want & k) != 0
        slot = slot | jnp.where(hit, 1 << j, 0)
    return slot


def reduce_orient(best_part, power_part, axis):
    n = lax.axis_size(axis)
    if not is_pow2(n):
        best = lax.pmax(best_part, axis)
        power = lax.psum(power_part, axis)
        return best, power
    width = best_part.shape[-1]
    joined = jnp.stack([best_part.reshape(-1, width), power_part.reshape(-1, width)], axis=0)
    return reduce_joined(joined, best_part.shape, axis)


def reduce_joined(joined, shape, axis):
    n = lax.axis_size(axis)
    rows = joined.shape[1]
    if not is_pow2(n) or n < 2 or rows % n != 0:
        best = lax.pmax(joined[0], axis)
        power = lax.psum(joined[1], axis)
        return best.reshape(shape), power.reshape(shape)
    me = lax.axis_index(axis)
    half = rows // 2
    bit = me % 2
    keep = lax.dynamic_slice_in_dim(joined, bit * half, half, axis=1)
    send = lax.dynamic_slice_in_dim(joined, (1 - bit) * half, half, axis=1)
    got = lax.ppermute(send, axis, xor_pairs(n, 1))
    cur = jnp.stack([jnp.maximum(keep[0], got[0]), keep[1] + got[1]])
    members = n // 2
    group = me // 2
    piece = half // members
    own = lax.dynamic_slice_in_dim(cur, group * piece, piece, axis=1)
    best, power = own[0], own[1]
    for m in range(1, members):
        out = lax.dynamic_slice_in_dim(cur, (group ^ m) * piece, piece, axis=1)
        got = lax.ppermute(out, axis, xor_pairs(n, 2 * m))
        best = jnp.maximum(best, got[0])
        power = power + got[1]
    done = jnp.stack([best, power])
    slots = [done] + [lax.ppermute(done, axis, xor_pairs(n, 2 * m)) for m in range(1, members)]
    pieces = jnp.stack(slots)[jnp.arange(members, dtype=jnp.int32) ^ group]
    mine = jnp.moveaxis(pieces, 0, 1).reshape(2, half, joined.shape[2])
    other = lax.ppermute(mine, axis, xor_pairs(n, 1))
    whole = jnp.where(bit == 1, jnp.concatenate([other, mine], axis=1), jnp.concatenate([mine, other], axis=1))
    return whole[0].reshape(shape), whole[1].reshape(shape)


def match_kernel(blocks, size, width, rows_t, tiles, peaks_n, l_ref, tm_ref, sp_ref, ct_ref, cr_ref, sr_ref, best_ref, pow_ref, m_ref):
    j = pl.program_id(0)

    @pl.when(j == 0)
    def _():
        best_ref[...] = jnp.full(best_ref.shape, lowest_score, jnp.float32)
        pow_ref[...] = jnp.zeros(pow_ref.shape, jnp.float32)

    for t in range(tiles):
        rows = pl.ds(t * rows_t, rows_t)
        image_re = sp_ref[0, rows, :].astype(jnp.float32)
        image_im = sp_ref[1, rows, :].astype(jnp.float32)
        tmpl_re = tm_ref[t, 0, 0].astype(jnp.float32)
        tmpl_im = tm_ref[t, 0, 1].astype(jnp.float32)
        m_ref[rows, pl.ds(0, size)] = (image_re * tmpl_re + image_im * tmpl_im).astype(jnp.bfloat16)
        m_ref[rows, pl.ds(size, size)] = (image_im * tmpl_re - image_re * tmpl_im).astype(jnp.bfloat16)

    for p in range(peaks_n):
        @pl.when(l_ref[p * blocks + j] > 0)
        def _():
            g = jnp.dot(m_ref[...], ct_ref[p], preferred_element_type=jnp.float32).astype(jnp.bfloat16)
            score = jnp.dot(cr_ref[p], g[:, :width], preferred_element_type=jnp.float32)
            score = score - jnp.dot(sr_ref[p], g[:, width:], preferred_element_type=jnp.float32)
            score = score / size
            best_ref[p] = jnp.maximum(best_ref[p], score)
            pow_ref[p] = pow_ref[p] + score * score


def match(flags, tmpl, spec, col_table, cos_t, sin_t):
    tiles, blocks, _, rows_t, size = tmpl.shape
    peaks_n, width = cos_t.shape[0], cos_t.shape[1]
    kernel = functools.partial(match_kernel, blocks, size, width, rows_t, tiles, peaks_n)
    flops = blocks * peaks_n * (2 * size * 2 * size * 2 * width + 2 * 2 * width * size * width)
    cost = pl.CostEstimate(flops=flops, transcendentals=0, bytes_accessed=tmpl.size * 2 + spec.size * 2 + col_table.size * 2)
    out = jax.ShapeDtypeStruct((peaks_n, width, width), jnp.float32)
    return pl.pallas_call(
        kernel,
        grid_spec=pltpu.PrefetchScalarGridSpec(
            num_scalar_prefetch=1,
            grid=(blocks,),
            in_specs=[
                pl.BlockSpec((tiles, 1, 2, rows_t, size), lambda j, l: (0, j, 0, 0, 0)),
                pl.BlockSpec((2, size, size), lambda j, l: (0, 0, 0)),
                pl.BlockSpec(col_table.shape, lambda j, l: (0, 0, 0)),
                pl.BlockSpec(cos_t.shape, lambda j, l: (0, 0, 0)),
                pl.BlockSpec(sin_t.shape, lambda j, l: (0, 0, 0)),
            ],
            out_specs=[
                pl.BlockSpec((peaks_n, width, width), lambda j, l: (0, 0, 0)),
                pl.BlockSpec((peaks_n, width, width), lambda j, l: (0, 0, 0)),
            ],
            scratch_shapes=[pltpu.VMEM((size, 2 * size), jnp.bfloat16)],
        ),
        out_shape=[out, out],
        compiler_params=pltpu.CompilerParams(dimension_semantics=("arbitrary",)),
        cost_estimate=cost,
    )(flags, tmpl, spec, col_table, cos_t, sin_t)


def rows_kernel(blocks, size, width, rows_t, peaks_n, chunk, n_steps, final, per, f_ref, ta_ref, tb_ref, rid_ref, off_ref, tma_ref, tmb_ref, sp_ref, ct_ref, cr_ref, sr_ref, *rest):
    if final:
        init_ref, out_ref, acc_ref, m_ref = rest
        best_ref, pow_ref = out_ref.at[0], out_ref.at[1]
    else:
        part_ref, acc_ref, m_ref = rest
    jj = pl.program_id(0)
    i = pl.program_id(1)
    span = 2 * rows_t

    if final:
        @pl.when((jj == 0) & (i == 0))
        def _():
            best_ref[...] = jnp.full(best_ref.shape, lowest_score, jnp.float32)
            pow_ref[...] = jnp.zeros(pow_ref.shape, jnp.float32)

        @pl.when(i == 0)
        def _():
            acc_ref[...] = init_ref[...]
    else:
        @pl.when(i == 0)
        def _():
            acc_ref[...] = jnp.zeros(acc_ref.shape, jnp.float32)

    for o in range(per):
        for u, tm_ref in enumerate((tma_ref, tmb_ref)):
            def mix(c, carry, u=u, o=o, tm_ref=tm_ref):
                row = pl.multiple_of(c * chunk, chunk)
                in_row = pl.multiple_of(off_ref[u] + c * chunk, chunk)
                out_row = pl.multiple_of(o * span + off_ref[u] + c * chunk, chunk)
                image_re = sp_ref[0, pl.ds(in_row, chunk), :].astype(jnp.float32)
                image_im = sp_ref[1, pl.ds(in_row, chunk), :].astype(jnp.float32)
                tmpl_re = tm_ref[0, o, 0, pl.ds(row, chunk), :].astype(jnp.float32)
                tmpl_im = tm_ref[0, o, 1, pl.ds(row, chunk), :].astype(jnp.float32)
                m_ref[pl.ds(out_row, chunk), pl.ds(0, size)] = (image_re * tmpl_re + image_im * tmpl_im).astype(jnp.bfloat16)
                m_ref[pl.ds(out_row, chunk), pl.ds(size, size)] = (image_im * tmpl_re - image_re * tmpl_im).astype(jnp.bfloat16)
                return carry

            lax.fori_loop(0, rows_t // chunk, mix, 0, unroll=4)

    for p in range(peaks_n):
        count = f_ref[p * blocks + per * jj]
        for o in range(1, per):
            count = count + f_ref[p * blocks + per * jj + o]

        @pl.when(count > 0)
        def _():
            g = jnp.dot(m_ref[...], ct_ref[p], preferred_element_type=jnp.float32).astype(jnp.bfloat16)
            for o in range(per):
                rows = slice(o * span, (o + 1) * span)
                part = jnp.dot(cr_ref[p], g[rows, :width], preferred_element_type=jnp.float32)
                part = part - jnp.dot(sr_ref[p], g[rows, width:], preferred_element_type=jnp.float32)
                acc_ref[p, o] = acc_ref[p, o] + part

    @pl.when(i == n_steps - 1)
    def _():
        if final:
            for p in range(peaks_n):
                for o in range(per):
                    @pl.when(f_ref[p * blocks + per * jj + o] > 0)
                    def _():
                        score = acc_ref[p, o] / size
                        best_ref[p] = jnp.maximum(best_ref[p], score)
                        pow_ref[p] = pow_ref[p] + score * score
        else:
            part_ref[...] = acc_ref[...]


def match_rows(flags, tas, tbs, rids, offs, tmpl_a, tmpl_b, spec, col_table, cos_t, sin_t, init=None):
    _, blocks, _, rows_t, size = tmpl_a.shape
    peaks_n, width = cos_t.shape[0], cos_t.shape[1]
    n_steps = tas.shape[0]
    final = init is not None
    chunk = math.gcd(rows_t, 16)
    span = 2 * rows_t
    per = 4 if blocks % 4 == 0 else 2
    kernel = functools.partial(rows_kernel, blocks, size, width, rows_t, peaks_n, chunk, n_steps, final, per)
    flops = blocks * peaks_n * n_steps * (2 * span * 2 * size * 2 * width + 2 * 2 * width * span * width)
    cost = pl.CostEstimate(flops=flops, transcendentals=0, bytes_accessed=n_steps * blocks * 2 * span * size * 4 + col_table.size * 2)
    in_specs = [
        pl.BlockSpec((1, per, 2, rows_t, size), lambda j, i, f, ta, tb, r, o: (ta[i], j, 0, 0, 0)),
        pl.BlockSpec((1, per, 2, rows_t, size), lambda j, i, f, ta, tb, r, o: (tb[i], j, 0, 0, 0)),
        pl.BlockSpec((2, span, size), lambda j, i, f, ta, tb, r, o: (0, r[i], 0)),
        pl.BlockSpec(col_table.shape, lambda j, i, f, ta, tb, r, o: (0, 0, 0)),
        pl.BlockSpec((peaks_n, width, span), lambda j, i, f, ta, tb, r, o: (0, 0, r[i])),
        pl.BlockSpec((peaks_n, width, span), lambda j, i, f, ta, tb, r, o: (0, 0, r[i])),
    ]
    args = [flags, tas, tbs, rids, offs, tmpl_a, tmpl_b, spec, col_table, cos_t, sin_t]
    part_spec = pl.BlockSpec((peaks_n, per, width, width), lambda j, i, f, ta, tb, r, o: (0, j, 0, 0))
    if final:
        in_specs.append(part_spec)
        args.append(init)
        out_shape = jax.ShapeDtypeStruct((2, peaks_n, width, width), jnp.float32)
        out_specs = pl.BlockSpec((2, peaks_n, width, width), lambda j, i, f, ta, tb, r, o: (0, 0, 0, 0))
    else:
        out_shape = jax.ShapeDtypeStruct((peaks_n, blocks, width, width), jnp.float32)
        out_specs = part_spec
    return pl.pallas_call(
        kernel,
        grid_spec=pltpu.PrefetchScalarGridSpec(
            num_scalar_prefetch=5,
            grid=(blocks // per, n_steps),
            in_specs=in_specs,
            out_specs=out_specs,
            scratch_shapes=[pltpu.VMEM((peaks_n, per, width, width), jnp.float32), pltpu.VMEM((per * span, 2 * size), jnp.bfloat16)],
        ),
        out_shape=out_shape,
        compiler_params=pltpu.CompilerParams(dimension_semantics=("arbitrary", "arbitrary")),
        cost_estimate=cost,
    )(*args)


def local(tile_spectra, template_spectra, peaks, listed):
    size = tile_spectra.shape[3]
    width = W
    tiles = lax.axis_size("tile")
    rows_t = template_spectra.shape[2]
    tmpl = lax.all_gather(template_spectra, "tile", axis=0)
    block_size = tmpl.shape[1]
    spec = gather_rows(tile_spectra[0], "orient")
    spec = jnp.moveaxis(spec, 0, 1).reshape(2, size, size)
    freqs = jnp.arange(size, dtype=jnp.int32)
    cos_row, sin_row = angle_tables(freqs, peaks[0][:, 0], size, width)
    cos_t = jnp.swapaxes(cos_row, 1, 2)
    sin_t = jnp.swapaxes(sin_row, 1, 2)
    col_table = col_tables(peaks[0], size, width)
    listed_ids = listed[0]
    global_ids = lax.axis_index("orient") * block_size + jnp.arange(block_size, dtype=jnp.int32)
    is_listed = jnp.any(listed_ids[:, :, None] == global_ids[None, None, :], axis=1)
    flags = is_listed.astype(jnp.int32).reshape(-1)
    best_shape = (listed.shape[1], width, width)
    if rows_t % 128 != 0 or tiles % 2 != 0 or block_size % 2 != 0:
        best_part, power_part = match(flags, tmpl, spec, col_table, cos_t, sin_t)
    else:
        me = lax.axis_index("tile")
        sibling = lax.ppermute(template_spectra, "tile", xor_pairs(tiles, 1))
        chip = me // 2
        odd = (me % 2).astype(jnp.int32)
        zero = jnp.zeros((1,), jnp.int32)
        near_offs = jnp.stack([odd, 1 - odd]) * rows_t
        own, sib = template_spectra[None], sibling[None]
        partial = match_rows(flags, zero, zero, chip[None].astype(jnp.int32), near_offs, own, sib, spec, col_table, cos_t, sin_t)
        far = far_chips(chip, tiles // 2)
        far_offs = jnp.array([0, rows_t], jnp.int32)
        joined = match_rows(flags, far * 2, far * 2 + 1, far, far_offs, tmpl, tmpl, spec, col_table, cos_t, sin_t, init=partial)
        best_all, power_all = reduce_joined(joined.reshape(2, -1, width), best_shape, "orient")
        return (best_all[None], (power_all / LIST)[None])
    best_all, power_all = reduce_orient(best_part, power_part, "orient")
    return (best_all[None], (power_all / LIST)[None])


def far_chips(chip, chips):
    steps = jnp.arange(chips - 1, dtype=jnp.int32)
    return steps + (steps >= chip).astype(jnp.int32)


def solution(mesh):
    placed = (
        P("tile", None, "orient", None),
        P("orient", None, "tile", None),
        P("tile", None, None),
        P("tile", None, None),
    )
    return jax.shard_map(
        local,
        mesh=mesh,
        in_specs=placed,
        out_specs=(P("tile", None, None, None), P("tile", None, None, None)),
        check_vma=False,
    )
```

```python
import functools
import math

import jax
import jax.numpy as jnp
from jax import lax
from jax.experimental import pallas as pl
from jax.experimental.pallas import tpu as pltpu
from jax.sharding import PartitionSpec as P

W = 128
LIST = 48


lowest_score = -1e30


def xor_pairs(n, k):
    return [(i, i ^ k) for i in range(n)]


def is_pow2(n):
    return n & (n - 1) == 0


def angle_tables(freqs, coords, size, width):
    offsets = jnp.arange(width, dtype=jnp.int32) - width // 2
    position = (coords[:, None] + offsets[None, :]) % size
    phase = freqs[None, :, None] * position[:, None, :] % size
    angle = phase.astype(jnp.float32) * (2.0 * math.pi / size)
    return (jnp.cos(angle).astype(jnp.bfloat16), jnp.sin(angle).astype(jnp.bfloat16))


def col_tables(peak_rows, size, width):
    freqs = jnp.arange(size, dtype=jnp.int32)
    cos_col, sin_col = angle_tables(freqs, peak_rows[:, 1], size, width)
    upper = jnp.concatenate([cos_col, sin_col], axis=-1)
    lower = jnp.concatenate([-sin_col, cos_col], axis=-1)
    return jnp.concatenate([upper, lower], axis=1)


def gather_rows(part, axis):
    n = lax.axis_size(axis)
    if not is_pow2(n):
        return lax.all_gather(part, axis)
    me = lax.axis_index(axis)
    blocks = part[None]
    k = n // 2
    while k >= 1:
        got = lax.ppermute(blocks, axis, xor_pairs(n, k))
        blocks = jnp.concatenate([blocks, got])
        k //= 2
    want = jnp.arange(n, dtype=jnp.int32) ^ me
    return blocks[order_of(want, n)]


def order_of(want, count):
    steps = int(math.log2(count))
    slot = jnp.zeros_like(want)
    for j in range(steps):
        k = count >> (j + 1)
        hit = (want & k) != 0
        slot = slot | jnp.where(hit, 1 << j, 0)
    return slot


def reduce_orient(best_part, power_part, axis):
    n = lax.axis_size(axis)
    if not is_pow2(n):
        best = lax.pmax(best_part, axis)
        power = lax.psum(power_part, axis)
        return best, power
    width = best_part.shape[-1]
    joined = jnp.stack([best_part.reshape(-1, width), power_part.reshape(-1, width)], axis=0)
    return reduce_joined(joined, best_part.shape, axis)


def reduce_joined(joined, shape, axis):
    n = lax.axis_size(axis)
    rows = joined.shape[1]
    if not is_pow2(n) or n < 2 or rows % n != 0:
        best = lax.pmax(joined[0], axis)
        power = lax.psum(joined[1], axis)
        return best.reshape(shape), power.reshape(shape)
    me = lax.axis_index(axis)
    half = rows // 2
    bit = me % 2
    keep = lax.dynamic_slice_in_dim(joined, bit * half, half, axis=1)
    send = lax.dynamic_slice_in_dim(joined, (1 - bit) * half, half, axis=1)
    got = lax.ppermute(send, axis, xor_pairs(n, 1))
    cur = jnp.stack([jnp.maximum(keep[0], got[0]), keep[1] + got[1]])
    members = n // 2
    group = me // 2
    piece = half // members
    own = lax.dynamic_slice_in_dim(cur, group * piece, piece, axis=1)
    best, power = own[0], own[1]
    for m in range(1, members):
        out = lax.dynamic_slice_in_dim(cur, (group ^ m) * piece, piece, axis=1)
        got = lax.ppermute(out, axis, xor_pairs(n, 2 * m))
        best = jnp.maximum(best, got[0])
        power = power + got[1]
    done = jnp.stack([best, power])
    slots = [done] + [lax.ppermute(done, axis, xor_pairs(n, 2 * m)) for m in range(1, members)]
    pieces = jnp.stack(slots)[jnp.arange(members, dtype=jnp.int32) ^ group]
    mine = jnp.moveaxis(pieces, 0, 1).reshape(2, half, joined.shape[2])
    other = lax.ppermute(mine, axis, xor_pairs(n, 1))
    whole = jnp.where(bit == 1, jnp.concatenate([other, mine], axis=1), jnp.concatenate([mine, other], axis=1))
    return whole[0].reshape(shape), whole[1].reshape(shape)


def match_kernel(blocks, size, width, rows_t, tiles, peaks_n, l_ref, tm_ref, sp_ref, ct_ref, cr_ref, sr_ref, best_ref, pow_ref, m_ref):
    j = pl.program_id(0)

    @pl.when(j == 0)
    def _():
        best_ref[...] = jnp.full(best_ref.shape, lowest_score, jnp.float32)
        pow_ref[...] = jnp.zeros(pow_ref.shape, jnp.float32)

    for t in range(tiles):
        rows = pl.ds(t * rows_t, rows_t)
        image_re = sp_ref[0, rows, :].astype(jnp.float32)
        image_im = sp_ref[1, rows, :].astype(jnp.float32)
        tmpl_re = tm_ref[t, 0, 0].astype(jnp.float32)
        tmpl_im = tm_ref[t, 0, 1].astype(jnp.float32)
        m_ref[rows, pl.ds(0, size)] = (image_re * tmpl_re + image_im * tmpl_im).astype(jnp.bfloat16)
        m_ref[rows, pl.ds(size, size)] = (image_im * tmpl_re - image_re * tmpl_im).astype(jnp.bfloat16)

    for p in range(peaks_n):
        @pl.when(l_ref[p * blocks + j] > 0)
        def _():
            g = jnp.dot(m_ref[...], ct_ref[p], preferred_element_type=jnp.float32).astype(jnp.bfloat16)
            score = jnp.dot(cr_ref[p], g[:, :width], preferred_element_type=jnp.float32)
            score = score - jnp.dot(sr_ref[p], g[:, width:], preferred_element_type=jnp.float32)
            score = score / size
            best_ref[p] = jnp.maximum(best_ref[p], score)
            pow_ref[p] = pow_ref[p] + score * score


def match(flags, tmpl, spec, col_table, cos_t, sin_t):
    tiles, blocks, _, rows_t, size = tmpl.shape
    peaks_n, width = cos_t.shape[0], cos_t.shape[1]
    kernel = functools.partial(match_kernel, blocks, size, width, rows_t, tiles, peaks_n)
    flops = blocks * peaks_n * (2 * size * 2 * size * 2 * width + 2 * 2 * width * size * width)
    cost = pl.CostEstimate(flops=flops, transcendentals=0, bytes_accessed=tmpl.size * 2 + spec.size * 2 + col_table.size * 2)
    out = jax.ShapeDtypeStruct((peaks_n, width, width), jnp.float32)
    return pl.pallas_call(
        kernel,
        grid_spec=pltpu.PrefetchScalarGridSpec(
            num_scalar_prefetch=1,
            grid=(blocks,),
            in_specs=[
                pl.BlockSpec((tiles, 1, 2, rows_t, size), lambda j, l: (0, j, 0, 0, 0)),
                pl.BlockSpec((2, size, size), lambda j, l: (0, 0, 0)),
                pl.BlockSpec(col_table.shape, lambda j, l: (0, 0, 0)),
                pl.BlockSpec(cos_t.shape, lambda j, l: (0, 0, 0)),
                pl.BlockSpec(sin_t.shape, lambda j, l: (0, 0, 0)),
            ],
            out_specs=[
                pl.BlockSpec((peaks_n, width, width), lambda j, l: (0, 0, 0)),
                pl.BlockSpec((peaks_n, width, width), lambda j, l: (0, 0, 0)),
            ],
            scratch_shapes=[pltpu.VMEM((size, 2 * size), jnp.bfloat16)],
        ),
        out_shape=[out, out],
        compiler_params=pltpu.CompilerParams(dimension_semantics=("arbitrary",)),
        cost_estimate=cost,
    )(flags, tmpl, spec, col_table, cos_t, sin_t)


def rows_kernel(blocks, size, width, rows_t, peaks_n, chunk, n_steps, final, per, f_ref, ta_ref, tb_ref, rid_ref, off_ref, tma_ref, tmb_ref, sp_ref, ct_ref, cr_ref, sr_ref, *rest):
    if final:
        init_ref, out_ref, acc_ref, m_ref, table_ref, table_sem = rest
        best_ref, pow_ref = out_ref.at[0], out_ref.at[1]
    else:
        part_ref, acc_ref, m_ref, table_ref, table_sem = rest
    jj = pl.program_id(0)
    i = pl.program_id(1)
    span = 2 * rows_t

    if final:
        @pl.when((jj == 0) & (i == 0))
        def _():
            best_ref[...] = jnp.full(best_ref.shape, lowest_score, jnp.float32)
            pow_ref[...] = jnp.zeros(pow_ref.shape, jnp.float32)

        @pl.when(i == 0)
        def _():
            acc_ref[...] = init_ref[...]
    else:
        @pl.when(i == 0)
        def _():
            acc_ref[...] = jnp.zeros(acc_ref.shape, jnp.float32)

    first = (pl.program_id(0) == 0) & (pl.program_id(1) == 0)
    table_copy = pltpu.make_async_copy(ct_ref, table_ref, table_sem)

    @pl.when(first)
    def _():
        table_copy.start()

    for o in range(per):
        for u, tm_ref in enumerate((tma_ref, tmb_ref)):
            def mix(c, carry, u=u, o=o, tm_ref=tm_ref):
                row = pl.multiple_of(c * chunk, chunk)
                in_row = pl.multiple_of(off_ref[u] + c * chunk, chunk)
                out_row = pl.multiple_of(o * span + off_ref[u] + c * chunk, chunk)
                image_re = sp_ref[0, pl.ds(in_row, chunk), :].astype(jnp.float32)
                image_im = sp_ref[1, pl.ds(in_row, chunk), :].astype(jnp.float32)
                tmpl_re = tm_ref[0, o, 0, pl.ds(row, chunk), :].astype(jnp.float32)
                tmpl_im = tm_ref[0, o, 1, pl.ds(row, chunk), :].astype(jnp.float32)
                m_ref[pl.ds(out_row, chunk), pl.ds(0, size)] = (image_re * tmpl_re + image_im * tmpl_im).astype(jnp.bfloat16)
                m_ref[pl.ds(out_row, chunk), pl.ds(size, size)] = (image_im * tmpl_re - image_re * tmpl_im).astype(jnp.bfloat16)
                return carry

            lax.fori_loop(0, rows_t // chunk, mix, 0, unroll=4)

    @pl.when(first)
    def _():
        table_copy.wait()

    for p in range(peaks_n):
        count = f_ref[p * blocks + per * jj]
        for o in range(1, per):
            count = count + f_ref[p * blocks + per * jj + o]

        @pl.when(count > 0)
        def _():
            g = jnp.dot(m_ref[...], table_ref[p], preferred_element_type=jnp.float32).astype(jnp.bfloat16)
            for o in range(per):
                rows = slice(o * span, (o + 1) * span)
                part = jnp.dot(cr_ref[p], g[rows, :width], preferred_element_type=jnp.float32)
                part = part - jnp.dot(sr_ref[p], g[rows, width:], preferred_element_type=jnp.float32)
                acc_ref[p, o] = acc_ref[p, o] + part

    @pl.when(i == n_steps - 1)
    def _():
        if final:
            for p in range(peaks_n):
                for o in range(per):
                    @pl.when(f_ref[p * blocks + per * jj + o] > 0)
                    def _():
                        score = acc_ref[p, o] / size
                        best_ref[p] = jnp.maximum(best_ref[p], score)
                        pow_ref[p] = pow_ref[p] + score * score
        else:
            part_ref[...] = acc_ref[...]


def match_rows(flags, tas, tbs, rids, offs, tmpl_a, tmpl_b, spec, col_table, cos_t, sin_t, init=None):
    _, blocks, _, rows_t, size = tmpl_a.shape
    peaks_n, width = cos_t.shape[0], cos_t.shape[1]
    n_steps = tas.shape[0]
    final = init is not None
    chunk = math.gcd(rows_t, 16)
    span = 2 * rows_t
    per = 4 if blocks % 4 == 0 else 2
    kernel = functools.partial(rows_kernel, blocks, size, width, rows_t, peaks_n, chunk, n_steps, final, per)
    flops = blocks * peaks_n * n_steps * (2 * span * 2 * size * 2 * width + 2 * 2 * width * span * width)
    cost = pl.CostEstimate(flops=flops, transcendentals=0, bytes_accessed=n_steps * blocks * 2 * span * size * 4 + col_table.size * 2)
    in_specs = [
        pl.BlockSpec((1, per, 2, rows_t, size), lambda j, i, f, ta, tb, r, o: (ta[i], j, 0, 0, 0)),
        pl.BlockSpec((1, per, 2, rows_t, size), lambda j, i, f, ta, tb, r, o: (tb[i], j, 0, 0, 0)),
        pl.BlockSpec((2, span, size), lambda j, i, f, ta, tb, r, o: (0, r[i], 0)),
        pl.BlockSpec(memory_space=pl.ANY),
        pl.BlockSpec((peaks_n, width, span), lambda j, i, f, ta, tb, r, o: (0, 0, r[i])),
        pl.BlockSpec((peaks_n, width, span), lambda j, i, f, ta, tb, r, o: (0, 0, r[i])),
    ]
    args = [flags, tas, tbs, rids, offs, tmpl_a, tmpl_b, spec, col_table, cos_t, sin_t]
    part_spec = pl.BlockSpec((peaks_n, per, width, width), lambda j, i, f, ta, tb, r, o: (0, j, 0, 0))
    if final:
        in_specs.append(part_spec)
        args.append(init)
        out_shape = jax.ShapeDtypeStruct((2, peaks_n, width, width), jnp.float32)
        out_specs = pl.BlockSpec((2, peaks_n, width, width), lambda j, i, f, ta, tb, r, o: (0, 0, 0, 0))
    else:
        out_shape = jax.ShapeDtypeStruct((peaks_n, blocks, width, width), jnp.float32)
        out_specs = part_spec
    return pl.pallas_call(
        kernel,
        grid_spec=pltpu.PrefetchScalarGridSpec(
            num_scalar_prefetch=5,
            grid=(blocks // per, n_steps),
            in_specs=in_specs,
            out_specs=out_specs,
            scratch_shapes=[pltpu.VMEM((peaks_n, per, width, width), jnp.float32), pltpu.VMEM((per * span, 2 * size), jnp.bfloat16),
                            pltpu.VMEM(col_table.shape, jnp.bfloat16), pltpu.SemaphoreType.DMA(())],
        ),
        out_shape=out_shape,
        compiler_params=pltpu.CompilerParams(dimension_semantics=("arbitrary", "arbitrary")),
        cost_estimate=cost,
    )(*args)


def local(tile_spectra, template_spectra, peaks, listed):
    size = tile_spectra.shape[3]
    width = W
    tiles = lax.axis_size("tile")
    rows_t = template_spectra.shape[2]
    tmpl = lax.all_gather(template_spectra, "tile", axis=0)
    block_size = tmpl.shape[1]
    spec = gather_rows(tile_spectra[0], "orient")
    spec = jnp.moveaxis(spec, 0, 1).reshape(2, size, size)
    freqs = jnp.arange(size, dtype=jnp.int32)
    cos_row, sin_row = angle_tables(freqs, peaks[0][:, 0], size, width)
    cos_t = jnp.swapaxes(cos_row, 1, 2)
    sin_t = jnp.swapaxes(sin_row, 1, 2)
    col_table = col_tables(peaks[0], size, width)
    listed_ids = listed[0]
    global_ids = lax.axis_index("orient") * block_size + jnp.arange(block_size, dtype=jnp.int32)
    is_listed = jnp.any(listed_ids[:, :, None] == global_ids[None, None, :], axis=1)
    flags = is_listed.astype(jnp.int32).reshape(-1)
    best_shape = (listed.shape[1], width, width)
    if rows_t % 128 != 0 or tiles % 2 != 0 or block_size % 2 != 0:
        best_part, power_part = match(flags, tmpl, spec, col_table, cos_t, sin_t)
    else:
        me = lax.axis_index("tile")
        sibling = lax.ppermute(template_spectra, "tile", xor_pairs(tiles, 1))
        chip = me // 2
        odd = (me % 2).astype(jnp.int32)
        zero = jnp.zeros((1,), jnp.int32)
        near_offs = jnp.stack([odd, 1 - odd]) * rows_t
        own, sib = template_spectra[None], sibling[None]
        partial = match_rows(flags, zero, zero, chip[None].astype(jnp.int32), near_offs, own, sib, spec, col_table, cos_t, sin_t)
        far = far_chips(chip, tiles // 2)
        far_offs = jnp.array([0, rows_t], jnp.int32)
        joined = match_rows(flags, far * 2, far * 2 + 1, far, far_offs, tmpl, tmpl, spec, col_table, cos_t, sin_t, init=partial)
        best_all, power_all = reduce_joined(joined.reshape(2, -1, width), best_shape, "orient")
        return (best_all[None], (power_all / LIST)[None])
    best_all, power_all = reduce_orient(best_part, power_part, "orient")
    return (best_all[None], (power_all / LIST)[None])


def far_chips(chip, chips):
    steps = jnp.arange(chips - 1, dtype=jnp.int32)
    return steps + (steps >= chip).astype(jnp.int32)


def solution(mesh):
    placed = (
        P("tile", None, "orient", None),
        P("orient", None, "tile", None),
        P("tile", None, None),
        P("tile", None, None),
    )
    return jax.shard_map(
        local,
        mesh=mesh,
        in_specs=placed,
        out_specs=(P("tile", None, None, None), P("tile", None, None, None)),
        check_vma=False,
    )
```

```python
import functools
import math

import jax
import jax.numpy as jnp
from jax import lax
from jax.experimental import pallas as pl
from jax.experimental.pallas import tpu as pltpu
from jax.sharding import PartitionSpec as P

W = 128
LIST = 48


lowest_score = -1e30


def xor_pairs(n, k):
    return [(i, i ^ k) for i in range(n)]


def is_pow2(n):
    return n & (n - 1) == 0


def angle_tables(freqs, coords, size, width):
    offsets = jnp.arange(width, dtype=jnp.int32) - width // 2
    position = (coords[:, None] + offsets[None, :]) % size
    phase = freqs[None, :, None] * position[:, None, :] % size
    angle = phase.astype(jnp.float32) * (2.0 * math.pi / size)
    return (jnp.cos(angle).astype(jnp.bfloat16), jnp.sin(angle).astype(jnp.bfloat16))


def col_tables(peak_rows, size, width):
    freqs = jnp.arange(size, dtype=jnp.int32)
    cos_col, sin_col = angle_tables(freqs, peak_rows[:, 1], size, width)
    upper = jnp.concatenate([cos_col, sin_col], axis=-1)
    lower = jnp.concatenate([-sin_col, cos_col], axis=-1)
    return jnp.concatenate([upper, lower], axis=1)


def gather_rows(part, axis):
    n = lax.axis_size(axis)
    if not is_pow2(n):
        return lax.all_gather(part, axis)
    me = lax.axis_index(axis)
    blocks = part[None]
    k = n // 2
    while k >= 1:
        got = lax.ppermute(blocks, axis, xor_pairs(n, k))
        blocks = jnp.concatenate([blocks, got])
        k //= 2
    want = jnp.arange(n, dtype=jnp.int32) ^ me
    return blocks[order_of(want, n)]


def order_of(want, count):
    steps = int(math.log2(count))
    slot = jnp.zeros_like(want)
    for j in range(steps):
        k = count >> (j + 1)
        hit = (want & k) != 0
        slot = slot | jnp.where(hit, 1 << j, 0)
    return slot


def reduce_orient(best_part, power_part, axis):
    n = lax.axis_size(axis)
    if not is_pow2(n):
        best = lax.pmax(best_part, axis)
        power = lax.psum(power_part, axis)
        return best, power
    width = best_part.shape[-1]
    joined = jnp.stack([best_part.reshape(-1, width), power_part.reshape(-1, width)], axis=0)
    return reduce_joined(joined, best_part.shape, axis)


def reduce_joined(joined, shape, axis):
    n = lax.axis_size(axis)
    rows = joined.shape[1]
    if not is_pow2(n) or n < 2 or rows % n != 0:
        best = lax.pmax(joined[0], axis)
        power = lax.psum(joined[1], axis)
        return best.reshape(shape), power.reshape(shape)
    me = lax.axis_index(axis)
    half = rows // 2
    bit = me % 2
    keep = lax.dynamic_slice_in_dim(joined, bit * half, half, axis=1)
    send = lax.dynamic_slice_in_dim(joined, (1 - bit) * half, half, axis=1)
    got = lax.ppermute(send, axis, xor_pairs(n, 1))
    cur = jnp.stack([jnp.maximum(keep[0], got[0]), keep[1] + got[1]])
    members = n // 2
    group = me // 2
    piece = half // members
    own = lax.dynamic_slice_in_dim(cur, group * piece, piece, axis=1)
    best, power = own[0], own[1]
    for m in range(1, members):
        out = lax.dynamic_slice_in_dim(cur, (group ^ m) * piece, piece, axis=1)
        got = lax.ppermute(out, axis, xor_pairs(n, 2 * m))
        best = jnp.maximum(best, got[0])
        power = power + got[1]
    done = jnp.stack([best, power])
    slots = [done] + [lax.ppermute(done, axis, xor_pairs(n, 2 * m)) for m in range(1, members)]
    pieces = jnp.stack(slots)[jnp.arange(members, dtype=jnp.int32) ^ group]
    mine = jnp.moveaxis(pieces, 0, 1).reshape(2, half, joined.shape[2])
    other = lax.ppermute(mine, axis, xor_pairs(n, 1))
    whole = jnp.where(bit == 1, jnp.concatenate([other, mine], axis=1), jnp.concatenate([mine, other], axis=1))
    return whole[0].reshape(shape), whole[1].reshape(shape)


def match_kernel(blocks, size, width, rows_t, tiles, peaks_n, l_ref, tm_ref, sp_ref, ct_ref, cr_ref, sr_ref, best_ref, pow_ref, m_ref):
    j = pl.program_id(0)

    @pl.when(j == 0)
    def _():
        best_ref[...] = jnp.full(best_ref.shape, lowest_score, jnp.float32)
        pow_ref[...] = jnp.zeros(pow_ref.shape, jnp.float32)

    for t in range(tiles):
        rows = pl.ds(t * rows_t, rows_t)
        image_re = sp_ref[0, rows, :].astype(jnp.float32)
        image_im = sp_ref[1, rows, :].astype(jnp.float32)
        tmpl_re = tm_ref[t, 0, 0].astype(jnp.float32)
        tmpl_im = tm_ref[t, 0, 1].astype(jnp.float32)
        m_ref[rows, pl.ds(0, size)] = (image_re * tmpl_re + image_im * tmpl_im).astype(jnp.bfloat16)
        m_ref[rows, pl.ds(size, size)] = (image_im * tmpl_re - image_re * tmpl_im).astype(jnp.bfloat16)

    for p in range(peaks_n):
        @pl.when(l_ref[p * blocks + j] > 0)
        def _():
            g = jnp.dot(m_ref[...], ct_ref[p], preferred_element_type=jnp.float32).astype(jnp.bfloat16)
            score = jnp.dot(cr_ref[p], g[:, :width], preferred_element_type=jnp.float32)
            score = score - jnp.dot(sr_ref[p], g[:, width:], preferred_element_type=jnp.float32)
            score = score / size
            best_ref[p] = jnp.maximum(best_ref[p], score)
            pow_ref[p] = pow_ref[p] + score * score


def match(flags, tmpl, spec, col_table, cos_t, sin_t):
    tiles, blocks, _, rows_t, size = tmpl.shape
    peaks_n, width = cos_t.shape[0], cos_t.shape[1]
    kernel = functools.partial(match_kernel, blocks, size, width, rows_t, tiles, peaks_n)
    flops = blocks * peaks_n * (2 * size * 2 * size * 2 * width + 2 * 2 * width * size * width)
    cost = pl.CostEstimate(flops=flops, transcendentals=0, bytes_accessed=tmpl.size * 2 + spec.size * 2 + col_table.size * 2)
    out = jax.ShapeDtypeStruct((peaks_n, width, width), jnp.float32)
    return pl.pallas_call(
        kernel,
        grid_spec=pltpu.PrefetchScalarGridSpec(
            num_scalar_prefetch=1,
            grid=(blocks,),
            in_specs=[
                pl.BlockSpec((tiles, 1, 2, rows_t, size), lambda j, l: (0, j, 0, 0, 0)),
                pl.BlockSpec((2, size, size), lambda j, l: (0, 0, 0)),
                pl.BlockSpec(col_table.shape, lambda j, l: (0, 0, 0)),
                pl.BlockSpec(cos_t.shape, lambda j, l: (0, 0, 0)),
                pl.BlockSpec(sin_t.shape, lambda j, l: (0, 0, 0)),
            ],
            out_specs=[
                pl.BlockSpec((peaks_n, width, width), lambda j, l: (0, 0, 0)),
                pl.BlockSpec((peaks_n, width, width), lambda j, l: (0, 0, 0)),
            ],
            scratch_shapes=[pltpu.VMEM((size, 2 * size), jnp.bfloat16)],
        ),
        out_shape=[out, out],
        compiler_params=pltpu.CompilerParams(dimension_semantics=("arbitrary",)),
        cost_estimate=cost,
    )(flags, tmpl, spec, col_table, cos_t, sin_t)


def rows_kernel(blocks, size, width, rows_t, peaks_n, chunk, n_steps, final, per, f_ref, ta_ref, tb_ref, rid_ref, off_ref, tma_ref, tmb_ref, sp_ref, ct_ref, cr_ref, sr_ref, *rest):
    if final:
        init_ref, out_ref, acc_ref, m_ref = rest
        best_ref, pow_ref = out_ref.at[0], out_ref.at[1]
    else:
        part_ref, acc_ref, m_ref = rest
    jj = pl.program_id(0)
    i = pl.program_id(1)
    span = 2 * rows_t

    if final:
        @pl.when((jj == 0) & (i == 0))
        def _():
            best_ref[...] = jnp.full(best_ref.shape, lowest_score, jnp.float32)
            pow_ref[...] = jnp.zeros(pow_ref.shape, jnp.float32)

        @pl.when(i == 0)
        def _():
            acc_ref[...] = init_ref[...]
    else:
        @pl.when(i == 0)
        def _():
            acc_ref[...] = jnp.zeros(acc_ref.shape, jnp.float32)

    for o in range(per):
        for u, tm_ref in enumerate((tma_ref, tmb_ref)):
            def mix(c, carry, u=u, o=o, tm_ref=tm_ref):
                row = pl.multiple_of(c * chunk, chunk)
                in_row = pl.multiple_of(off_ref[u] + c * chunk, chunk)
                out_row = pl.multiple_of(o * span + off_ref[u] + c * chunk, chunk)
                image_re = sp_ref[0, pl.ds(in_row, chunk), :].astype(jnp.float32)
                image_im = sp_ref[1, pl.ds(in_row, chunk), :].astype(jnp.float32)
                tmpl_re = tm_ref[0, o, 0, pl.ds(row, chunk), :].astype(jnp.float32)
                tmpl_im = tm_ref[0, o, 1, pl.ds(row, chunk), :].astype(jnp.float32)
                m_ref[pl.ds(out_row, chunk), pl.ds(0, size)] = (image_re * tmpl_re + image_im * tmpl_im).astype(jnp.bfloat16)
                m_ref[pl.ds(out_row, chunk), pl.ds(size, size)] = (image_im * tmpl_re - image_re * tmpl_im).astype(jnp.bfloat16)
                return carry

            lax.fori_loop(0, rows_t // chunk, mix, 0, unroll=4)

    for p in range(peaks_n):
        count = f_ref[p * blocks + per * jj]
        for o in range(1, per):
            count = count + f_ref[p * blocks + per * jj + o]

        @pl.when(count > 0)
        def _():
            g = jnp.dot(m_ref[...], ct_ref[p], preferred_element_type=jnp.float32).astype(jnp.bfloat16)
            for o in range(per):
                rows = slice(o * span, (o + 1) * span)
                part = jnp.dot(cr_ref[p], g[rows, :width], preferred_element_type=jnp.float32)
                part = part - jnp.dot(sr_ref[p], g[rows, width:], preferred_element_type=jnp.float32)
                acc_ref[p, o] = acc_ref[p, o] + part

    @pl.when(i == n_steps - 1)
    def _():
        if final:
            for p in range(peaks_n):
                for o in range(per):
                    @pl.when(f_ref[p * blocks + per * jj + o] > 0)
                    def _():
                        score = acc_ref[p, o] / size
                        best_ref[p] = jnp.maximum(best_ref[p], score)
                        pow_ref[p] = pow_ref[p] + score * score
        else:
            part_ref[...] = acc_ref[...]


def match_rows(flags, tas, tbs, rids, offs, tmpl_a, tmpl_b, spec, col_table, cos_t, sin_t, init=None):
    _, blocks, _, rows_t, size = tmpl_a.shape
    peaks_n, width = cos_t.shape[0], cos_t.shape[1]
    n_steps = tas.shape[0]
    final = init is not None
    chunk = math.gcd(rows_t, 16)
    span = 2 * rows_t
    per = 8 if blocks % 8 == 0 else (4 if blocks % 4 == 0 else 2)
    kernel = functools.partial(rows_kernel, blocks, size, width, rows_t, peaks_n, chunk, n_steps, final, per)
    flops = blocks * peaks_n * n_steps * (2 * span * 2 * size * 2 * width + 2 * 2 * width * span * width)
    cost = pl.CostEstimate(flops=flops, transcendentals=0, bytes_accessed=n_steps * blocks * 2 * span * size * 4 + col_table.size * 2)
    in_specs = [
        pl.BlockSpec((1, per, 2, rows_t, size), lambda j, i, f, ta, tb, r, o: (ta[i], j, 0, 0, 0)),
        pl.BlockSpec((1, per, 2, rows_t, size), lambda j, i, f, ta, tb, r, o: (tb[i], j, 0, 0, 0)),
        pl.BlockSpec((2, span, size), lambda j, i, f, ta, tb, r, o: (0, r[i], 0)),
        pl.BlockSpec(col_table.shape, lambda j, i, f, ta, tb, r, o: (0, 0, 0)),
        pl.BlockSpec((peaks_n, width, span), lambda j, i, f, ta, tb, r, o: (0, 0, r[i])),
        pl.BlockSpec((peaks_n, width, span), lambda j, i, f, ta, tb, r, o: (0, 0, r[i])),
    ]
    args = [flags, tas, tbs, rids, offs, tmpl_a, tmpl_b, spec, col_table, cos_t, sin_t]
    part_spec = pl.BlockSpec((peaks_n, per, width, width), lambda j, i, f, ta, tb, r, o: (0, j, 0, 0))
    if final:
        in_specs.append(part_spec)
        args.append(init)
        out_shape = jax.ShapeDtypeStruct((2, peaks_n, width, width), jnp.float32)
        out_specs = pl.BlockSpec((2, peaks_n, width, width), lambda j, i, f, ta, tb, r, o: (0, 0, 0, 0))
    else:
        out_shape = jax.ShapeDtypeStruct((peaks_n, blocks, width, width), jnp.float32)
        out_specs = part_spec
    return pl.pallas_call(
        kernel,
        grid_spec=pltpu.PrefetchScalarGridSpec(
            num_scalar_prefetch=5,
            grid=(blocks // per, n_steps),
            in_specs=in_specs,
            out_specs=out_specs,
            scratch_shapes=[pltpu.VMEM((peaks_n, per, width, width), jnp.float32), pltpu.VMEM((per * span, 2 * size), jnp.bfloat16)],
        ),
        out_shape=out_shape,
        compiler_params=pltpu.CompilerParams(dimension_semantics=("arbitrary", "arbitrary")),
        cost_estimate=cost,
    )(*args)


def local(tile_spectra, template_spectra, peaks, listed):
    size = tile_spectra.shape[3]
    width = W
    tiles = lax.axis_size("tile")
    rows_t = template_spectra.shape[2]
    tmpl = lax.all_gather(template_spectra, "tile", axis=0)
    block_size = tmpl.shape[1]
    spec = gather_rows(tile_spectra[0], "orient")
    spec = jnp.moveaxis(spec, 0, 1).reshape(2, size, size)
    freqs = jnp.arange(size, dtype=jnp.int32)
    cos_row, sin_row = angle_tables(freqs, peaks[0][:, 0], size, width)
    cos_t = jnp.swapaxes(cos_row, 1, 2)
    sin_t = jnp.swapaxes(sin_row, 1, 2)
    col_table = col_tables(peaks[0], size, width)
    listed_ids = listed[0]
    global_ids = lax.axis_index("orient") * block_size + jnp.arange(block_size, dtype=jnp.int32)
    is_listed = jnp.any(listed_ids[:, :, None] == global_ids[None, None, :], axis=1)
    flags = is_listed.astype(jnp.int32).reshape(-1)
    best_shape = (listed.shape[1], width, width)
    if rows_t % 128 != 0 or tiles % 2 != 0 or block_size % 2 != 0:
        best_part, power_part = match(flags, tmpl, spec, col_table, cos_t, sin_t)
    else:
        me = lax.axis_index("tile")
        sibling = lax.ppermute(template_spectra, "tile", xor_pairs(tiles, 1))
        chip = me // 2
        odd = (me % 2).astype(jnp.int32)
        zero = jnp.zeros((1,), jnp.int32)
        near_offs = jnp.stack([odd, 1 - odd]) * rows_t
        own, sib = template_spectra[None], sibling[None]
        partial = match_rows(flags, zero, zero, chip[None].astype(jnp.int32), near_offs, own, sib, spec, col_table, cos_t, sin_t)
        far = far_chips(chip, tiles // 2)
        far_offs = jnp.array([0, rows_t], jnp.int32)
        joined = match_rows(flags, far * 2, far * 2 + 1, far, far_offs, tmpl, tmpl, spec, col_table, cos_t, sin_t, init=partial)
        best_all, power_all = reduce_joined(joined.reshape(2, -1, width), best_shape, "orient")
        return (best_all[None], (power_all / LIST)[None])
    best_all, power_all = reduce_orient(best_part, power_part, "orient")
    return (best_all[None], (power_all / LIST)[None])


def far_chips(chip, chips):
    steps = jnp.arange(chips - 1, dtype=jnp.int32)
    return steps + (steps >= chip).astype(jnp.int32)


def solution(mesh):
    placed = (
        P("tile", None, "orient", None),
        P("orient", None, "tile", None),
        P("tile", None, None),
        P("tile", None, None),
    )
    return jax.shard_map(
        local,
        mesh=mesh,
        in_specs=placed,
        out_specs=(P("tile", None, None, None), P("tile", None, None, None)),
        check_vma=False,
    )
```

```python
import functools
import math

import jax
import jax.numpy as jnp
from jax import lax
from jax.experimental import pallas as pl
from jax.experimental.pallas import tpu as pltpu
from jax.sharding import PartitionSpec as P

W = 128
LIST = 48


lowest_score = -1e30


def xor_pairs(n, k):
    return [(i, i ^ k) for i in range(n)]


def is_pow2(n):
    return n & (n - 1) == 0


def angle_tables(freqs, coords, size, width):
    offsets = jnp.arange(width, dtype=jnp.int32) - width // 2
    position = (coords[:, None] + offsets[None, :]) % size
    phase = freqs[None, :, None] * position[:, None, :] % size
    angle = phase.astype(jnp.float32) * (2.0 * math.pi / size)
    return (jnp.cos(angle).astype(jnp.bfloat16), jnp.sin(angle).astype(jnp.bfloat16))


def col_tables(peak_rows, size, width):
    freqs = jnp.arange(size, dtype=jnp.int32)
    cos_col, sin_col = angle_tables(freqs, peak_rows[:, 1], size, width)
    upper = jnp.concatenate([cos_col, sin_col], axis=-1)
    lower = jnp.concatenate([-sin_col, cos_col], axis=-1)
    return jnp.concatenate([upper, lower], axis=1)


def gather_rows(part, axis):
    n = lax.axis_size(axis)
    if not is_pow2(n):
        return lax.all_gather(part, axis)
    me = lax.axis_index(axis)
    blocks = part[None]
    k = n // 2
    while k >= 1:
        got = lax.ppermute(blocks, axis, xor_pairs(n, k))
        blocks = jnp.concatenate([blocks, got])
        k //= 2
    want = jnp.arange(n, dtype=jnp.int32) ^ me
    return blocks[order_of(want, n)]


def order_of(want, count):
    steps = int(math.log2(count))
    slot = jnp.zeros_like(want)
    for j in range(steps):
        k = count >> (j + 1)
        hit = (want & k) != 0
        slot = slot | jnp.where(hit, 1 << j, 0)
    return slot


def reduce_orient(best_part, power_part, axis):
    n = lax.axis_size(axis)
    if not is_pow2(n):
        best = lax.pmax(best_part, axis)
        power = lax.psum(power_part, axis)
        return best, power
    width = best_part.shape[-1]
    joined = jnp.stack([best_part.reshape(-1, width), power_part.reshape(-1, width)], axis=0)
    return reduce_joined(joined, best_part.shape, axis)


def reduce_joined(joined, shape, axis):
    n = lax.axis_size(axis)
    rows = joined.shape[1]
    if not is_pow2(n) or n < 2 or rows % n != 0:
        best = lax.pmax(joined[0], axis)
        power = lax.psum(joined[1], axis)
        return best.reshape(shape), power.reshape(shape)
    me = lax.axis_index(axis)
    bit = me % 2
    members = n // 2
    group = me // 2
    quarter = rows // members
    own = lax.dynamic_slice_in_dim(joined, group * quarter, quarter, axis=1)
    best, power = own[0], own[1]
    for m in range(1, members):
        out = lax.dynamic_slice_in_dim(joined, (group ^ m) * quarter, quarter, axis=1)
        got = lax.ppermute(out, axis, xor_pairs(n, 2 * m))
        best = jnp.maximum(best, got[0])
        power = power + got[1]
    cur = jnp.stack([best, power])
    half = quarter // 2
    keep = lax.dynamic_slice_in_dim(cur, bit * half, half, axis=1)
    send = lax.dynamic_slice_in_dim(cur, (1 - bit) * half, half, axis=1)
    got = lax.ppermute(send, axis, xor_pairs(n, 1))
    done = jnp.stack([jnp.maximum(keep[0], got[0]), keep[1] + got[1]])
    other = lax.ppermute(done, axis, xor_pairs(n, 1))
    mine = jnp.where(bit == 1, jnp.concatenate([other, done], axis=1), jnp.concatenate([done, other], axis=1))
    slots = [mine] + [lax.ppermute(mine, axis, xor_pairs(n, 2 * m)) for m in range(1, members)]
    pieces = jnp.stack(slots)[jnp.arange(members, dtype=jnp.int32) ^ group]
    whole = jnp.moveaxis(pieces, 0, 1).reshape(2, rows, joined.shape[2])
    return whole[0].reshape(shape), whole[1].reshape(shape)


def match_kernel(blocks, size, width, rows_t, tiles, peaks_n, l_ref, tm_ref, sp_ref, ct_ref, cr_ref, sr_ref, best_ref, pow_ref, m_ref):
    j = pl.program_id(0)

    @pl.when(j == 0)
    def _():
        best_ref[...] = jnp.full(best_ref.shape, lowest_score, jnp.float32)
        pow_ref[...] = jnp.zeros(pow_ref.shape, jnp.float32)

    for t in range(tiles):
        rows = pl.ds(t * rows_t, rows_t)
        image_re = sp_ref[0, rows, :].astype(jnp.float32)
        image_im = sp_ref[1, rows, :].astype(jnp.float32)
        tmpl_re = tm_ref[t, 0, 0].astype(jnp.float32)
        tmpl_im = tm_ref[t, 0, 1].astype(jnp.float32)
        m_ref[rows, pl.ds(0, size)] = (image_re * tmpl_re + image_im * tmpl_im).astype(jnp.bfloat16)
        m_ref[rows, pl.ds(size, size)] = (image_im * tmpl_re - image_re * tmpl_im).astype(jnp.bfloat16)

    for p in range(peaks_n):
        @pl.when(l_ref[p * blocks + j] > 0)
        def _():
            g = jnp.dot(m_ref[...], ct_ref[p], preferred_element_type=jnp.float32).astype(jnp.bfloat16)
            score = jnp.dot(cr_ref[p], g[:, :width], preferred_element_type=jnp.float32)
            score = score - jnp.dot(sr_ref[p], g[:, width:], preferred_element_type=jnp.float32)
            score = score / size
            best_ref[p] = jnp.maximum(best_ref[p], score)
            pow_ref[p] = pow_ref[p] + score * score


def match(flags, tmpl, spec, col_table, cos_t, sin_t):
    tiles, blocks, _, rows_t, size = tmpl.shape
    peaks_n, width = cos_t.shape[0], cos_t.shape[1]
    kernel = functools.partial(match_kernel, blocks, size, width, rows_t, tiles, peaks_n)
    flops = blocks * peaks_n * (2 * size * 2 * size * 2 * width + 2 * 2 * width * size * width)
    cost = pl.CostEstimate(flops=flops, transcendentals=0, bytes_accessed=tmpl.size * 2 + spec.size * 2 + col_table.size * 2)
    out = jax.ShapeDtypeStruct((peaks_n, width, width), jnp.float32)
    return pl.pallas_call(
        kernel,
        grid_spec=pltpu.PrefetchScalarGridSpec(
            num_scalar_prefetch=1,
            grid=(blocks,),
            in_specs=[
                pl.BlockSpec((tiles, 1, 2, rows_t, size), lambda j, l: (0, j, 0, 0, 0)),
                pl.BlockSpec((2, size, size), lambda j, l: (0, 0, 0)),
                pl.BlockSpec(col_table.shape, lambda j, l: (0, 0, 0)),
                pl.BlockSpec(cos_t.shape, lambda j, l: (0, 0, 0)),
                pl.BlockSpec(sin_t.shape, lambda j, l: (0, 0, 0)),
            ],
            out_specs=[
                pl.BlockSpec((peaks_n, width, width), lambda j, l: (0, 0, 0)),
                pl.BlockSpec((peaks_n, width, width), lambda j, l: (0, 0, 0)),
            ],
            scratch_shapes=[pltpu.VMEM((size, 2 * size), jnp.bfloat16)],
        ),
        out_shape=[out, out],
        compiler_params=pltpu.CompilerParams(dimension_semantics=("arbitrary",)),
        cost_estimate=cost,
    )(flags, tmpl, spec, col_table, cos_t, sin_t)


def rows_kernel(blocks, size, width, rows_t, peaks_n, chunk, n_steps, final, per, f_ref, ta_ref, tb_ref, rid_ref, off_ref, tma_ref, tmb_ref, sp_ref, ct_ref, cr_ref, sr_ref, *rest):
    if final:
        init_ref, out_ref, acc_ref, m_ref = rest
        best_ref, pow_ref = out_ref.at[0], out_ref.at[1]
    else:
        part_ref, acc_ref, m_ref = rest
    jj = pl.program_id(0)
    i = pl.program_id(1)
    span = 2 * rows_t

    if final:
        @pl.when((jj == 0) & (i == 0))
        def _():
            best_ref[...] = jnp.full(best_ref.shape, lowest_score, jnp.float32)
            pow_ref[...] = jnp.zeros(pow_ref.shape, jnp.float32)

        @pl.when(i == 0)
        def _():
            acc_ref[...] = init_ref[...]
    else:
        @pl.when(i == 0)
        def _():
            acc_ref[...] = jnp.zeros(acc_ref.shape, jnp.float32)

    for o in range(per):
        for u, tm_ref in enumerate((tma_ref, tmb_ref)):
            def mix(c, carry, u=u, o=o, tm_ref=tm_ref):
                row = pl.multiple_of(c * chunk, chunk)
                in_row = pl.multiple_of(off_ref[u] + c * chunk, chunk)
                out_row = pl.multiple_of(o * span + off_ref[u] + c * chunk, chunk)
                image_re = sp_ref[0, pl.ds(in_row, chunk), :].astype(jnp.float32)
                image_im = sp_ref[1, pl.ds(in_row, chunk), :].astype(jnp.float32)
                tmpl_re = tm_ref[0, o, 0, pl.ds(row, chunk), :].astype(jnp.float32)
                tmpl_im = tm_ref[0, o, 1, pl.ds(row, chunk), :].astype(jnp.float32)
                m_ref[pl.ds(out_row, chunk), pl.ds(0, size)] = (image_re * tmpl_re + image_im * tmpl_im).astype(jnp.bfloat16)
                m_ref[pl.ds(out_row, chunk), pl.ds(size, size)] = (image_im * tmpl_re - image_re * tmpl_im).astype(jnp.bfloat16)
                return carry

            lax.fori_loop(0, rows_t // chunk, mix, 0, unroll=4)

    for p in range(peaks_n):
        count = f_ref[p * blocks + per * jj]
        for o in range(1, per):
            count = count + f_ref[p * blocks + per * jj + o]

        @pl.when(count > 0)
        def _():
            g = jnp.dot(m_ref[...], ct_ref[p], preferred_element_type=jnp.float32).astype(jnp.bfloat16)
            for o in range(per):
                rows = slice(o * span, (o + 1) * span)
                part = jnp.dot(cr_ref[p], g[rows, :width], preferred_element_type=jnp.float32)
                part = part - jnp.dot(sr_ref[p], g[rows, width:], preferred_element_type=jnp.float32)
                acc_ref[p, o] = acc_ref[p, o] + part

    @pl.when(i == n_steps - 1)
    def _():
        if final:
            for p in range(peaks_n):
                for o in range(per):
                    @pl.when(f_ref[p * blocks + per * jj + o] > 0)
                    def _():
                        score = acc_ref[p, o] / size
                        best_ref[p] = jnp.maximum(best_ref[p], score)
                        pow_ref[p] = pow_ref[p] + score * score
        else:
            part_ref[...] = acc_ref[...]


def match_rows(flags, tas, tbs, rids, offs, tmpl_a, tmpl_b, spec, col_table, cos_t, sin_t, init=None):
    _, blocks, _, rows_t, size = tmpl_a.shape
    peaks_n, width = cos_t.shape[0], cos_t.shape[1]
    n_steps = tas.shape[0]
    final = init is not None
    chunk = math.gcd(rows_t, 16)
    span = 2 * rows_t
    per = 4 if blocks % 4 == 0 else 2
    kernel = functools.partial(rows_kernel, blocks, size, width, rows_t, peaks_n, chunk, n_steps, final, per)
    flops = blocks * peaks_n * n_steps * (2 * span * 2 * size * 2 * width + 2 * 2 * width * span * width)
    cost = pl.CostEstimate(flops=flops, transcendentals=0, bytes_accessed=n_steps * blocks * 2 * span * size * 4 + col_table.size * 2)
    in_specs = [
        pl.BlockSpec((1, per, 2, rows_t, size), lambda j, i, f, ta, tb, r, o: (ta[i], j, 0, 0, 0)),
        pl.BlockSpec((1, per, 2, rows_t, size), lambda j, i, f, ta, tb, r, o: (tb[i], j, 0, 0, 0)),
        pl.BlockSpec((2, span, size), lambda j, i, f, ta, tb, r, o: (0, r[i], 0)),
        pl.BlockSpec(col_table.shape, lambda j, i, f, ta, tb, r, o: (0, 0, 0)),
        pl.BlockSpec((peaks_n, width, span), lambda j, i, f, ta, tb, r, o: (0, 0, r[i])),
        pl.BlockSpec((peaks_n, width, span), lambda j, i, f, ta, tb, r, o: (0, 0, r[i])),
    ]
    args = [flags, tas, tbs, rids, offs, tmpl_a, tmpl_b, spec, col_table, cos_t, sin_t]
    part_spec = pl.BlockSpec((peaks_n, per, width, width), lambda j, i, f, ta, tb, r, o: (0, j, 0, 0))
    if final:
        in_specs.append(part_spec)
        args.append(init)
        out_shape = jax.ShapeDtypeStruct((2, peaks_n, width, width), jnp.float32)
        out_specs = pl.BlockSpec((2, peaks_n, width, width), lambda j, i, f, ta, tb, r, o: (0, 0, 0, 0))
    else:
        out_shape = jax.ShapeDtypeStruct((peaks_n, blocks, width, width), jnp.float32)
        out_specs = part_spec
    return pl.pallas_call(
        kernel,
        grid_spec=pltpu.PrefetchScalarGridSpec(
            num_scalar_prefetch=5,
            grid=(blocks // per, n_steps),
            in_specs=in_specs,
            out_specs=out_specs,
            scratch_shapes=[pltpu.VMEM((peaks_n, per, width, width), jnp.float32), pltpu.VMEM((per * span, 2 * size), jnp.bfloat16)],
        ),
        out_shape=out_shape,
        compiler_params=pltpu.CompilerParams(dimension_semantics=("arbitrary", "arbitrary")),
        cost_estimate=cost,
    )(*args)


def local(tile_spectra, template_spectra, peaks, listed):
    size = tile_spectra.shape[3]
    width = W
    tiles = lax.axis_size("tile")
    rows_t = template_spectra.shape[2]
    tmpl = lax.all_gather(template_spectra, "tile", axis=0)
    block_size = tmpl.shape[1]
    spec = gather_rows(tile_spectra[0], "orient")
    spec = jnp.moveaxis(spec, 0, 1).reshape(2, size, size)
    freqs = jnp.arange(size, dtype=jnp.int32)
    cos_row, sin_row = angle_tables(freqs, peaks[0][:, 0], size, width)
    cos_t = jnp.swapaxes(cos_row, 1, 2)
    sin_t = jnp.swapaxes(sin_row, 1, 2)
    col_table = col_tables(peaks[0], size, width)
    listed_ids = listed[0]
    global_ids = lax.axis_index("orient") * block_size + jnp.arange(block_size, dtype=jnp.int32)
    is_listed = jnp.any(listed_ids[:, :, None] == global_ids[None, None, :], axis=1)
    flags = is_listed.astype(jnp.int32).reshape(-1)
    best_shape = (listed.shape[1], width, width)
    if rows_t % 128 != 0 or tiles % 2 != 0 or block_size % 2 != 0:
        best_part, power_part = match(flags, tmpl, spec, col_table, cos_t, sin_t)
    else:
        me = lax.axis_index("tile")
        sibling = lax.ppermute(template_spectra, "tile", xor_pairs(tiles, 1))
        chip = me // 2
        odd = (me % 2).astype(jnp.int32)
        zero = jnp.zeros((1,), jnp.int32)
        near_offs = jnp.stack([odd, 1 - odd]) * rows_t
        own, sib = template_spectra[None], sibling[None]
        partial = match_rows(flags, zero, zero, chip[None].astype(jnp.int32), near_offs, own, sib, spec, col_table, cos_t, sin_t)
        far = far_chips(chip, tiles // 2)
        far_offs = jnp.array([0, rows_t], jnp.int32)
        joined = match_rows(flags, far * 2, far * 2 + 1, far, far_offs, tmpl, tmpl, spec, col_table, cos_t, sin_t, init=partial)
        best_all, power_all = reduce_joined(joined.reshape(2, -1, width), best_shape, "orient")
        return (best_all[None], (power_all / LIST)[None])
    best_all, power_all = reduce_orient(best_part, power_part, "orient")
    return (best_all[None], (power_all / LIST)[None])


def far_chips(chip, chips):
    steps = jnp.arange(chips - 1, dtype=jnp.int32)
    return steps + (steps >= chip).astype(jnp.int32)


def solution(mesh):
    placed = (
        P("tile", None, "orient", None),
        P("orient", None, "tile", None),
        P("tile", None, None),
        P("tile", None, None),
    )
    return jax.shard_map(
        local,
        mesh=mesh,
        in_specs=placed,
        out_specs=(P("tile", None, None, None), P("tile", None, None, None)),
        check_vma=False,
    )
```

```python
import functools
import math

import jax
import jax.numpy as jnp
from jax import lax
from jax.experimental import pallas as pl
from jax.experimental.pallas import tpu as pltpu
from jax.sharding import PartitionSpec as P

W = 128
LIST = 48


lowest_score = -1e30


def xor_pairs(n, k):
    return [(i, i ^ k) for i in range(n)]


def is_pow2(n):
    return n & (n - 1) == 0


def angle_tables(freqs, coords, size, width):
    offsets = jnp.arange(width, dtype=jnp.int32) - width // 2
    position = (coords[:, None] + offsets[None, :]) % size
    phase = freqs[None, :, None] * position[:, None, :] % size
    angle = phase.astype(jnp.float32) * (2.0 * math.pi / size)
    return (jnp.cos(angle).astype(jnp.bfloat16), jnp.sin(angle).astype(jnp.bfloat16))


def col_tables(peak_rows, size, width):
    freqs = jnp.arange(size, dtype=jnp.int32)
    cos_col, sin_col = angle_tables(freqs, peak_rows[:, 1], size, width)
    upper = jnp.concatenate([cos_col, sin_col], axis=-1)
    lower = jnp.concatenate([-sin_col, cos_col], axis=-1)
    return jnp.concatenate([upper, lower], axis=1)


def gather_rows(part, axis):
    n = lax.axis_size(axis)
    if not is_pow2(n):
        return lax.all_gather(part, axis)
    me = lax.axis_index(axis)
    blocks = part[None]
    k = n // 2
    while k >= 1:
        got = lax.ppermute(blocks, axis, xor_pairs(n, k))
        blocks = jnp.concatenate([blocks, got])
        k //= 2
    want = jnp.arange(n, dtype=jnp.int32) ^ me
    return blocks[order_of(want, n)]


def order_of(want, count):
    steps = int(math.log2(count))
    slot = jnp.zeros_like(want)
    for j in range(steps):
        k = count >> (j + 1)
        hit = (want & k) != 0
        slot = slot | jnp.where(hit, 1 << j, 0)
    return slot


def reduce_orient(best_part, power_part, axis, scale):
    n = lax.axis_size(axis)
    if not is_pow2(n):
        best = lax.pmax(best_part, axis)
        power = lax.psum(power_part, axis)
        return best, power / scale
    width = best_part.shape[-1]
    joined = jnp.stack([best_part.reshape(-1, width), power_part.reshape(-1, width)], axis=0)
    return reduce_joined(joined, best_part.shape, axis, scale)


def reduce_joined(joined, shape, axis, scale):
    n = lax.axis_size(axis)
    rows = joined.shape[1]
    if not is_pow2(n) or n < 2 or rows % n != 0:
        best = lax.pmax(joined[0], axis)
        power = lax.psum(joined[1], axis) / scale
        return best.reshape(shape), power.reshape(shape)
    me = lax.axis_index(axis)
    half = rows // 2
    bit = me % 2
    keep = lax.dynamic_slice_in_dim(joined, bit * half, half, axis=1)
    send = lax.dynamic_slice_in_dim(joined, (1 - bit) * half, half, axis=1)
    got = lax.ppermute(send, axis, xor_pairs(n, 1))
    cur = jnp.stack([jnp.maximum(keep[0], got[0]), keep[1] + got[1]])
    members = n // 2
    group = me // 2
    piece = half // members
    own = lax.dynamic_slice_in_dim(cur, group * piece, piece, axis=1)
    best, power = own[0], own[1]
    for m in range(1, members):
        out = lax.dynamic_slice_in_dim(cur, (group ^ m) * piece, piece, axis=1)
        got = lax.ppermute(out, axis, xor_pairs(n, 2 * m))
        best = jnp.maximum(best, got[0])
        power = power + got[1]
    done = jnp.stack([best, power / scale])
    slots = [done] + [lax.ppermute(done, axis, xor_pairs(n, 2 * m)) for m in range(1, members)]
    pieces = jnp.stack(slots)[jnp.arange(members, dtype=jnp.int32) ^ group]
    mine = jnp.moveaxis(pieces, 0, 1).reshape(2, half, joined.shape[2])
    other = lax.ppermute(mine, axis, xor_pairs(n, 1))
    whole = jnp.where(bit == 1, jnp.concatenate([other, mine], axis=1), jnp.concatenate([mine, other], axis=1))
    return whole[0].reshape(shape), whole[1].reshape(shape)


def match_kernel(blocks, size, width, rows_t, tiles, peaks_n, l_ref, tm_ref, sp_ref, ct_ref, cr_ref, sr_ref, best_ref, pow_ref, m_ref):
    j = pl.program_id(0)

    @pl.when(j == 0)
    def _():
        best_ref[...] = jnp.full(best_ref.shape, lowest_score, jnp.float32)
        pow_ref[...] = jnp.zeros(pow_ref.shape, jnp.float32)

    for t in range(tiles):
        rows = pl.ds(t * rows_t, rows_t)
        image_re = sp_ref[0, rows, :].astype(jnp.float32)
        image_im = sp_ref[1, rows, :].astype(jnp.float32)
        tmpl_re = tm_ref[t, 0, 0].astype(jnp.float32)
        tmpl_im = tm_ref[t, 0, 1].astype(jnp.float32)
        m_ref[rows, pl.ds(0, size)] = (image_re * tmpl_re + image_im * tmpl_im).astype(jnp.bfloat16)
        m_ref[rows, pl.ds(size, size)] = (image_im * tmpl_re - image_re * tmpl_im).astype(jnp.bfloat16)

    for p in range(peaks_n):
        @pl.when(l_ref[p * blocks + j] > 0)
        def _():
            g = jnp.dot(m_ref[...], ct_ref[p], preferred_element_type=jnp.float32).astype(jnp.bfloat16)
            score = jnp.dot(cr_ref[p], g[:, :width], preferred_element_type=jnp.float32)
            score = score - jnp.dot(sr_ref[p], g[:, width:], preferred_element_type=jnp.float32)
            score = score / size
            best_ref[p] = jnp.maximum(best_ref[p], score)
            pow_ref[p] = pow_ref[p] + score * score


def match(flags, tmpl, spec, col_table, cos_t, sin_t):
    tiles, blocks, _, rows_t, size = tmpl.shape
    peaks_n, width = cos_t.shape[0], cos_t.shape[1]
    kernel = functools.partial(match_kernel, blocks, size, width, rows_t, tiles, peaks_n)
    flops = blocks * peaks_n * (2 * size * 2 * size * 2 * width + 2 * 2 * width * size * width)
    cost = pl.CostEstimate(flops=flops, transcendentals=0, bytes_accessed=tmpl.size * 2 + spec.size * 2 + col_table.size * 2)
    out = jax.ShapeDtypeStruct((peaks_n, width, width), jnp.float32)
    return pl.pallas_call(
        kernel,
        grid_spec=pltpu.PrefetchScalarGridSpec(
            num_scalar_prefetch=1,
            grid=(blocks,),
            in_specs=[
                pl.BlockSpec((tiles, 1, 2, rows_t, size), lambda j, l: (0, j, 0, 0, 0)),
                pl.BlockSpec((2, size, size), lambda j, l: (0, 0, 0)),
                pl.BlockSpec(col_table.shape, lambda j, l: (0, 0, 0)),
                pl.BlockSpec(cos_t.shape, lambda j, l: (0, 0, 0)),
                pl.BlockSpec(sin_t.shape, lambda j, l: (0, 0, 0)),
            ],
            out_specs=[
                pl.BlockSpec((peaks_n, width, width), lambda j, l: (0, 0, 0)),
                pl.BlockSpec((peaks_n, width, width), lambda j, l: (0, 0, 0)),
            ],
            scratch_shapes=[pltpu.VMEM((size, 2 * size), jnp.bfloat16)],
        ),
        out_shape=[out, out],
        compiler_params=pltpu.CompilerParams(dimension_semantics=("arbitrary",)),
        cost_estimate=cost,
    )(flags, tmpl, spec, col_table, cos_t, sin_t)


def rows_kernel(blocks, size, width, rows_t, peaks_n, chunk, n_steps, final, per, f_ref, ta_ref, tb_ref, rid_ref, off_ref, tma_ref, tmb_ref, sp_ref, ct_ref, cr_ref, sr_ref, *rest):
    if final:
        init_ref, out_ref, acc_ref, m_ref = rest
        best_ref, pow_ref = out_ref.at[0], out_ref.at[1]
    else:
        part_ref, acc_ref, m_ref = rest
    jj = pl.program_id(0)
    i = pl.program_id(1)
    span = 2 * rows_t

    if final:
        @pl.when((jj == 0) & (i == 0))
        def _():
            best_ref[...] = jnp.full(best_ref.shape, lowest_score, jnp.float32)
            pow_ref[...] = jnp.zeros(pow_ref.shape, jnp.float32)

        @pl.when(i == 0)
        def _():
            acc_ref[...] = init_ref[...]
    else:
        @pl.when(i == 0)
        def _():
            acc_ref[...] = jnp.zeros(acc_ref.shape, jnp.float32)

    for o in range(per):
        for u, tm_ref in enumerate((tma_ref, tmb_ref)):
            def mix(c, carry, u=u, o=o, tm_ref=tm_ref):
                row = pl.multiple_of(c * chunk, chunk)
                in_row = pl.multiple_of(off_ref[u] + c * chunk, chunk)
                out_row = pl.multiple_of(o * span + off_ref[u] + c * chunk, chunk)
                image_re = sp_ref[0, pl.ds(in_row, chunk), :].astype(jnp.float32)
                image_im = sp_ref[1, pl.ds(in_row, chunk), :].astype(jnp.float32)
                tmpl_re = tm_ref[0, o, 0, pl.ds(row, chunk), :].astype(jnp.float32)
                tmpl_im = tm_ref[0, o, 1, pl.ds(row, chunk), :].astype(jnp.float32)
                m_ref[pl.ds(out_row, chunk), pl.ds(0, size)] = (image_re * tmpl_re + image_im * tmpl_im).astype(jnp.bfloat16)
                m_ref[pl.ds(out_row, chunk), pl.ds(size, size)] = (image_im * tmpl_re - image_re * tmpl_im).astype(jnp.bfloat16)
                return carry

            lax.fori_loop(0, rows_t // chunk, mix, 0, unroll=4)

    for p in range(peaks_n):
        count = f_ref[p * blocks + per * jj]
        for o in range(1, per):
            count = count + f_ref[p * blocks + per * jj + o]

        @pl.when(count > 0)
        def _():
            g = jnp.dot(m_ref[...], ct_ref[p], preferred_element_type=jnp.float32).astype(jnp.bfloat16)
            for o in range(per):
                rows = slice(o * span, (o + 1) * span)
                part = jnp.dot(cr_ref[p], g[rows, :width], preferred_element_type=jnp.float32)
                part = part - jnp.dot(sr_ref[p], g[rows, width:], preferred_element_type=jnp.float32)
                acc_ref[p, o] = acc_ref[p, o] + part

    @pl.when(i == n_steps - 1)
    def _():
        if final:
            for p in range(peaks_n):
                for o in range(per):
                    @pl.when(f_ref[p * blocks + per * jj + o] > 0)
                    def _():
                        score = acc_ref[p, o] / size
                        best_ref[p] = jnp.maximum(best_ref[p], score)
                        pow_ref[p] = pow_ref[p] + score * score
        else:
            part_ref[...] = acc_ref[...]


def match_rows(flags, tas, tbs, rids, offs, tmpl_a, tmpl_b, spec, col_table, cos_t, sin_t, init=None):
    _, blocks, _, rows_t, size = tmpl_a.shape
    peaks_n, width = cos_t.shape[0], cos_t.shape[1]
    n_steps = tas.shape[0]
    final = init is not None
    chunk = math.gcd(rows_t, 16)
    span = 2 * rows_t
    per = 4 if blocks % 4 == 0 else 2
    kernel = functools.partial(rows_kernel, blocks, size, width, rows_t, peaks_n, chunk, n_steps, final, per)
    flops = blocks * peaks_n * n_steps * (2 * span * 2 * size * 2 * width + 2 * 2 * width * span * width)
    cost = pl.CostEstimate(flops=flops, transcendentals=0, bytes_accessed=n_steps * blocks * 2 * span * size * 4 + col_table.size * 2)
    in_specs = [
        pl.BlockSpec((1, per, 2, rows_t, size), lambda j, i, f, ta, tb, r, o: (ta[i], j, 0, 0, 0)),
        pl.BlockSpec((1, per, 2, rows_t, size), lambda j, i, f, ta, tb, r, o: (tb[i], j, 0, 0, 0)),
        pl.BlockSpec((2, span, size), lambda j, i, f, ta, tb, r, o: (0, r[i], 0)),
        pl.BlockSpec(col_table.shape, lambda j, i, f, ta, tb, r, o: (0, 0, 0)),
        pl.BlockSpec((peaks_n, width, span), lambda j, i, f, ta, tb, r, o: (0, 0, r[i])),
        pl.BlockSpec((peaks_n, width, span), lambda j, i, f, ta, tb, r, o: (0, 0, r[i])),
    ]
    args = [flags, tas, tbs, rids, offs, tmpl_a, tmpl_b, spec, col_table, cos_t, sin_t]
    part_spec = pl.BlockSpec((peaks_n, per, width, width), lambda j, i, f, ta, tb, r, o: (0, j, 0, 0))
    if final:
        in_specs.append(part_spec)
        args.append(init)
        out_shape = jax.ShapeDtypeStruct((2, peaks_n, width, width), jnp.float32)
        out_specs = pl.BlockSpec((2, peaks_n, width, width), lambda j, i, f, ta, tb, r, o: (0, 0, 0, 0))
    else:
        out_shape = jax.ShapeDtypeStruct((peaks_n, blocks, width, width), jnp.float32)
        out_specs = part_spec
    return pl.pallas_call(
        kernel,
        grid_spec=pltpu.PrefetchScalarGridSpec(
            num_scalar_prefetch=5,
            grid=(blocks // per, n_steps),
            in_specs=in_specs,
            out_specs=out_specs,
            scratch_shapes=[pltpu.VMEM((peaks_n, per, width, width), jnp.float32), pltpu.VMEM((per * span, 2 * size), jnp.bfloat16)],
        ),
        out_shape=out_shape,
        compiler_params=pltpu.CompilerParams(dimension_semantics=("arbitrary", "arbitrary")),
        cost_estimate=cost,
    )(*args)


def local(tile_spectra, template_spectra, peaks, listed):
    size = tile_spectra.shape[3]
    width = W
    tiles = lax.axis_size("tile")
    rows_t = template_spectra.shape[2]
    tmpl = lax.all_gather(template_spectra, "tile", axis=0)
    block_size = tmpl.shape[1]
    spec = gather_rows(tile_spectra[0], "orient")
    spec = jnp.moveaxis(spec, 0, 1).reshape(2, size, size)
    freqs = jnp.arange(size, dtype=jnp.int32)
    cos_row, sin_row = angle_tables(freqs, peaks[0][:, 0], size, width)
    cos_t = jnp.swapaxes(cos_row, 1, 2)
    sin_t = jnp.swapaxes(sin_row, 1, 2)
    col_table = col_tables(peaks[0], size, width)
    listed_ids = listed[0]
    global_ids = lax.axis_index("orient") * block_size + jnp.arange(block_size, dtype=jnp.int32)
    is_listed = jnp.any(listed_ids[:, :, None] == global_ids[None, None, :], axis=1)
    flags = is_listed.astype(jnp.int32).reshape(-1)
    best_shape = (listed.shape[1], width, width)
    if rows_t % 128 != 0 or tiles % 2 != 0 or block_size % 2 != 0:
        best_part, power_part = match(flags, tmpl, spec, col_table, cos_t, sin_t)
    else:
        me = lax.axis_index("tile")
        sibling = lax.ppermute(template_spectra, "tile", xor_pairs(tiles, 1))
        chip = me // 2
        odd = (me % 2).astype(jnp.int32)
        zero = jnp.zeros((1,), jnp.int32)
        near_offs = jnp.stack([odd, 1 - odd]) * rows_t
        own, sib = template_spectra[None], sibling[None]
        partial = match_rows(flags, zero, zero, chip[None].astype(jnp.int32), near_offs, own, sib, spec, col_table, cos_t, sin_t)
        far = far_chips(chip, tiles // 2)
        far_offs = jnp.array([0, rows_t], jnp.int32)
        joined = match_rows(flags, far * 2, far * 2 + 1, far, far_offs, tmpl, tmpl, spec, col_table, cos_t, sin_t, init=partial)
        best_all, power_all = reduce_joined(joined.reshape(2, -1, width), best_shape, "orient", LIST)
        return (best_all[None], power_all[None])
    best_all, power_all = reduce_orient(best_part, power_part, "orient", LIST)
    return (best_all[None], power_all[None])


def far_chips(chip, chips):
    steps = jnp.arange(chips - 1, dtype=jnp.int32)
    return steps + (steps >= chip).astype(jnp.int32)


def solution(mesh):
    placed = (
        P("tile", None, "orient", None),
        P("orient", None, "tile", None),
        P("tile", None, None),
        P("tile", None, None),
    )
    return jax.shard_map(
        local,
        mesh=mesh,
        in_specs=placed,
        out_specs=(P("tile", None, None, None), P("tile", None, None, None)),
        check_vma=False,
    )
```
